256 devices in a mesh: ctx: 16 (over z, core), tp: 8 (over x, y_hi), run: 2 (over y_lo).
Axes of the slice: x: 4, y: 4 (y_hi: 2, y_lo: 2; y = y_hi * 2 + y_lo), z: 8, core: 2. Of those that a mesh axis runs over, the one named last changes fastest.
Arguments:
- tokens: bfloat16 [8192, 5120], P(('run', 'ctx')), parts along dimension 0, may hold values from -28 to 28
- block_order: int32 [64], replicated, may hold values from 0 to 63, each once
- doc_lengths: int32 [16], replicated, may hold values from 1 to 1024, 4096 in all
- patch_pos: int32 [1024], P(('run', 'ctx')), parts along dimension 0, may hold values from 0 to 4095, as said below
- clean_rows: bfloat16 [1024, 5120], P(('run', 'ctx')), parts along dimension 0, may hold values from -6 to 6
- w_query: bfloat16 [5120, 5120], P(None, 'tp'), may hold values from -0.078125 to 0.078125
- q_bias: bfloat16 [5120], P('tp'), may hold values from -3 to 3
- w_key: bfloat16 [5120, 1024], P(None, 'tp'), may hold values from -0.078125 to 0.078125
- k_bias: bfloat16 [1024], P('tp'), may hold values from -3 to 3
- w_value: bfloat16 [5120, 1024], P(None, 'tp'), may hold values from -0.078125 to 0.078125
- v_bias: bfloat16 [1024], P('tp'), may hold values from -3 to 3
Outputs:
- attended: bfloat16 [8192, 5120], P(('run', 'ctx'), 'tp'), parts along dimension 0
The draws below stay inside these ranges and needn't reach their ends.
There are 2 independent parts, one for each index of `run`. The reference program is written for one: setup_inputs(seed, part) draws one part's arguments, and reference() takes and returns one part's arrays. A program takes and returns all parts, laid end to end along the dimension named above; an argument that names none is the same for every part. Nothing has to cross between parts.
Inputs may be any that keep to these rules, and one draw needn't show every extreme that they name: `block_order`: every block index appears exactly once. `doc_lengths`: the lengths sum to 4096 and the largest equals 1024. `patch_pos`: the 512 positions are distinct positions of the sequence, the first and the last position among them.
All inputs are finite; a program needn't handle non-finite values.
Results may differ from the reference program's by a relative error of at most 0.0076.
Values may be sent and summed in bfloat16 or wider, within the bound.
No kernel may reach another device: no remote copies, remote signals or barrier semaphores. Data moves between devices by JAX's collectives and lax.ppermute only.
A program may use at most 64 MiB of HBM per device.

```python
import math
import jax
import jax.numpy as jnp
import numpy as np
from jax import lax

D = 5120
QH = 40
KVH = 8
HD = 128
BLOCK = 64
NDOC = 16
TOKENS = 4096
NBLOCKS = 64
PATCHES = 512
MOST_DOC = 1024


def draw_tokens(key, part):
    return jnp.clip(jax.random.normal(key, (TOKENS, D), jnp.float32), -6.0, 6.0).astype(jnp.bfloat16)


def draw_patch_pos(key, part):
    inner = jax.random.permutation(jax.random.fold_in(key, 7), TOKENS - 2)[:PATCHES - 2].astype(jnp.int32) + 1
    ends = jnp.array([0, TOKENS - 1], dtype=jnp.int32)
    joined = jnp.concatenate([ends, inner])
    return jax.random.permutation(jax.random.fold_in(key, 11), joined).astype(jnp.int32)


def block_scale(own_key, dims, cuts, smallest, high):
    level = 1.0
    for axis_at, blocks in cuts:
        draws = jax.random.uniform(jax.random.fold_in(jax.random.fold_in(own_key, 6), axis_at), (blocks,), jnp.float32, smallest / len(cuts), high / len(cuts))
        level = level * jnp.repeat(jnp.exp(draws), dims[axis_at] // blocks).reshape((-1,) + (1,) * (len(dims) - 1 - axis_at))
    return level


def profile(number_of, total, bound, skew):
    loads = [(1 << 20) // math.isqrt(standing ** skew) + 1 for standing in range(2, number_of + 1)]
    spare, given = total - bound - (number_of - 1), [1] * (number_of - 1)
    while spare > 0:
        movable = [i for i in range(number_of - 1) if given[i] < bound]
        mass, left = sum([loads[i] for i in movable]), spare
        for i in movable:
            addition = min(bound - given[i], max(1, left * loads[i] // mass), spare)
            given[i] = given[i] + addition
            spare = spare - addition
    return np.array([bound] + given)


def uneven(own_key, amount, total, bound, skew):
    if amount == 2:
        one = jax.random.randint(own_key, (), max(1, total - bound), min(bound, total - 1) + 1)
        return jnp.stack([one, total - one])
    tallies = jnp.asarray(profile(amount, total, bound, skew), jnp.int32)
    twos = (amount - 1) // 2
    giver, taker = tallies[1:1 + 2 * twos:2], tallies[2:2 + 2 * twos:2]
    slack = jnp.minimum(giver - 1, bound - taker)
    moved = jax.random.randint(jax.random.fold_in(own_key, 1), (twos,), 0, 1 << 20) % (slack + 1)
    tallies = tallies.at[1:1 + 2 * twos:2].set(giver - moved).at[2:2 + 2 * twos:2].set(taker + moved)
    return tallies[jax.random.permutation(jax.random.fold_in(own_key, 2), amount)]


def scatter_about(rng, shape, spread, reach, pieces=(), kind=jnp.bfloat16):
    values = spread * jax.random.normal(rng, shape, jnp.float32)
    if pieces:
        values = values * block_scale(rng, shape, pieces, -0.22, 0.18)
    return jnp.clip(values, -reach, reach).astype(kind)


def setup_inputs(seed: int = 0, part: int = 0) -> dict:
    seeds = jax.random.split(jax.random.key(seed), 12)
    own_keys = jax.random.split(jax.random.fold_in(seeds[11], part), 12)
    return {
        "tokens": draw_tokens(jax.random.fold_in(jax.random.fold_in(seeds[11], part), 71), part),
        "block_order": jax.random.permutation(seeds[1], NBLOCKS).astype(jnp.int32),
        "doc_lengths": uneven(seeds[2], NDOC, TOKENS, MOST_DOC, 2).astype(jnp.int32),
        "patch_pos": draw_patch_pos(jax.random.fold_in(jax.random.fold_in(seeds[11], part), 71), part),
        "clean_rows": scatter_about(own_keys[4], (PATCHES, D), 1.0, 6.0, ((0, 16),)),
        "w_query": scatter_about(seeds[5], (D, QH * HD), D ** -0.5, 0.078125, ((1, 8),)),
        "q_bias": scatter_about(seeds[6], (QH * HD,), 0.5, 3.0, ((0, 8),)),
        "w_key": scatter_about(seeds[7], (D, KVH * HD), D ** -0.5, 0.078125, ((1, 8),)),
        "k_bias": scatter_about(seeds[8], (KVH * HD,), 0.5, 3.0, ((0, 8),)),
        "w_value": scatter_about(seeds[9], (D, KVH * HD), D ** -0.5, 0.078125, ((1, 8),)),
        "v_bias": scatter_about(seeds[10], (KVH * HD,), 0.5, 3.0, ((0, 8),)),
    }


THETA = 1000000.0


def rotate(head_rows, offset):
    half = head_rows.shape[-1] // 2
    frequency = jnp.power(jnp.float32(THETA), -2.0 * jnp.arange(half, dtype=jnp.float32) / head_rows.shape[-1])
    angles = offset.astype(jnp.float32)[:, None] * frequency[None, :]
    cosines = jnp.cos(angles)[:, None, :]
    sines = jnp.sin(angles)[:, None, :]
    first_half = head_rows[..., :half]
    second_half = head_rows[..., half:]
    return jnp.concatenate([first_half * cosines - second_half * sines, second_half * cosines + first_half * sines], axis=-1)


def project(source, weight, bias, offset, rotated):
    result = jnp.dot(source, weight, preferred_element_type=jnp.float32) + bias.astype(jnp.float32)[None, :]
    if rotated:
        result = rotate(result.reshape(source.shape[0], -1, HD), offset).reshape(source.shape[0], -1)
    return result.astype(jnp.bfloat16)


def slot_places(order, first_row, row_count):
    slots = first_row + jnp.arange(row_count, dtype=jnp.int32)
    owners = slots // BLOCK
    selector = owners[:, None] == jnp.arange(order.shape[0], dtype=jnp.int32)[None, :]
    picked = jnp.sum(jnp.where(selector, order[None, :], 0), axis=1).astype(jnp.int32)
    return picked * BLOCK + slots % BLOCK


def document_info(places, lengths):
    bounds = jnp.cumsum(lengths).astype(jnp.int32)
    passed = places[:, None] >= bounds[None, :]
    documents = jnp.sum(passed.astype(jnp.int32), axis=1).astype(jnp.int32)
    starts = jnp.sum(jnp.where(passed, lengths[None, :], 0), axis=1).astype(jnp.int32)
    return documents, places - starts


def reference(tokens, block_order, doc_lengths, patch_pos, clean_rows, w_query, q_bias, w_key, k_bias, w_value, v_bias):
    places = slot_places(block_order, jnp.int32(0), TOKENS)
    documents, offset = document_info(places, doc_lengths)
    matches = places[:, None] == patch_pos[None, :]
    present = jnp.any(matches, axis=1)
    chosen = jnp.sum(jnp.where(matches, jnp.arange(PATCHES, dtype=jnp.int32)[None, :], 0), axis=1).astype(jnp.int32)
    patched = jnp.where(present[:, None], clean_rows[chosen], tokens)
    group_size = QH // KVH
    query = project(patched, w_query, q_bias, offset, True).reshape(TOKENS, KVH, group_size, HD)
    keys = project(patched, w_key, k_bias, offset, True).reshape(TOKENS, KVH, HD)
    values = project(patched, w_value, v_bias, offset, False).reshape(TOKENS, KVH, HD)
    visible = (documents[:, None] == documents[None, :]) & (places[None, :] <= places[:, None])
    score_scale = HD ** -0.5

    def one_head(operands):
        group_query, head_keys, head_values = operands
        scores = jnp.einsum("tgd,sd->gts", group_query.astype(jnp.float32), head_keys.astype(jnp.float32), precision=lax.Precision.HIGHEST) * score_scale
        masked = jnp.where(visible[None], scores, -1e30)
        peak = jnp.max(masked, axis=-1, keepdims=True)
        weights = jnp.where(visible[None], jnp.exp(masked - peak), 0.0)
        total = jnp.sum(weights, axis=-1)
        rounded = lax.optimization_barrier(weights.astype(jnp.bfloat16))
        mixed = jnp.einsum("gts,sd->tgd", rounded.astype(jnp.float32), head_values.astype(jnp.float32), precision=lax.Precision.HIGHEST)
        return mixed / jnp.transpose(total)[:, :, None]

    outputs = lax.map(one_head, (jnp.transpose(query, (1, 0, 2, 3)), jnp.transpose(keys, (1, 0, 2)), jnp.transpose(values, (1, 0, 2))))
    return jnp.transpose(outputs, (1, 0, 2, 3)).reshape(TOKENS, QH * HD).astype(jnp.bfloat16)
```

```python
import jax
import jax.numpy as jnp
from jax import lax
from jax.sharding import PartitionSpec as P

HD = 128
BLOCK = 64
MOST_DOC = 1024


THETA = 1000000.0


def rotate(head_rows, offset):
    half = head_rows.shape[-1] // 2
    frequency = jnp.power(
        jnp.float32(THETA), -2.0 * jnp.arange(half, dtype=jnp.float32) / head_rows.shape[-1]
    )
    angles = offset.astype(jnp.float32)[:, None] * frequency[None, :]
    cosines = jnp.cos(angles)[:, None, :]
    sines = jnp.sin(angles)[:, None, :]
    first_half = head_rows[..., :half]
    second_half = head_rows[..., half:]
    return jnp.concatenate(
        [first_half * cosines - second_half * sines, second_half * cosines + first_half * sines],
        axis=-1,
    )


def project(source, weight, bias, offset, rotated):
    result = (
        jnp.dot(source, weight, preferred_element_type=jnp.float32)
        + bias.astype(jnp.float32)[None, :]
    )
    if rotated:
        result = rotate(result.reshape(source.shape[0], -1, HD), offset).reshape(
            source.shape[0], -1
        )
    return result.astype(jnp.bfloat16)


def slot_places(order, first_row, row_count):
    slots = first_row + jnp.arange(row_count, dtype=jnp.int32)
    owners = slots // BLOCK
    selector = owners[:, None] == jnp.arange(order.shape[0], dtype=jnp.int32)[None, :]
    picked = jnp.sum(jnp.where(selector, order[None, :], 0), axis=1)
    return picked * BLOCK + slots % BLOCK


def document_of(places, bounds):
    return jnp.sum((places[..., None] >= bounds).astype(jnp.int32), axis=-1)


def document_info(places, lengths):
    bounds = jnp.cumsum(lengths)
    passed = places[:, None] >= bounds[None, :]
    documents = jnp.sum(passed.astype(jnp.int32), axis=1)
    starts = jnp.sum(jnp.where(passed, lengths[None, :], 0), axis=1)
    return (documents, places - starts)


def body(
    tokens,
    block_order,
    doc_lengths,
    patch_pos,
    clean_rows,
    w_query,
    q_bias,
    w_key,
    k_bias,
    w_value,
    v_bias,
):
    rows = tokens.shape[0]
    patches = patch_pos.shape[0]
    nblocks = block_order.shape[0]
    heads = w_query.shape[1] // HD
    me = lax.axis_index("ctx")
    places = slot_places(block_order, me * rows, rows)
    documents, offset = document_info(places, doc_lengths)
    patch_offset = document_info(patch_pos, doc_lengths)[1]

    source = jnp.concatenate([tokens, clean_rows], axis=0)
    both_offset = jnp.concatenate([offset, patch_offset], axis=0)
    query = project(source, w_query, q_bias, both_offset, True)
    keys = project(source, w_key, k_bias, both_offset, True)
    values = project(source, w_value, v_bias, both_offset, False)

    coded = jnp.zeros((16, HD), jnp.bfloat16)
    coded = coded.at[0, :patches].set((patch_pos // BLOCK).astype(jnp.bfloat16))
    coded = coded.at[1, :patches].set((patch_pos % BLOCK).astype(jnp.bfloat16))
    parts = [keys[:rows], values[:rows], keys[rows:], values[rows:]]
    parts += [query[rows:, h * HD:(h + 1) * HD] for h in range(heads)]
    parts.append(coded)
    packed = jnp.concatenate(parts, axis=0)
    gathered = lax.all_gather(packed, "ctx", axis=0, tiled=False)
    peers = gathered.shape[0]
    total_rows = peers * rows

    at = 0
    slot_keys = gathered[:, at:at + rows].reshape(total_rows, HD)
    at += rows
    slot_values = gathered[:, at:at + rows].reshape(total_rows, HD)
    at += rows
    clean_keys = gathered[:, at:at + patches].reshape(peers * patches, HD)
    at += patches
    clean_values = gathered[:, at:at + patches].reshape(peers * patches, HD)
    at += patches
    clean_query = gathered[:, at:at + heads * patches].reshape(peers, heads, patches, HD)
    at += heads * patches
    code = gathered[:, at:at + 2, :patches].astype(jnp.float32)
    positions = (code[:, 0] * BLOCK + code[:, 1]).astype(jnp.int32)

    match = places[:, None, None] == positions[None]
    present = jnp.any(match, axis=(1, 2))
    picked = jnp.einsum(
        "spr,phrd->shd", match.astype(jnp.bfloat16), clean_query,
        preferred_element_type=jnp.float32,
    ).astype(jnp.bfloat16)
    query = jnp.where(present[:, None, None], picked, query[:rows].reshape(rows, heads, HD))

    inverse = jnp.zeros((nblocks,), jnp.int32).at[block_order].set(
        jnp.arange(nblocks, dtype=jnp.int32)
    )
    flat_positions = positions.reshape(-1)

    def to_sequence(slot_rows, clean):
        ordered = slot_rows.reshape(nblocks, BLOCK, HD)[inverse].reshape(total_rows, HD)
        ordered = ordered.at[flat_positions].set(clean, unique_indices=True)
        return jnp.concatenate([jnp.zeros((MOST_DOC, HD), jnp.bfloat16), ordered], axis=0)

    padded_keys = to_sequence(slot_keys, clean_keys)
    padded_values = to_sequence(slot_values, clean_values)

    window = MOST_DOC + BLOCK
    qblocks = rows // BLOCK
    seq_blocks = lax.dynamic_slice_in_dim(block_order, me * qblocks, qblocks)
    starts = seq_blocks * BLOCK

    def take(padded):
        return jax.vmap(lambda s: lax.dynamic_slice_in_dim(padded, s, window))(starts)

    window_keys = take(padded_keys)
    window_values = take(padded_values)
    key_places = starts[:, None] - MOST_DOC + jnp.arange(window, dtype=jnp.int32)[None, :]
    bounds = jnp.cumsum(doc_lengths)
    key_documents = document_of(key_places, bounds)
    query_places = places.reshape(qblocks, BLOCK)
    query_documents = documents.reshape(qblocks, BLOCK)
    visible = (
        (query_documents[:, :, None] == key_documents[:, None, :])
        & (key_places[:, None, :] <= query_places[:, :, None])
        & (key_places[:, None, :] >= 0)
    )[:, None]
    score_scale = HD ** (-0.5)
    scores = (
        jnp.einsum(
            "bqhd,bkd->bhqk",
            query.reshape(qblocks, BLOCK, heads, HD),
            window_keys,
            preferred_element_type=jnp.float32,
        )
        * score_scale
    )
    masked = jnp.where(visible, scores, -1e30)
    peak = jnp.max(masked, axis=-1, keepdims=True)
    weights = jnp.where(visible, jnp.exp(masked - peak), 0.0)
    total = jnp.sum(weights, axis=-1)
    mixed = jnp.einsum(
        "bhqk,bkd->bqhd",
        weights.astype(jnp.bfloat16),
        window_values,
        preferred_element_type=jnp.float32,
    )
    out = mixed / jnp.transpose(total, (0, 2, 1))[..., None]
    return out.reshape(rows, heads * HD).astype(jnp.bfloat16)


def solution(mesh):
    in_specs = (
        P(("run", "ctx"), None),
        P(),
        P(),
        P(("run", "ctx")),
        P(("run", "ctx"), None),
        P(None, "tp"),
        P("tp"),
        P(None, "tp"),
        P("tp"),
        P(None, "tp"),
        P("tp"),
    )
    out_specs = P(("run", "ctx"), "tp")
    return jax.shard_map(body, mesh=mesh, in_specs=in_specs, out_specs=out_specs, check_vma=False)
```

```python
import jax
import jax.numpy as jnp
from jax import lax
from jax.sharding import PartitionSpec as P

HD = 128
BLOCK = 64
MOST_DOC = 1024


THETA = 1000000.0


def rotate(head_rows, offset):
    half = head_rows.shape[-1] // 2
    frequency = jnp.power(
        jnp.float32(THETA), -2.0 * jnp.arange(half, dtype=jnp.float32) / head_rows.shape[-1]
    )
    angles = offset.astype(jnp.float32)[:, None] * frequency[None, :]
    cosines = jnp.cos(angles)[:, None, :]
    sines = jnp.sin(angles)[:, None, :]
    first_half = head_rows[..., :half]
    second_half = head_rows[..., half:]
    return jnp.concatenate(
        [first_half * cosines - second_half * sines, second_half * cosines + first_half * sines],
        axis=-1,
    )


def project(source, weight, bias, offset, rotated):
    result = (
        jnp.dot(source, weight, preferred_element_type=jnp.float32)
        + bias.astype(jnp.float32)[None, :]
    )
    if rotated:
        result = rotate(result.reshape(source.shape[0], -1, HD), offset).reshape(
            source.shape[0], -1
        )
    return result.astype(jnp.bfloat16)


def slot_places(order, first_row, row_count):
    slots = first_row + jnp.arange(row_count, dtype=jnp.int32)
    owners = slots // BLOCK
    selector = owners[:, None] == jnp.arange(order.shape[0], dtype=jnp.int32)[None, :]
    picked = jnp.sum(jnp.where(selector, order[None, :], 0), axis=1)
    return picked * BLOCK + slots % BLOCK


def document_of(places, bounds):
    return jnp.sum((places[..., None] >= bounds).astype(jnp.int32), axis=-1)


def document_info(places, lengths):
    bounds = jnp.cumsum(lengths)
    passed = places[:, None] >= bounds[None, :]
    documents = jnp.sum(passed.astype(jnp.int32), axis=1)
    starts = jnp.sum(jnp.where(passed, lengths[None, :], 0), axis=1)
    return (documents, places - starts)


def body(
    tokens,
    block_order,
    doc_lengths,
    patch_pos,
    clean_rows,
    w_query,
    q_bias,
    w_key,
    k_bias,
    w_value,
    v_bias,
):
    rows = tokens.shape[0]
    patches = patch_pos.shape[0]
    nblocks = block_order.shape[0]
    heads = w_query.shape[1] // HD
    me = lax.axis_index("ctx")
    places = slot_places(block_order, me * rows, rows)
    documents, offset = document_info(places, doc_lengths)
    patch_offset = document_info(patch_pos, doc_lengths)[1]

    keys = project(tokens, w_key, k_bias, offset, True)
    values = project(tokens, w_value, v_bias, offset, False)
    clean_query = project(clean_rows, w_query, q_bias, patch_offset, True)
    clean_keys = project(clean_rows, w_key, k_bias, patch_offset, True)
    clean_values = project(clean_rows, w_value, v_bias, patch_offset, False)

    width = 2 * HD
    coded = jnp.zeros((16, width), jnp.bfloat16)
    coded = coded.at[0, :patches].set((patch_pos // BLOCK).astype(jnp.bfloat16))
    coded = coded.at[1, :patches].set((patch_pos % BLOCK).astype(jnp.bfloat16))
    pairs = (heads + 1) // 2
    padded_query = jnp.pad(clean_query, ((0, 0), (0, pairs * width - heads * HD)))
    parts = [
        jnp.concatenate([keys, values], axis=1),
        jnp.concatenate([clean_keys, clean_values], axis=1),
    ]
    parts += [padded_query[:, p * width:(p + 1) * width] for p in range(pairs)]
    parts.append(coded)
    packed = jnp.concatenate(parts, axis=0)
    gathered = lax.all_gather(packed, "ctx", axis=0, tiled=False)
    peers = gathered.shape[0]
    total_rows = peers * rows

    at = 0
    slot_kv = gathered[:, at:at + rows].reshape(total_rows, width)
    at += rows
    clean_kv = gathered[:, at:at + patches].reshape(peers * patches, width)
    at += patches
    clean_q = gathered[:, at:at + pairs * patches].reshape(peers, pairs, patches, width)
    at += pairs * patches
    code = gathered[:, at:at + 2, :patches].astype(jnp.float32)
    positions = (code[:, 0] * BLOCK + code[:, 1]).astype(jnp.int32)

    query = project(tokens, w_query, q_bias, offset, True).reshape(rows, heads, HD)
    match = places[:, None, None] == positions[None]
    present = jnp.any(match, axis=(1, 2))
    picked = jnp.einsum(
        "spr,pqrd->sqd", match.astype(jnp.bfloat16), clean_q,
        preferred_element_type=jnp.float32,
    ).astype(jnp.bfloat16).reshape(rows, pairs * width)[:, :heads * HD]
    query = jnp.where(present[:, None, None], picked.reshape(rows, heads, HD), query)

    inverse = jnp.zeros((nblocks,), jnp.int32).at[block_order].set(
        jnp.arange(nblocks, dtype=jnp.int32)
    )
    flat_positions = positions.reshape(-1)
    patch_slots = inverse[flat_positions // BLOCK] * BLOCK + flat_positions % BLOCK
    slot_kv = slot_kv.at[patch_slots].set(clean_kv, unique_indices=True)

    window = MOST_DOC + BLOCK
    qblocks = rows // BLOCK
    seq_blocks = lax.dynamic_slice_in_dim(block_order, me * qblocks, qblocks)
    starts = seq_blocks * BLOCK

    back = MOST_DOC // BLOCK
    wanted = seq_blocks[:, None] - back + jnp.arange(back + 1, dtype=jnp.int32)[None, :]
    window_slots = inverse[jnp.clip(wanted, 0, nblocks - 1)]
    window_kv = slot_kv.reshape(nblocks, BLOCK, width)[window_slots].reshape(qblocks, window, width)
    window_keys = window_kv[..., :HD]
    window_values = window_kv[..., HD:]
    key_places = starts[:, None] - MOST_DOC + jnp.arange(window, dtype=jnp.int32)[None, :]
    bounds = jnp.cumsum(doc_lengths)
    key_documents = document_of(key_places, bounds)
    query_places = places.reshape(qblocks, BLOCK)
    query_documents = documents.reshape(qblocks, BLOCK)
    visible = (
        (query_documents[:, :, None] == key_documents[:, None, :])
        & (key_places[:, None, :] <= query_places[:, :, None])
        & (key_places[:, None, :] >= 0)
    )[:, None]
    score_scale = HD ** (-0.5)
    scores = (
        jnp.einsum(
            "bqhd,bkd->bhqk",
            query.reshape(qblocks, BLOCK, heads, HD),
            window_keys,
            preferred_element_type=jnp.float32,
        )
        * score_scale
    )
    masked = jnp.where(visible, scores, -1e30)
    peak = jnp.max(masked, axis=-1, keepdims=True)
    weights = jnp.where(visible, jnp.exp(masked - peak), 0.0)
    total = jnp.sum(weights, axis=-1)
    mixed = jnp.einsum(
        "bhqk,bkd->bqhd",
        weights.astype(jnp.bfloat16),
        window_values,
        preferred_element_type=jnp.float32,
    )
    out = mixed / jnp.transpose(total, (0, 2, 1))[..., None]
    return out.reshape(rows, heads * HD).astype(jnp.bfloat16)


def solution(mesh):
    in_specs = (
        P(("run", "ctx"), None),
        P(),
        P(),
        P(("run", "ctx")),
        P(("run", "ctx"), None),
        P(None, "tp"),
        P("tp"),
        P(None, "tp"),
        P("tp"),
        P(None, "tp"),
        P("tp"),
    )
    out_specs = P(("run", "ctx"), "tp")
    return jax.shard_map(body, mesh=mesh, in_specs=in_specs, out_specs=out_specs, check_vma=False)
```

```python
import jax
import jax.numpy as jnp
from jax import lax
from jax.sharding import PartitionSpec as P

HD = 128
BLOCK = 64
MOST_DOC = 1024


THETA = 1000000.0


def rotate(head_rows, offset):
    half = head_rows.shape[-1] // 2
    frequency = jnp.power(
        jnp.float32(THETA), -2.0 * jnp.arange(half, dtype=jnp.float32) / head_rows.shape[-1]
    )
    angles = offset.astype(jnp.float32)[:, None] * frequency[None, :]
    cosines = jnp.cos(angles)[:, None, :]
    sines = jnp.sin(angles)[:, None, :]
    first_half = head_rows[..., :half]
    second_half = head_rows[..., half:]
    return jnp.concatenate(
        [first_half * cosines - second_half * sines, second_half * cosines + first_half * sines],
        axis=-1,
    )


def project(source, weight, bias, offset, rotated):
    result = (
        jnp.dot(source, weight, preferred_element_type=jnp.float32)
        + bias.astype(jnp.float32)[None, :]
    )
    if rotated:
        result = rotate(result.reshape(source.shape[0], -1, HD), offset).reshape(
            source.shape[0], -1
        )
    return result.astype(jnp.bfloat16)


def slot_places(order, first_row, row_count):
    slots = first_row + jnp.arange(row_count, dtype=jnp.int32)
    owners = slots // BLOCK
    selector = owners[:, None] == jnp.arange(order.shape[0], dtype=jnp.int32)[None, :]
    picked = jnp.sum(jnp.where(selector, order[None, :], 0), axis=1)
    return picked * BLOCK + slots % BLOCK


def document_of(places, bounds):
    return jnp.sum((places[..., None] >= bounds).astype(jnp.int32), axis=-1)


def document_info(places, lengths):
    bounds = jnp.cumsum(lengths)
    passed = places[:, None] >= bounds[None, :]
    documents = jnp.sum(passed.astype(jnp.int32), axis=1)
    starts = jnp.sum(jnp.where(passed, lengths[None, :], 0), axis=1)
    return (documents, places - starts)


def body(
    tokens,
    block_order,
    doc_lengths,
    patch_pos,
    clean_rows,
    w_query,
    q_bias,
    w_key,
    k_bias,
    w_value,
    v_bias,
):
    rows = tokens.shape[0]
    patches = patch_pos.shape[0]
    nblocks = block_order.shape[0]
    heads = w_query.shape[1] // HD
    me = lax.axis_index("ctx")
    places = slot_places(block_order, me * rows, rows)
    documents, offset = document_info(places, doc_lengths)
    patch_offset = document_info(patch_pos, doc_lengths)[1]

    keys = project(tokens, w_key, k_bias, offset, True)
    values = project(tokens, w_value, v_bias, offset, False)
    clean_query = project(clean_rows, w_query, q_bias, patch_offset, True)
    clean_keys = project(clean_rows, w_key, k_bias, patch_offset, True)
    clean_values = project(clean_rows, w_value, v_bias, patch_offset, False)

    width = 2 * HD
    coded = jnp.zeros((16, width), jnp.bfloat16)
    coded = coded.at[0, :patches].set((patch_pos // BLOCK).astype(jnp.bfloat16))
    coded = coded.at[1, :patches].set((patch_pos % BLOCK).astype(jnp.bfloat16))
    pairs = (heads + 1) // 2
    padded_query = jnp.pad(clean_query, ((0, 0), (0, pairs * width - heads * HD)))
    parts = [
        jnp.concatenate([keys, values], axis=1),
        jnp.concatenate([clean_keys, clean_values], axis=1),
    ]
    parts += [padded_query[:, p * width:(p + 1) * width] for p in range(pairs)]
    parts.append(coded)
    packed = jnp.concatenate(parts, axis=0)
    gathered = lax.all_gather(packed, "ctx", axis=0, tiled=False)
    peers = gathered.shape[0]
    total_rows = peers * rows

    at = 0
    slot_kv = gathered[:, at:at + rows].reshape(total_rows, width)
    at += rows
    clean_kv = gathered[:, at:at + patches].reshape(peers * patches, width)
    at += patches
    clean_q = gathered[:, at:at + pairs * patches].reshape(peers, pairs, patches, width)
    at += pairs * patches
    code = gathered[:, at:at + 2, :patches].astype(jnp.float32)
    positions = (code[:, 0] * BLOCK + code[:, 1]).astype(jnp.int32)

    query = project(tokens, w_query, q_bias, offset, True)
    flat_positions = positions.reshape(-1)
    match = places[:, None] == flat_positions[None, :]
    present = jnp.any(match, axis=1)
    clean_q = jnp.transpose(clean_q, (0, 2, 1, 3)).reshape(peers * patches, pairs * width)
    picked = jnp.dot(
        match.astype(jnp.bfloat16), clean_q, preferred_element_type=jnp.float32
    ).astype(jnp.bfloat16)[:, :heads * HD]
    query = jnp.where(present[:, None], picked, query)

    inverse = jnp.zeros((nblocks,), jnp.int32).at[block_order].set(
        jnp.arange(nblocks, dtype=jnp.int32)
    )

    window = MOST_DOC + BLOCK
    qblocks = rows // BLOCK
    seq_blocks = lax.dynamic_slice_in_dim(block_order, me * qblocks, qblocks)
    starts = seq_blocks * BLOCK

    back = MOST_DOC // BLOCK
    wanted = seq_blocks[:, None] - back + jnp.arange(back + 1, dtype=jnp.int32)[None, :]
    window_slots = inverse[jnp.clip(wanted, 0, nblocks - 1)]
    window_kv = slot_kv.reshape(nblocks, BLOCK, width)[window_slots].reshape(qblocks, window, width)
    key_places = starts[:, None] - MOST_DOC + jnp.arange(window, dtype=jnp.int32)[None, :]
    key_match = key_places[:, :, None] == flat_positions[None, None, :]
    key_present = jnp.any(key_match, axis=-1)
    key_picked = jnp.einsum(
        "bkj,jd->bkd", key_match.astype(jnp.bfloat16), clean_kv,
        preferred_element_type=jnp.float32,
    ).astype(jnp.bfloat16)
    window_kv = jnp.where(key_present[..., None], key_picked, window_kv)
    window_keys = window_kv[..., :HD]
    window_values = window_kv[..., HD:]
    bounds = jnp.cumsum(doc_lengths)
    key_documents = document_of(key_places, bounds)
    query_places = places.reshape(qblocks, BLOCK)
    query_documents = documents.reshape(qblocks, BLOCK)
    visible = (
        (query_documents[:, :, None] == key_documents[:, None, :])
        & (key_places[:, None, :] <= query_places[:, :, None])
        & (key_places[:, None, :] >= 0)
    )[:, None]
    score_scale = HD ** (-0.5)
    scores = (
        jnp.einsum(
            "bqhd,bkd->bhqk",
            query.reshape(qblocks, BLOCK, heads, HD),
            window_keys,
            preferred_element_type=jnp.float32,
        )
        * score_scale
    )
    masked = jnp.where(visible, scores, -1e30)
    peak = jnp.max(masked, axis=-1, keepdims=True)
    weights = jnp.where(visible, jnp.exp(masked - peak), 0.0)
    total = jnp.sum(weights, axis=-1)
    mixed = jnp.einsum(
        "bhqk,bkd->bqhd",
        weights.astype(jnp.bfloat16),
        window_values,
        preferred_element_type=jnp.float32,
    )
    out = mixed / jnp.transpose(total, (0, 2, 1))[..., None]
    return out.reshape(rows, heads * HD).astype(jnp.bfloat16)


def solution(mesh):
    in_specs = (
        P(("run", "ctx"), None),
        P(),
        P(),
        P(("run", "ctx")),
        P(("run", "ctx"), None),
        P(None, "tp"),
        P("tp"),
        P(None, "tp"),
        P("tp"),
        P(None, "tp"),
        P("tp"),
    )
    out_specs = P(("run", "ctx"), "tp")
    return jax.shard_map(body, mesh=mesh, in_specs=in_specs, out_specs=out_specs, check_vma=False)
```

```python
import jax
import jax.numpy as jnp
from jax import lax
from jax.sharding import PartitionSpec as P

HD = 128
BLOCK = 64
MOST_DOC = 1024


THETA = 1000000.0


def rotate(head_rows, offset):
    half = head_rows.shape[-1] // 2
    frequency = jnp.power(
        jnp.float32(THETA), -2.0 * jnp.arange(half, dtype=jnp.float32) / head_rows.shape[-1]
    )
    angles = offset.astype(jnp.float32)[:, None] * frequency[None, :]
    cosines = jnp.cos(angles)[:, None, :]
    sines = jnp.sin(angles)[:, None, :]
    first_half = head_rows[..., :half]
    second_half = head_rows[..., half:]
    return jnp.concatenate(
        [first_half * cosines - second_half * sines, second_half * cosines + first_half * sines],
        axis=-1,
    )


def project(source, weight, bias, offset, rotated):
    result = (
        jnp.dot(source, weight, preferred_element_type=jnp.float32)
        + bias.astype(jnp.float32)[None, :]
    )
    if rotated:
        result = rotate(result.reshape(source.shape[0], -1, HD), offset).reshape(
            source.shape[0], -1
        )
    return result.astype(jnp.bfloat16)


def slot_places(order, first_row, row_count):
    slots = first_row + jnp.arange(row_count, dtype=jnp.int32)
    owners = slots // BLOCK
    selector = owners[:, None] == jnp.arange(order.shape[0], dtype=jnp.int32)[None, :]
    picked = jnp.sum(jnp.where(selector, order[None, :], 0), axis=1)
    return picked * BLOCK + slots % BLOCK


def document_of(places, bounds):
    return jnp.sum((places[..., None] >= bounds).astype(jnp.int32), axis=-1)


def document_info(places, lengths):
    bounds = jnp.cumsum(lengths)
    passed = places[:, None] >= bounds[None, :]
    documents = jnp.sum(passed.astype(jnp.int32), axis=1)
    starts = jnp.sum(jnp.where(passed, lengths[None, :], 0), axis=1)
    return (documents, places - starts)


def body(
    tokens,
    block_order,
    doc_lengths,
    patch_pos,
    clean_rows,
    w_query,
    q_bias,
    w_key,
    k_bias,
    w_value,
    v_bias,
):
    rows = tokens.shape[0]
    patches = patch_pos.shape[0]
    nblocks = block_order.shape[0]
    heads = w_query.shape[1] // HD
    me = lax.axis_index("ctx")
    places = slot_places(block_order, me * rows, rows)
    documents, offset = document_info(places, doc_lengths)
    patch_offset = document_info(patch_pos, doc_lengths)[1]

    keys = project(tokens, w_key, k_bias, offset, True)
    values = project(tokens, w_value, v_bias, offset, False)
    clean_query = project(clean_rows, w_query, q_bias, patch_offset, True)
    clean_keys = project(clean_rows, w_key, k_bias, patch_offset, True)
    clean_values = project(clean_rows, w_value, v_bias, patch_offset, False)

    width = 2 * HD
    pairs = (heads + 1) // 2
    spare = pairs * width - heads * HD
    coded = jnp.stack(
        [(patch_pos // BLOCK).astype(jnp.bfloat16), (patch_pos % BLOCK).astype(jnp.bfloat16)], axis=1
    )
    padded_query = jnp.concatenate(
        [clean_query, coded, jnp.zeros((patches, spare - 2), jnp.bfloat16)], axis=1
    )
    parts = [
        jnp.concatenate([keys, values], axis=1),
        jnp.concatenate([clean_keys, clean_values], axis=1),
    ]
    parts += [padded_query[:, p * width:(p + 1) * width] for p in range(pairs)]
    packed = jnp.concatenate(parts, axis=0)
    lines = packed.shape[0]
    gathered = lax.all_gather(packed, "ctx", axis=0, tiled=False)
    peers = gathered.shape[0]
    per_peer = lines // BLOCK
    local_blocks = rows // BLOCK

    clean_kv = gathered[:, rows:rows + patches].reshape(peers * patches, width)
    clean_q = gathered[:, rows + patches:].reshape(peers, pairs, patches, width)
    clean_q = jnp.transpose(clean_q, (0, 2, 1, 3)).reshape(peers * patches, pairs * width)
    code = clean_q[:, heads * HD:heads * HD + 2].astype(jnp.float32)
    positions = (code[:, 0] * BLOCK + code[:, 1]).astype(jnp.int32)
    bounds = jnp.cumsum(doc_lengths)
    clean_documents = document_of(positions, bounds)

    query = project(tokens, w_query, q_bias, offset, True)
    match = places[:, None] == positions[None, :]
    present = jnp.any(match, axis=1)
    picked = jnp.dot(
        match.astype(jnp.bfloat16), clean_q, preferred_element_type=jnp.float32
    ).astype(jnp.bfloat16)[:, :heads * HD]
    query = jnp.where(present[:, None], picked, query)

    inverse = jnp.zeros((nblocks,), jnp.int32).at[block_order].set(
        jnp.arange(nblocks, dtype=jnp.int32)
    )
    patched_place = jnp.zeros((nblocks * BLOCK,), jnp.bool_).at[positions].set(True)

    window = MOST_DOC + BLOCK
    back = MOST_DOC // BLOCK
    seq_blocks = lax.dynamic_slice_in_dim(block_order, me * local_blocks, local_blocks)
    starts = seq_blocks * BLOCK
    wanted = seq_blocks[:, None] - back + jnp.arange(back + 1, dtype=jnp.int32)[None, :]
    window_slots = inverse[jnp.clip(wanted, 0, nblocks - 1)]
    window_blocks = (window_slots // local_blocks) * per_peer + window_slots % local_blocks
    window_kv = gathered.reshape(peers * per_peer, BLOCK, width)[window_blocks].reshape(
        local_blocks, window, width
    )
    key_places = starts[:, None] - MOST_DOC + jnp.arange(window, dtype=jnp.int32)[None, :]
    key_documents = document_of(key_places, bounds)
    key_kept = (key_places >= 0) & ~patched_place[jnp.clip(key_places, 0, nblocks * BLOCK - 1)]
    query_places = places.reshape(local_blocks, BLOCK)
    query_documents = documents.reshape(local_blocks, BLOCK)
    visible = (
        (query_documents[:, :, None] == key_documents[:, None, :])
        & (key_places[:, None, :] <= query_places[:, :, None])
        & key_kept[:, None, :]
    )[:, None]
    clean_visible = (
        (query_documents[:, :, None] == clean_documents[None, None, :])
        & (positions[None, None, :] <= query_places[:, :, None])
    )[:, None]
    score_scale = HD ** (-0.5)
    grouped = query.reshape(local_blocks, BLOCK, heads, HD)
    scores = (
        jnp.einsum(
            "bqhd,bkd->bhqk", grouped, window_kv[..., :HD], preferred_element_type=jnp.float32
        )
        * score_scale
    )
    clean_scores = (
        jnp.einsum(
            "bqhd,kd->bhqk", grouped, clean_kv[:, :HD], preferred_element_type=jnp.float32
        )
        * score_scale
    )
    masked = jnp.where(visible, scores, -1e30)
    clean_masked = jnp.where(clean_visible, clean_scores, -1e30)
    peak = jnp.maximum(
        jnp.max(masked, axis=-1, keepdims=True), jnp.max(clean_masked, axis=-1, keepdims=True)
    )
    weights = jnp.where(visible, jnp.exp(masked - peak), 0.0)
    clean_weights = jnp.where(clean_visible, jnp.exp(clean_masked - peak), 0.0)
    total = jnp.sum(weights, axis=-1) + jnp.sum(clean_weights, axis=-1)
    mixed = jnp.einsum(
        "bhqk,bkd->bqhd",
        weights.astype(jnp.bfloat16),
        window_kv[..., HD:],
        preferred_element_type=jnp.float32,
    ) + jnp.einsum(
        "bhqk,kd->bqhd",
        clean_weights.astype(jnp.bfloat16),
        clean_kv[:, HD:],
        preferred_element_type=jnp.float32,
    )
    out = mixed / jnp.transpose(total, (0, 2, 1))[..., None]
    return out.reshape(rows, heads * HD).astype(jnp.bfloat16)


def solution(mesh):
    in_specs = (
        P(("run", "ctx"), None),
        P(),
        P(),
        P(("run", "ctx")),
        P(("run", "ctx"), None),
        P(None, "tp"),
        P("tp"),
        P(None, "tp"),
        P("tp"),
        P(None, "tp"),
        P("tp"),
    )
    out_specs = P(("run", "ctx"), "tp")
    return jax.shard_map(body, mesh=mesh, in_specs=in_specs, out_specs=out_specs, check_vma=False)
```

```python
import jax
import jax.numpy as jnp
from jax import lax
from jax.sharding import PartitionSpec as P

HD = 128
BLOCK = 64
MOST_DOC = 1024


THETA = 1000000.0


def rotate(head_rows, offset):
    half = head_rows.shape[-1] // 2
    frequency = jnp.power(
        jnp.float32(THETA), -2.0 * jnp.arange(half, dtype=jnp.float32) / head_rows.shape[-1]
    )
    angles = offset.astype(jnp.float32)[:, None] * frequency[None, :]
    cosines = jnp.cos(angles)[:, None, :]
    sines = jnp.sin(angles)[:, None, :]
    first_half = head_rows[..., :half]
    second_half = head_rows[..., half:]
    return jnp.concatenate(
        [first_half * cosines - second_half * sines, second_half * cosines + first_half * sines],
        axis=-1,
    )


def project(source, weight, bias, offset, rotated):
    result = (
        jnp.dot(source, weight, preferred_element_type=jnp.float32)
        + bias.astype(jnp.float32)[None, :]
    )
    if rotated:
        result = rotate(result.reshape(source.shape[0], -1, HD), offset).reshape(
            source.shape[0], -1
        )
    return result.astype(jnp.bfloat16)


def slot_places(order, first_row, row_count):
    slots = first_row + jnp.arange(row_count, dtype=jnp.int32)
    owners = slots // BLOCK
    selector = owners[:, None] == jnp.arange(order.shape[0], dtype=jnp.int32)[None, :]
    picked = jnp.sum(jnp.where(selector, order[None, :], 0), axis=1)
    return picked * BLOCK + slots % BLOCK


def document_of(places, bounds):
    return jnp.sum((places[..., None] >= bounds).astype(jnp.int32), axis=-1)


def document_info(places, lengths):
    bounds = jnp.cumsum(lengths)
    passed = places[:, None] >= bounds[None, :]
    documents = jnp.sum(passed.astype(jnp.int32), axis=1)
    starts = jnp.sum(jnp.where(passed, lengths[None, :], 0), axis=1)
    return (documents, places - starts)


def body(
    tokens,
    block_order,
    doc_lengths,
    patch_pos,
    clean_rows,
    w_query,
    q_bias,
    w_key,
    k_bias,
    w_value,
    v_bias,
):
    rows = tokens.shape[0]
    patches = patch_pos.shape[0]
    nblocks = block_order.shape[0]
    heads = w_query.shape[1] // HD
    me = lax.axis_index("ctx")
    places = slot_places(block_order, me * rows, rows)
    documents, offset = document_info(places, doc_lengths)
    patch_offset = document_info(patch_pos, doc_lengths)[1]

    keys = project(tokens, w_key, k_bias, offset, True)
    values = project(tokens, w_value, v_bias, offset, False)
    clean_query = project(clean_rows, w_query, q_bias, patch_offset, True)
    clean_keys = project(clean_rows, w_key, k_bias, patch_offset, True)
    clean_values = project(clean_rows, w_value, v_bias, patch_offset, False)

    width = 2 * HD
    pairs = (heads + 1) // 2
    spare = pairs * width - heads * HD
    coded = jnp.stack(
        [(patch_pos // BLOCK).astype(jnp.bfloat16), (patch_pos % BLOCK).astype(jnp.bfloat16)], axis=1
    )
    padded_query = jnp.concatenate(
        [clean_query, coded, jnp.zeros((patches, spare - 2), jnp.bfloat16)], axis=1
    )
    parts = [
        jnp.concatenate([keys, values], axis=1),
        jnp.concatenate([clean_keys, clean_values], axis=1),
    ]
    parts += [padded_query[:, p * width:(p + 1) * width] for p in range(pairs)]
    packed = jnp.concatenate(parts, axis=0)
    lines = packed.shape[0]
    gathered = lax.all_gather(packed, "ctx", axis=0, tiled=False)
    peers = gathered.shape[0]
    per_peer = lines // BLOCK
    local_blocks = rows // BLOCK

    clean_kv = gathered[:, rows:rows + patches].reshape(peers * patches, width)
    clean_q = gathered[:, rows + patches:].reshape(peers, pairs, patches, width)
    clean_q = jnp.transpose(clean_q, (0, 2, 1, 3)).reshape(peers * patches, pairs * width)
    code = clean_q[:, heads * HD:heads * HD + 2].astype(jnp.float32)
    positions = (code[:, 0] * BLOCK + code[:, 1]).astype(jnp.int32)
    bounds = jnp.cumsum(doc_lengths)
    clean_documents = document_of(positions, bounds)

    query = project(tokens, w_query, q_bias, offset, True)
    match = places[:, None] == positions[None, :]
    present = jnp.any(match, axis=1)
    picked = jnp.dot(
        match.astype(jnp.bfloat16), clean_q, preferred_element_type=jnp.float32
    ).astype(jnp.bfloat16)[:, :heads * HD]
    query = jnp.where(present[:, None], picked, query)

    inverse = jnp.zeros((nblocks,), jnp.int32).at[block_order].set(
        jnp.arange(nblocks, dtype=jnp.int32)
    )
    patched_place = jnp.zeros((nblocks * BLOCK,), jnp.bool_).at[positions].set(True)

    window = MOST_DOC + BLOCK
    back = MOST_DOC // BLOCK
    seq_blocks = lax.dynamic_slice_in_dim(block_order, me * local_blocks, local_blocks)
    starts = seq_blocks * BLOCK
    wanted = seq_blocks[:, None] - back + jnp.arange(back + 1, dtype=jnp.int32)[None, :]
    window_slots = inverse[jnp.clip(wanted, 0, nblocks - 1)]
    window_blocks = (window_slots // local_blocks) * per_peer + window_slots % local_blocks
    window_kv = gathered.reshape(peers * per_peer, BLOCK, width)[window_blocks].reshape(
        local_blocks, window, width
    )
    key_places = starts[:, None] - MOST_DOC + jnp.arange(window, dtype=jnp.int32)[None, :]
    key_documents = document_of(key_places, bounds)
    window_patched = patched_place.reshape(nblocks, BLOCK)[jnp.clip(wanted, 0, nblocks - 1)]
    key_kept = (key_places >= 0) & ~window_patched.reshape(local_blocks, window)
    query_places = places.reshape(local_blocks, BLOCK)
    query_documents = documents.reshape(local_blocks, BLOCK)
    visible = (
        (query_documents[:, :, None] == key_documents[:, None, :])
        & (key_places[:, None, :] <= query_places[:, :, None])
        & key_kept[:, None, :]
    )[:, None]
    clean_visible = (
        (query_documents[:, :, None] == clean_documents[None, None, :])
        & (positions[None, None, :] <= query_places[:, :, None])
    )[:, None]
    score_scale = HD ** (-0.5)
    grouped = query.reshape(local_blocks, BLOCK, heads, HD)
    scores = (
        jnp.einsum(
            "bqhd,bkd->bhqk", grouped, window_kv[..., :HD], preferred_element_type=jnp.float32
        )
        * score_scale
    )
    clean_scores = (
        jnp.einsum(
            "bqhd,kd->bhqk", grouped, clean_kv[:, :HD], preferred_element_type=jnp.float32
        )
        * score_scale
    )
    masked = jnp.where(visible, scores, -1e30)
    clean_masked = jnp.where(clean_visible, clean_scores, -1e30)
    peak = jnp.maximum(
        jnp.max(masked, axis=-1, keepdims=True), jnp.max(clean_masked, axis=-1, keepdims=True)
    )
    weights = jnp.where(visible, jnp.exp(masked - peak), 0.0)
    clean_weights = jnp.where(clean_visible, jnp.exp(clean_masked - peak), 0.0)
    total = jnp.sum(weights, axis=-1) + jnp.sum(clean_weights, axis=-1)
    mixed = jnp.einsum(
        "bhqk,bkd->bqhd",
        weights.astype(jnp.bfloat16),
        window_kv[..., HD:],
        preferred_element_type=jnp.float32,
    ) + jnp.einsum(
        "bhqk,kd->bqhd",
        clean_weights.astype(jnp.bfloat16),
        clean_kv[:, HD:],
        preferred_element_type=jnp.float32,
    )
    out = mixed / jnp.transpose(total, (0, 2, 1))[..., None]
    return out.reshape(rows, heads * HD).astype(jnp.bfloat16)


def solution(mesh):
    in_specs = (
        P(("run", "ctx"), None),
        P(),
        P(),
        P(("run", "ctx")),
        P(("run", "ctx"), None),
        P(None, "tp"),
        P("tp"),
        P(None, "tp"),
        P("tp"),
        P(None, "tp"),
        P("tp"),
    )
    out_specs = P(("run", "ctx"), "tp")
    return jax.shard_map(body, mesh=mesh, in_specs=in_specs, out_specs=out_specs, check_vma=False)
```

```python
import jax
import jax.numpy as jnp
from jax import lax
from jax.sharding import PartitionSpec as P

HD = 128
BLOCK = 64
MOST_DOC = 1024


THETA = 1000000.0


def rotate(head_rows, offset):
    half = head_rows.shape[-1] // 2
    frequency = jnp.power(
        jnp.float32(THETA), -2.0 * jnp.arange(half, dtype=jnp.float32) / head_rows.shape[-1]
    )
    angles = offset.astype(jnp.float32)[:, None] * frequency[None, :]
    cosines = jnp.cos(angles)[:, None, :]
    sines = jnp.sin(angles)[:, None, :]
    first_half = head_rows[..., :half]
    second_half = head_rows[..., half:]
    return jnp.concatenate(
        [first_half * cosines - second_half * sines, second_half * cosines + first_half * sines],
        axis=-1,
    )


def project(source, weight, bias, offset, rotated):
    result = (
        jnp.dot(source, weight, preferred_element_type=jnp.float32)
        + bias.astype(jnp.float32)[None, :]
    )
    if rotated:
        result = rotate(result.reshape(source.shape[0], -1, HD), offset).reshape(
            source.shape[0], -1
        )
    return result.astype(jnp.bfloat16)


def slot_places(order, first_row, row_count):
    slots = first_row + jnp.arange(row_count, dtype=jnp.int32)
    owners = slots // BLOCK
    selector = owners[:, None] == jnp.arange(order.shape[0], dtype=jnp.int32)[None, :]
    picked = jnp.sum(jnp.where(selector, order[None, :], 0), axis=1)
    return picked * BLOCK + slots % BLOCK


def document_of(places, bounds):
    return jnp.sum((places[..., None] >= bounds).astype(jnp.int32), axis=-1)


def document_info(places, lengths):
    bounds = jnp.cumsum(lengths)
    passed = places[:, None] >= bounds[None, :]
    documents = jnp.sum(passed.astype(jnp.int32), axis=1)
    starts = jnp.sum(jnp.where(passed, lengths[None, :], 0), axis=1)
    return (documents, places - starts)


def body(
    tokens,
    block_order,
    doc_lengths,
    patch_pos,
    clean_rows,
    w_query,
    q_bias,
    w_key,
    k_bias,
    w_value,
    v_bias,
):
    rows = tokens.shape[0]
    patches = patch_pos.shape[0]
    nblocks = block_order.shape[0]
    heads = w_query.shape[1] // HD
    me = lax.axis_index("ctx")
    places = slot_places(block_order, me * rows, rows)
    documents, offset = document_info(places, doc_lengths)
    patch_offset = document_info(patch_pos, doc_lengths)[1]

    keys = project(tokens, w_key, k_bias, offset, True)
    values = project(tokens, w_value, v_bias, offset, False)
    clean_query = project(clean_rows, w_query, q_bias, patch_offset, True)
    clean_keys = project(clean_rows, w_key, k_bias, patch_offset, True)
    clean_values = project(clean_rows, w_value, v_bias, patch_offset, False)

    width = 2 * HD
    pairs = (heads + 1) // 2
    spare = pairs * width - heads * HD
    coded = jnp.stack(
        [(patch_pos // BLOCK).astype(jnp.bfloat16), (patch_pos % BLOCK).astype(jnp.bfloat16)], axis=1
    )
    padded_query = jnp.concatenate(
        [clean_query, coded, jnp.zeros((patches, spare - 2), jnp.bfloat16)], axis=1
    )
    parts = [
        jnp.concatenate([keys, values], axis=1),
        jnp.concatenate([clean_keys, clean_values], axis=1),
    ]
    parts += [padded_query[:, p * width:(p + 1) * width] for p in range(pairs)]
    packed = jnp.concatenate(parts, axis=0)
    lines = packed.shape[0]
    peers = lax.psum(1, "ctx")
    rightward = [(i, (i + 1) % peers) for i in range(peers)]
    leftward = [(i, (i - 1) % peers) for i in range(peers)]
    from_left, from_right = [], []
    going_right = going_left = packed
    for step in range(1, peers // 2 + 1):
        going_right = lax.ppermute(going_right, "ctx", rightward)
        from_left.append(going_right)
        if step < peers - peers // 2:
            going_left = lax.ppermute(going_left, "ctx", leftward)
            from_right.append(going_left)
    gathered = jnp.stack([packed] + from_right + from_left[::-1])
    per_peer = lines // BLOCK
    local_blocks = rows // BLOCK

    clean_kv = gathered[:, rows:rows + patches].reshape(peers * patches, width)
    clean_q = gathered[:, rows + patches:].reshape(peers, pairs, patches, width)
    clean_q = jnp.transpose(clean_q, (0, 2, 1, 3)).reshape(peers * patches, pairs * width)
    code = clean_q[:, heads * HD:heads * HD + 2].astype(jnp.float32)
    positions = (code[:, 0] * BLOCK + code[:, 1]).astype(jnp.int32)
    bounds = jnp.cumsum(doc_lengths)
    clean_documents = document_of(positions, bounds)

    query = project(tokens, w_query, q_bias, offset, True)
    match = places[:, None] == positions[None, :]
    present = jnp.any(match, axis=1)
    picked = jnp.dot(
        match.astype(jnp.bfloat16), clean_q, preferred_element_type=jnp.float32
    ).astype(jnp.bfloat16)[:, :heads * HD]
    query = jnp.where(present[:, None], picked, query)

    inverse = jnp.zeros((nblocks,), jnp.int32).at[block_order].set(
        jnp.arange(nblocks, dtype=jnp.int32)
    )
    patched_place = jnp.zeros((nblocks * BLOCK,), jnp.bool_).at[positions].set(True)

    window = MOST_DOC + BLOCK
    back = MOST_DOC // BLOCK
    seq_blocks = lax.dynamic_slice_in_dim(block_order, me * local_blocks, local_blocks)
    starts = seq_blocks * BLOCK
    wanted = seq_blocks[:, None] - back + jnp.arange(back + 1, dtype=jnp.int32)[None, :]
    window_slots = inverse[jnp.clip(wanted, 0, nblocks - 1)]
    relative = (window_slots // local_blocks - me + peers) % peers
    window_blocks = relative * per_peer + window_slots % local_blocks
    window_kv = gathered.reshape(peers * per_peer, BLOCK, width)[window_blocks].reshape(
        local_blocks, window, width
    )
    key_places = starts[:, None] - MOST_DOC + jnp.arange(window, dtype=jnp.int32)[None, :]
    key_documents = document_of(key_places, bounds)
    window_patched = patched_place.reshape(nblocks, BLOCK)[jnp.clip(wanted, 0, nblocks - 1)]
    key_kept = (key_places >= 0) & ~window_patched.reshape(local_blocks, window)
    query_places = places.reshape(local_blocks, BLOCK)
    query_documents = documents.reshape(local_blocks, BLOCK)
    visible = (
        (query_documents[:, :, None] == key_documents[:, None, :])
        & (key_places[:, None, :] <= query_places[:, :, None])
        & key_kept[:, None, :]
    )[:, None]
    clean_visible = (
        (query_documents[:, :, None] == clean_documents[None, None, :])
        & (positions[None, None, :] <= query_places[:, :, None])
    )[:, None]
    score_scale = HD ** (-0.5)
    grouped = query.reshape(local_blocks, BLOCK, heads, HD)
    scores = (
        jnp.einsum(
            "bqhd,bkd->bhqk", grouped, window_kv[..., :HD], preferred_element_type=jnp.float32
        )
        * score_scale
    )
    clean_scores = (
        jnp.einsum(
            "bqhd,kd->bhqk", grouped, clean_kv[:, :HD], preferred_element_type=jnp.float32
        )
        * score_scale
    )
    masked = jnp.where(visible, scores, -1e30)
    clean_masked = jnp.where(clean_visible, clean_scores, -1e30)
    peak = jnp.maximum(
        jnp.max(masked, axis=-1, keepdims=True), jnp.max(clean_masked, axis=-1, keepdims=True)
    )
    weights = jnp.where(visible, jnp.exp(masked - peak), 0.0)
    clean_weights = jnp.where(clean_visible, jnp.exp(clean_masked - peak), 0.0)
    total = jnp.sum(weights, axis=-1) + jnp.sum(clean_weights, axis=-1)
    mixed = jnp.einsum(
        "bhqk,bkd->bqhd",
        weights.astype(jnp.bfloat16),
        window_kv[..., HD:],
        preferred_element_type=jnp.float32,
    ) + jnp.einsum(
        "bhqk,kd->bqhd",
        clean_weights.astype(jnp.bfloat16),
        clean_kv[:, HD:],
        preferred_element_type=jnp.float32,
    )
    out = mixed / jnp.transpose(total, (0, 2, 1))[..., None]
    return out.reshape(rows, heads * HD).astype(jnp.bfloat16)


def solution(mesh):
    in_specs = (
        P(("run", "ctx"), None),
        P(),
        P(),
        P(("run", "ctx")),
        P(("run", "ctx"), None),
        P(None, "tp"),
        P("tp"),
        P(None, "tp"),
        P("tp"),
        P(None, "tp"),
        P("tp"),
    )
    out_specs = P(("run", "ctx"), "tp")
    return jax.shard_map(body, mesh=mesh, in_specs=in_specs, out_specs=out_specs, check_vma=False)
```

```python
import jax
import jax.numpy as jnp
from jax import lax
from jax.sharding import PartitionSpec as P

HD = 128
BLOCK = 64
MOST_DOC = 1024


THETA = 1000000.0


def rotate(head_rows, offset):
    half = head_rows.shape[-1] // 2
    frequency = jnp.power(
        jnp.float32(THETA), -2.0 * jnp.arange(half, dtype=jnp.float32) / head_rows.shape[-1]
    )
    angles = offset.astype(jnp.float32)[:, None] * frequency[None, :]
    cosines = jnp.cos(angles)[:, None, :]
    sines = jnp.sin(angles)[:, None, :]
    first_half = head_rows[..., :half]
    second_half = head_rows[..., half:]
    return jnp.concatenate(
        [first_half * cosines - second_half * sines, second_half * cosines + first_half * sines],
        axis=-1,
    )


def project(source, weight, bias, offset, rotated):
    result = (
        jnp.dot(source, weight, preferred_element_type=jnp.float32)
        + bias.astype(jnp.float32)[None, :]
    )
    if rotated:
        result = rotate(result.reshape(source.shape[0], -1, HD), offset).reshape(
            source.shape[0], -1
        )
    return result.astype(jnp.bfloat16)


def slot_places(order, first_row, row_count):
    slots = first_row + jnp.arange(row_count, dtype=jnp.int32)
    owners = slots // BLOCK
    selector = owners[:, None] == jnp.arange(order.shape[0], dtype=jnp.int32)[None, :]
    picked = jnp.sum(jnp.where(selector, order[None, :], 0), axis=1)
    return picked * BLOCK + slots % BLOCK


def document_of(places, bounds):
    return jnp.sum((places[..., None] >= bounds).astype(jnp.int32), axis=-1)


def document_info(places, lengths):
    bounds = jnp.cumsum(lengths)
    passed = places[:, None] >= bounds[None, :]
    documents = jnp.sum(passed.astype(jnp.int32), axis=1)
    starts = jnp.sum(jnp.where(passed, lengths[None, :], 0), axis=1)
    return (documents, places - starts)


def body(
    tokens,
    block_order,
    doc_lengths,
    patch_pos,
    clean_rows,
    w_query,
    q_bias,
    w_key,
    k_bias,
    w_value,
    v_bias,
):
    rows = tokens.shape[0]
    patches = patch_pos.shape[0]
    nblocks = block_order.shape[0]
    heads = w_query.shape[1] // HD
    me = lax.axis_index("ctx")
    places = slot_places(block_order, me * rows, rows)
    documents, offset = document_info(places, doc_lengths)
    patch_offset = document_info(patch_pos, doc_lengths)[1]

    keys = project(tokens, w_key, k_bias, offset, True)
    values = project(tokens, w_value, v_bias, offset, False)
    clean_query = project(clean_rows, w_query, q_bias, patch_offset, True)
    clean_keys = project(clean_rows, w_key, k_bias, patch_offset, True)
    clean_values = project(clean_rows, w_value, v_bias, patch_offset, False)

    width = 2 * HD
    pairs = (heads + 1) // 2
    spare = pairs * width - heads * HD
    coded = jnp.stack(
        [(patch_pos // BLOCK).astype(jnp.bfloat16), (patch_pos % BLOCK).astype(jnp.bfloat16)], axis=1
    )
    padded_query = jnp.concatenate(
        [clean_query, coded, jnp.zeros((patches, spare - 2), jnp.bfloat16)], axis=1
    )
    parts = [
        jnp.concatenate([keys, values], axis=1),
        jnp.concatenate([clean_keys, clean_values], axis=1),
    ]
    parts += [padded_query[:, p * width:(p + 1) * width] for p in range(pairs)]
    packed = jnp.concatenate(parts, axis=0)
    lines = packed.shape[0]
    gathered = lax.all_gather(packed, "ctx", axis=0, tiled=False)
    peers = gathered.shape[0]
    per_peer = lines // BLOCK
    local_blocks = rows // BLOCK

    clean_kv = gathered[:, rows:rows + patches].reshape(peers * patches, width)
    first_q = rows + patches
    last = first_q + (pairs - 1) * patches
    code = gathered[:, last:last + patches, heads * HD - (pairs - 1) * width:][..., :2]
    code = code.reshape(peers * patches, 2).astype(jnp.float32)
    positions = (code[:, 0] * BLOCK + code[:, 1]).astype(jnp.int32)
    bounds = jnp.cumsum(doc_lengths)
    clean_documents = document_of(positions, bounds)

    query = project(tokens, w_query, q_bias, offset, True)
    match = (places[:, None] == positions[None, :]).astype(jnp.bfloat16)
    present = jnp.any(places[:, None] == positions[None, :], axis=1)
    picked = jnp.concatenate(
        [
            jnp.dot(
                match,
                gathered[:, first_q + p * patches:first_q + (p + 1) * patches].reshape(
                    peers * patches, width
                ),
                preferred_element_type=jnp.float32,
            )
            for p in range(pairs)
        ],
        axis=1,
    ).astype(jnp.bfloat16)[:, :heads * HD]
    query = jnp.where(present[:, None], picked, query)

    inverse = jnp.zeros((nblocks,), jnp.int32).at[block_order].set(
        jnp.arange(nblocks, dtype=jnp.int32)
    )
    block_hit = (positions[None, :] // BLOCK == jnp.arange(nblocks, dtype=jnp.int32)[:, None])
    row_hit = (positions[:, None] % BLOCK == jnp.arange(BLOCK, dtype=jnp.int32)[None, :])
    patched_place = jnp.dot(
        block_hit.astype(jnp.bfloat16), row_hit.astype(jnp.bfloat16),
        preferred_element_type=jnp.float32,
    ) > 0.5

    window = MOST_DOC + BLOCK
    back = MOST_DOC // BLOCK
    seq_blocks = lax.dynamic_slice_in_dim(block_order, me * local_blocks, local_blocks)
    starts = seq_blocks * BLOCK
    wanted = seq_blocks[:, None] - back + jnp.arange(back + 1, dtype=jnp.int32)[None, :]
    window_slots = inverse[jnp.clip(wanted, 0, nblocks - 1)]
    window_blocks = (window_slots // local_blocks) * per_peer + window_slots % local_blocks
    window_kv = gathered.reshape(peers * per_peer, BLOCK, width)[window_blocks].reshape(
        local_blocks, window, width
    )
    key_places = starts[:, None] - MOST_DOC + jnp.arange(window, dtype=jnp.int32)[None, :]
    key_documents = document_of(key_places, bounds)
    window_patched = patched_place[jnp.clip(wanted, 0, nblocks - 1)]
    key_kept = (key_places >= 0) & ~window_patched.reshape(local_blocks, window)
    query_places = places.reshape(local_blocks, BLOCK)
    query_documents = documents.reshape(local_blocks, BLOCK)
    visible = (
        (query_documents[:, :, None] == key_documents[:, None, :])
        & (key_places[:, None, :] <= query_places[:, :, None])
        & key_kept[:, None, :]
    )[:, None]
    clean_visible = (
        (query_documents[:, :, None] == clean_documents[None, None, :])
        & (positions[None, None, :] <= query_places[:, :, None])
    )[:, None]
    score_scale = HD ** (-0.5)
    grouped = query.reshape(local_blocks, BLOCK, heads, HD)
    scores = (
        jnp.einsum(
            "bqhd,bkd->bhqk", grouped, window_kv[..., :HD], preferred_element_type=jnp.float32
        )
        * score_scale
    )
    clean_scores = (
        jnp.einsum(
            "bqhd,kd->bhqk", grouped, clean_kv[:, :HD], preferred_element_type=jnp.float32
        )
        * score_scale
    )
    masked = jnp.where(visible, scores, -1e30)
    clean_masked = jnp.where(clean_visible, clean_scores, -1e30)
    peak = jnp.maximum(
        jnp.max(masked, axis=-1, keepdims=True), jnp.max(clean_masked, axis=-1, keepdims=True)
    )
    weights = jnp.where(visible, jnp.exp(masked - peak), 0.0)
    clean_weights = jnp.where(clean_visible, jnp.exp(clean_masked - peak), 0.0)
    total = jnp.sum(weights, axis=-1) + jnp.sum(clean_weights, axis=-1)
    mixed = jnp.einsum(
        "bhqk,bkd->bqhd",
        weights.astype(jnp.bfloat16),
        window_kv[..., HD:],
        preferred_element_type=jnp.float32,
    ) + jnp.einsum(
        "bhqk,kd->bqhd",
        clean_weights.astype(jnp.bfloat16),
        clean_kv[:, HD:],
        preferred_element_type=jnp.float32,
    )
    out = mixed / jnp.transpose(total, (0, 2, 1))[..., None]
    return out.reshape(rows, heads * HD).astype(jnp.bfloat16)


def solution(mesh):
    in_specs = (
        P(("run", "ctx"), None),
        P(),
        P(),
        P(("run", "ctx")),
        P(("run", "ctx"), None),
        P(None, "tp"),
        P("tp"),
        P(None, "tp"),
        P("tp"),
        P(None, "tp"),
        P("tp"),
    )
    out_specs = P(("run", "ctx"), "tp")
    return jax.shard_map(body, mesh=mesh, in_specs=in_specs, out_specs=out_specs, check_vma=False)
```

```python
import jax
import jax.numpy as jnp
from jax import lax
from jax.experimental import pallas as pl
from jax.experimental.pallas import tpu as pltpu
from jax.sharding import PartitionSpec as P

HD = 128
BLOCK = 64
MOST_DOC = 1024


THETA = 1000000.0


def rotate(head_rows, offset):
    half = head_rows.shape[-1] // 2
    frequency = jnp.power(
        jnp.float32(THETA), -2.0 * jnp.arange(half, dtype=jnp.float32) / head_rows.shape[-1]
    )
    angles = offset.astype(jnp.float32)[:, None] * frequency[None, :]
    cosines = jnp.cos(angles)[:, None, :]
    sines = jnp.sin(angles)[:, None, :]
    first_half = head_rows[..., :half]
    second_half = head_rows[..., half:]
    return jnp.concatenate(
        [first_half * cosines - second_half * sines, second_half * cosines + first_half * sines],
        axis=-1,
    )


def project(source, weight, bias, offset, rotated):
    result = (
        jnp.dot(source, weight, preferred_element_type=jnp.float32)
        + bias.astype(jnp.float32)[None, :]
    )
    if rotated:
        result = rotate(result.reshape(source.shape[0], -1, HD), offset).reshape(
            source.shape[0], -1
        )
    return result.astype(jnp.bfloat16)


def slot_places(order, first_row, row_count):
    slots = first_row + jnp.arange(row_count, dtype=jnp.int32)
    owners = slots // BLOCK
    selector = owners[:, None] == jnp.arange(order.shape[0], dtype=jnp.int32)[None, :]
    picked = jnp.sum(jnp.where(selector, order[None, :], 0), axis=1)
    return picked * BLOCK + slots % BLOCK


def document_of(places, bounds):
    return jnp.sum((places[..., None] >= bounds).astype(jnp.int32), axis=-1)


def document_info(places, lengths):
    bounds = jnp.cumsum(lengths)
    passed = places[:, None] >= bounds[None, :]
    documents = jnp.sum(passed.astype(jnp.int32), axis=1)
    starts = jnp.sum(jnp.where(passed, lengths[None, :], 0), axis=1)
    return (documents, places - starts)


def body(
    tokens,
    block_order,
    doc_lengths,
    patch_pos,
    clean_rows,
    w_query,
    q_bias,
    w_key,
    k_bias,
    w_value,
    v_bias,
):
    rows = tokens.shape[0]
    patches = patch_pos.shape[0]
    nblocks = block_order.shape[0]
    heads = w_query.shape[1] // HD
    me = lax.axis_index("ctx")
    places = slot_places(block_order, me * rows, rows)
    documents, offset = document_info(places, doc_lengths)
    patch_offset = document_info(patch_pos, doc_lengths)[1]

    keys = project(tokens, w_key, k_bias, offset, True)
    values = project(tokens, w_value, v_bias, offset, False)
    clean_query = project(clean_rows, w_query, q_bias, patch_offset, True)
    clean_keys = project(clean_rows, w_key, k_bias, patch_offset, True)
    clean_values = project(clean_rows, w_value, v_bias, patch_offset, False)

    width = 2 * HD
    pairs = (heads + 1) // 2
    spare = pairs * width - heads * HD
    coded = jnp.stack(
        [(patch_pos // BLOCK).astype(jnp.bfloat16), (patch_pos % BLOCK).astype(jnp.bfloat16)], axis=1
    )
    padded_query = jnp.concatenate(
        [clean_query, coded, jnp.zeros((patches, spare - 2), jnp.bfloat16)], axis=1
    )
    parts = [
        jnp.concatenate([keys, values], axis=1),
        jnp.concatenate([clean_keys, clean_values], axis=1),
    ]
    parts += [padded_query[:, p * width:(p + 1) * width] for p in range(pairs)]
    packed = jnp.concatenate(parts, axis=0)
    lines = packed.shape[0]
    gathered = lax.all_gather(packed, "ctx", axis=0, tiled=False)
    peers = gathered.shape[0]
    per_peer = lines // BLOCK
    local_blocks = rows // BLOCK

    first_q = rows + patches
    last = first_q + (pairs - 1) * patches
    code = gathered[:, last:last + patches, heads * HD - (pairs - 1) * width:][..., :2]
    code = code.reshape(peers * patches, 2).astype(jnp.float32)
    positions = (code[:, 0] * BLOCK + code[:, 1]).astype(jnp.int32)
    bounds = jnp.cumsum(doc_lengths)
    clean_documents = document_of(positions, bounds)
    query = project(tokens, w_query, q_bias, offset, True)

    inverse = jnp.zeros((nblocks,), jnp.int32).at[block_order].set(
        jnp.arange(nblocks, dtype=jnp.int32)
    )
    block_hit = (positions[None, :] // BLOCK == jnp.arange(nblocks, dtype=jnp.int32)[:, None])
    row_hit = (positions[:, None] % BLOCK == jnp.arange(BLOCK, dtype=jnp.int32)[None, :])
    patched_place = jnp.dot(
        block_hit.astype(jnp.bfloat16), row_hit.astype(jnp.bfloat16),
        preferred_element_type=jnp.float32,
    ) > 0.5

    back = MOST_DOC // BLOCK + 1
    window = (back + 1) * BLOCK
    seq_blocks = lax.dynamic_slice_in_dim(block_order, me * local_blocks, local_blocks)
    wanted = seq_blocks[:, None] - back + jnp.arange(back + 1, dtype=jnp.int32)[None, :]
    window_slots = inverse[jnp.clip(wanted, 0, nblocks - 1)]
    window_blocks = (window_slots // local_blocks) * per_peer + window_slots % local_blocks
    key_places = seq_blocks[:, None] * BLOCK - back * BLOCK + jnp.arange(window, dtype=jnp.int32)[None, :]
    key_documents = document_of(key_places, bounds)
    window_patched = patched_place[jnp.clip(wanted, 0, nblocks - 1)].reshape(local_blocks, window)
    key_kept = ((key_places >= 0) & ~window_patched).astype(jnp.int32)

    return attend(
        window_blocks.reshape(-1),
        gathered.reshape(peers * lines, width),
        query,
        places[:, None],
        documents[:, None],
        key_places,
        key_documents,
        key_kept,
        positions[None, :],
        clean_documents[None, :],
        heads=heads,
        patches=patches,
        lines=lines,
        pairs=pairs,
        back=back,
    )


def attend(window_blocks, gathered, query, query_places, query_documents, key_places,
           key_documents, key_kept, clean_places, clean_documents, *, heads, patches, lines,
           pairs, back):
    rows = query.shape[0]
    width = gathered.shape[1]
    peers = gathered.shape[0] // lines
    local_blocks = rows // BLOCK
    window = (back + 1) * BLOCK
    clean_count = peers * patches
    score_scale = HD ** (-0.5)

    def kernel(blocks_ref, g_ref, q_ref, qp_ref, qd_ref, kp_ref, kd_ref, kk_ref, cp_ref, cd_ref,
               out_ref, window_kv, clean_kv, clean_q):
        for p in range(peers):
            base = p * lines + rows
            clean_kv[p * patches:(p + 1) * patches, :] = g_ref[base:base + patches, :]
            for k in range(pairs):
                at = base + patches + k * patches
                clean_q[p * patches:(p + 1) * patches, k * width:(k + 1) * width] = g_ref[at:at + patches, :]
        match = qp_ref[...] == cp_ref[...]
        hit = match.astype(jnp.float32)
        present = jnp.sum(hit, axis=1, keepdims=True) > 0.5
        picked = jnp.dot(
            hit.astype(jnp.bfloat16), clean_q[...], preferred_element_type=jnp.float32
        ).astype(jnp.bfloat16)
        clean_visible_all = qd_ref[...] == cd_ref[...]
        for b in range(local_blocks):
            for j in range(back + 1):
                block = blocks_ref[b * (back + 1) + j]
                start = pl.multiple_of(block * BLOCK, BLOCK)
                window_kv[j * BLOCK:(j + 1) * BLOCK, :] = g_ref[pl.ds(start, BLOCK), :]
            rows_at = slice(b * BLOCK, (b + 1) * BLOCK)
            qp = qp_ref[rows_at, :]
            qd = qd_ref[rows_at, :]
            kp = kp_ref[b:b + 1, :]
            visible = (qd == kd_ref[b:b + 1, :]) & (kp <= qp) & (kk_ref[b:b + 1, :] != 0)
            clean_visible = clean_visible_all[rows_at, :] & (cp_ref[...] <= qp)
            block_present = present[rows_at, :]
            for h in range(heads):
                cols = slice(h * HD, (h + 1) * HD)
                q = jnp.where(block_present, picked[rows_at, cols], q_ref[rows_at, cols])
                scores = lax.dot_general(
                    q, window_kv[:, :HD], (((1,), (1,)), ((), ())),
                    preferred_element_type=jnp.float32,
                ) * score_scale
                clean_scores = lax.dot_general(
                    q, clean_kv[:, :HD], (((1,), (1,)), ((), ())),
                    preferred_element_type=jnp.float32,
                ) * score_scale
                masked = jnp.where(visible, scores, -1e30)
                clean_masked = jnp.where(clean_visible, clean_scores, -1e30)
                peak = jnp.maximum(
                    jnp.max(masked, axis=1, keepdims=True),
                    jnp.max(clean_masked, axis=1, keepdims=True),
                )
                weights = jnp.where(visible, jnp.exp(masked - peak), 0.0)
                clean_weights = jnp.where(clean_visible, jnp.exp(clean_masked - peak), 0.0)
                total = jnp.sum(weights, axis=1, keepdims=True) + jnp.sum(
                    clean_weights, axis=1, keepdims=True
                )
                mixed = jnp.dot(
                    weights.astype(jnp.bfloat16), window_kv[:, HD:],
                    preferred_element_type=jnp.float32,
                ) + jnp.dot(
                    clean_weights.astype(jnp.bfloat16), clean_kv[:, HD:],
                    preferred_element_type=jnp.float32,
                )
                out_ref[rows_at, cols] = (mixed / total).astype(out_ref.dtype)

    full = lambda shape: pl.BlockSpec(shape, lambda i, *_: (0,) * len(shape))
    operands = (gathered, query, query_places, query_documents, key_places, key_documents,
                key_kept, clean_places, clean_documents)
    return pl.pallas_call(
        kernel,
        out_shape=jax.ShapeDtypeStruct(query.shape, query.dtype),
        grid_spec=pltpu.PrefetchScalarGridSpec(
            num_scalar_prefetch=1,
            grid=(1,),
            in_specs=[full(x.shape) for x in operands],
            out_specs=full(query.shape),
            scratch_shapes=[
                pltpu.VMEM((window, width), jnp.bfloat16),
                pltpu.VMEM((clean_count, width), jnp.bfloat16),
                pltpu.VMEM((clean_count, pairs * width), jnp.bfloat16),
            ],
        ),
        compiler_params=pltpu.CompilerParams(vmem_limit_bytes=48 * 1024 * 1024),
    )(window_blocks, *operands)


def solution(mesh):
    in_specs = (
        P(("run", "ctx"), None),
        P(),
        P(),
        P(("run", "ctx")),
        P(("run", "ctx"), None),
        P(None, "tp"),
        P("tp"),
        P(None, "tp"),
        P("tp"),
        P(None, "tp"),
        P("tp"),
    )
    out_specs = P(("run", "ctx"), "tp")
    return jax.shard_map(body, mesh=mesh, in_specs=in_specs, out_specs=out_specs, check_vma=False)
```

```python
import jax
import jax.numpy as jnp
from jax import lax
from jax.experimental import pallas as pl
from jax.experimental.pallas import tpu as pltpu
from jax.sharding import PartitionSpec as P

HD = 128
BLOCK = 64
MOST_DOC = 1024


THETA = 1000000.0


def rotate(head_rows, offset):
    half = head_rows.shape[-1] // 2
    frequency = jnp.power(
        jnp.float32(THETA), -2.0 * jnp.arange(half, dtype=jnp.float32) / head_rows.shape[-1]
    )
    angles = offset.astype(jnp.float32)[:, None] * frequency[None, :]
    cosines = jnp.cos(angles)[:, None, :]
    sines = jnp.sin(angles)[:, None, :]
    first_half = head_rows[..., :half]
    second_half = head_rows[..., half:]
    return jnp.concatenate(
        [first_half * cosines - second_half * sines, second_half * cosines + first_half * sines],
        axis=-1,
    )


def project(source, weight, bias, offset, rotated):
    result = (
        jnp.dot(source, weight, preferred_element_type=jnp.float32)
        + bias.astype(jnp.float32)[None, :]
    )
    if rotated:
        result = rotate(result.reshape(source.shape[0], -1, HD), offset).reshape(
            source.shape[0], -1
        )
    return result.astype(jnp.bfloat16)


def slot_places(order, first_row, row_count):
    slots = first_row + jnp.arange(row_count, dtype=jnp.int32)
    owners = slots // BLOCK
    selector = owners[:, None] == jnp.arange(order.shape[0], dtype=jnp.int32)[None, :]
    picked = jnp.sum(jnp.where(selector, order[None, :], 0), axis=1)
    return picked * BLOCK + slots % BLOCK


def document_of(places, bounds):
    return jnp.sum((places[..., None] >= bounds).astype(jnp.int32), axis=-1)


def document_info(places, lengths):
    bounds = jnp.cumsum(lengths)
    passed = places[:, None] >= bounds[None, :]
    documents = jnp.sum(passed.astype(jnp.int32), axis=1)
    starts = jnp.sum(jnp.where(passed, lengths[None, :], 0), axis=1)
    return (documents, places - starts)


def body(
    tokens,
    block_order,
    doc_lengths,
    patch_pos,
    clean_rows,
    w_query,
    q_bias,
    w_key,
    k_bias,
    w_value,
    v_bias,
):
    rows = tokens.shape[0]
    patches = patch_pos.shape[0]
    nblocks = block_order.shape[0]
    heads = w_query.shape[1] // HD
    me = lax.axis_index("ctx")
    places = slot_places(block_order, me * rows, rows)
    documents, offset = document_info(places, doc_lengths)
    patch_offset = document_info(patch_pos, doc_lengths)[1]

    width = 2 * HD
    pairs = (heads + 1) // 2
    coded = jnp.zeros((patches, HD), jnp.bfloat16)
    coded = coded.at[:, 0].set((patch_pos // BLOCK).astype(jnp.bfloat16))
    coded = coded.at[:, 1].set((patch_pos % BLOCK).astype(jnp.bfloat16))
    packed = pack(tokens, clean_rows, w_query, w_key, w_value,
                  q_bias.astype(jnp.float32)[None, :], k_bias.astype(jnp.float32)[None, :],
                  v_bias.astype(jnp.float32)[None, :], *rope_tables(offset),
                  *rope_tables(patch_offset), coded)
    lines = packed.shape[0]
    gathered = lax.all_gather(packed, "ctx", axis=0, tiled=False)
    peers = gathered.shape[0]
    per_peer = lines // BLOCK
    local_blocks = rows // BLOCK

    first_q = rows + patches
    last = first_q + (pairs - 1) * patches
    code = gathered[:, last:last + patches, heads * HD - (pairs - 1) * width:][..., :2]
    code = code.reshape(peers * patches, 2).astype(jnp.float32)
    positions = (code[:, 0] * BLOCK + code[:, 1]).astype(jnp.int32)
    bounds = jnp.cumsum(doc_lengths)
    clean_documents = document_of(positions, bounds)
    query = project(tokens, w_query, q_bias, offset, True)

    inverse = jnp.zeros((nblocks,), jnp.int32).at[block_order].set(
        jnp.arange(nblocks, dtype=jnp.int32)
    )
    block_hit = (positions[None, :] // BLOCK == jnp.arange(nblocks, dtype=jnp.int32)[:, None])
    row_hit = (positions[:, None] % BLOCK == jnp.arange(BLOCK, dtype=jnp.int32)[None, :])
    patched_place = jnp.dot(
        block_hit.astype(jnp.bfloat16), row_hit.astype(jnp.bfloat16),
        preferred_element_type=jnp.float32,
    ) > 0.5

    back = MOST_DOC // BLOCK + 1
    window = (back + 1) * BLOCK
    seq_blocks = lax.dynamic_slice_in_dim(block_order, me * local_blocks, local_blocks)
    wanted = seq_blocks[:, None] - back + jnp.arange(back + 1, dtype=jnp.int32)[None, :]
    window_slots = inverse[jnp.clip(wanted, 0, nblocks - 1)]
    window_blocks = (window_slots // local_blocks) * per_peer + window_slots % local_blocks
    key_places = seq_blocks[:, None] * BLOCK - back * BLOCK + jnp.arange(window, dtype=jnp.int32)[None, :]
    key_documents = document_of(key_places, bounds)
    window_patched = patched_place[jnp.clip(wanted, 0, nblocks - 1)].reshape(local_blocks, window)
    key_kept = ((key_places >= 0) & ~window_patched).astype(jnp.int32)

    return attend(
        window_blocks.reshape(-1),
        gathered.reshape(peers * lines, width),
        query,
        places[:, None],
        documents[:, None],
        key_places,
        key_documents,
        key_kept,
        positions[None, :],
        clean_documents[None, :],
        heads=heads,
        patches=patches,
        lines=lines,
        pairs=pairs,
        back=back,
    )


def rope_tables(offset):
    half = HD // 2
    frequency = jnp.power(jnp.float32(THETA), -2.0 * jnp.arange(half, dtype=jnp.float32) / HD)
    angles = offset.astype(jnp.float32)[:, None] * frequency[None, :]
    cosines, sines = jnp.cos(angles), jnp.sin(angles)
    return (jnp.concatenate([cosines, cosines], axis=1), jnp.concatenate([-sines, sines], axis=1))


def pack(tokens, clean_rows, w_query, w_key, w_value, q_bias, k_bias, v_bias, cos_rows,
         sin_rows, cos_clean, sin_clean, coded):
    rows = tokens.shape[0]
    patches = clean_rows.shape[0]
    heads = w_query.shape[1] // HD
    width = 2 * HD
    pairs = (heads + 1) // 2
    lines = rows + patches + pairs * patches

    def kernel(t_ref, c_ref, wq_ref, wk_ref, wv_ref, qb_ref, kb_ref, vb_ref, cr_ref, sr_ref,
               cc_ref, sc_ref, code_ref, out_ref):
        def rope(x, cos, sin):
            return x * cos + pltpu.roll(x, HD // 2, 1) * sin

        t = t_ref[...]
        c = c_ref[...]
        keys = jnp.dot(t, wk_ref[...], preferred_element_type=jnp.float32) + kb_ref[...]
        values = jnp.dot(t, wv_ref[...], preferred_element_type=jnp.float32) + vb_ref[...]
        out_ref[0:rows, 0:HD] = rope(keys, cr_ref[...], sr_ref[...]).astype(out_ref.dtype)
        out_ref[0:rows, HD:width] = values.astype(out_ref.dtype)
        keys = jnp.dot(c, wk_ref[...], preferred_element_type=jnp.float32) + kb_ref[...]
        values = jnp.dot(c, wv_ref[...], preferred_element_type=jnp.float32) + vb_ref[...]
        out_ref[rows:rows + patches, 0:HD] = rope(keys, cc_ref[...], sc_ref[...]).astype(out_ref.dtype)
        out_ref[rows:rows + patches, HD:width] = values.astype(out_ref.dtype)
        query = jnp.dot(c, wq_ref[...], preferred_element_type=jnp.float32) + qb_ref[...]
        for h in range(heads):
            at = rows + patches + (h // 2) * patches
            col = (h % 2) * HD
            head = rope(query[:, h * HD:(h + 1) * HD], cc_ref[...], sc_ref[...])
            out_ref[at:at + patches, col:col + HD] = head.astype(out_ref.dtype)
        at = rows + patches + (pairs - 1) * patches
        col = (heads % 2) * HD
        out_ref[at:at + patches, col:col + HD] = code_ref[...]
        if col + HD < width:
            out_ref[at:at + patches, col + HD:width] = jnp.zeros((patches, width - col - HD), out_ref.dtype)

    operands = (tokens, clean_rows, w_query, w_key, w_value, q_bias, k_bias, v_bias, cos_rows,
                sin_rows, cos_clean, sin_clean, coded)
    full = lambda shape: pl.BlockSpec(shape, lambda i: (0,) * len(shape))
    return pl.pallas_call(
        kernel,
        out_shape=jax.ShapeDtypeStruct((lines, width), jnp.bfloat16),
        grid=(1,),
        in_specs=[full(x.shape) for x in operands],
        out_specs=full((lines, width)),
        compiler_params=pltpu.CompilerParams(vmem_limit_bytes=48 * 1024 * 1024),
    )(*operands)


def attend(window_blocks, gathered, query, query_places, query_documents, key_places,
           key_documents, key_kept, clean_places, clean_documents, *, heads, patches, lines,
           pairs, back):
    rows = query.shape[0]
    width = gathered.shape[1]
    peers = gathered.shape[0] // lines
    local_blocks = rows // BLOCK
    window = (back + 1) * BLOCK
    clean_count = peers * patches
    score_scale = HD ** (-0.5)

    def kernel(blocks_ref, g_ref, q_ref, qp_ref, qd_ref, kp_ref, kd_ref, kk_ref, cp_ref, cd_ref,
               out_ref, window_kv, clean_kv, clean_q):
        for p in range(peers):
            base = p * lines + rows
            clean_kv[p * patches:(p + 1) * patches, :] = g_ref[base:base + patches, :]
            for k in range(pairs):
                at = base + patches + k * patches
                clean_q[p * patches:(p + 1) * patches, k * width:(k + 1) * width] = g_ref[at:at + patches, :]
        match = qp_ref[...] == cp_ref[...]
        hit = match.astype(jnp.float32)
        present = jnp.sum(hit, axis=1, keepdims=True) > 0.5
        picked = jnp.dot(
            hit.astype(jnp.bfloat16), clean_q[...], preferred_element_type=jnp.float32
        ).astype(jnp.bfloat16)
        clean_visible_all = qd_ref[...] == cd_ref[...]
        for b in range(local_blocks):
            for j in range(back + 1):
                block = blocks_ref[b * (back + 1) + j]
                start = pl.multiple_of(block * BLOCK, BLOCK)
                window_kv[j * BLOCK:(j + 1) * BLOCK, :] = g_ref[pl.ds(start, BLOCK), :]
            rows_at = slice(b * BLOCK, (b + 1) * BLOCK)
            qp = qp_ref[rows_at, :]
            qd = qd_ref[rows_at, :]
            kp = kp_ref[b:b + 1, :]
            visible = (qd == kd_ref[b:b + 1, :]) & (kp <= qp) & (kk_ref[b:b + 1, :] != 0)
            clean_visible = clean_visible_all[rows_at, :] & (cp_ref[...] <= qp)
            block_present = present[rows_at, :]
            for h in range(heads):
                cols = slice(h * HD, (h + 1) * HD)
                q = jnp.where(block_present, picked[rows_at, cols], q_ref[rows_at, cols])
                scores = lax.dot_general(
                    q, window_kv[:, :HD], (((1,), (1,)), ((), ())),
                    preferred_element_type=jnp.float32,
                ) * score_scale
                clean_scores = lax.dot_general(
                    q, clean_kv[:, :HD], (((1,), (1,)), ((), ())),
                    preferred_element_type=jnp.float32,
                ) * score_scale
                masked = jnp.where(visible, scores, -1e30)
                clean_masked = jnp.where(clean_visible, clean_scores, -1e30)
                peak = jnp.maximum(
                    jnp.max(masked, axis=1, keepdims=True),
                    jnp.max(clean_masked, axis=1, keepdims=True),
                )
                weights = jnp.where(visible, jnp.exp(masked - peak), 0.0)
                clean_weights = jnp.where(clean_visible, jnp.exp(clean_masked - peak), 0.0)
                total = jnp.sum(weights, axis=1, keepdims=True) + jnp.sum(
                    clean_weights, axis=1, keepdims=True
                )
                mixed = jnp.dot(
                    weights.astype(jnp.bfloat16), window_kv[:, HD:],
                    preferred_element_type=jnp.float32,
                ) + jnp.dot(
                    clean_weights.astype(jnp.bfloat16), clean_kv[:, HD:],
                    preferred_element_type=jnp.float32,
                )
                out_ref[rows_at, cols] = (mixed / total).astype(out_ref.dtype)

    full = lambda shape: pl.BlockSpec(shape, lambda i, *_: (0,) * len(shape))
    operands = (gathered, query, query_places, query_documents, key_places, key_documents,
                key_kept, clean_places, clean_documents)
    return pl.pallas_call(
        kernel,
        out_shape=jax.ShapeDtypeStruct(query.shape, query.dtype),
        grid_spec=pltpu.PrefetchScalarGridSpec(
            num_scalar_prefetch=1,
            grid=(1,),
            in_specs=[full(x.shape) for x in operands],
            out_specs=full(query.shape),
            scratch_shapes=[
                pltpu.VMEM((window, width), jnp.bfloat16),
                pltpu.VMEM((clean_count, width), jnp.bfloat16),
                pltpu.VMEM((clean_count, pairs * width), jnp.bfloat16),
            ],
        ),
        compiler_params=pltpu.CompilerParams(vmem_limit_bytes=48 * 1024 * 1024),
    )(window_blocks, *operands)


def solution(mesh):
    in_specs = (
        P(("run", "ctx"), None),
        P(),
        P(),
        P(("run", "ctx")),
        P(("run", "ctx"), None),
        P(None, "tp"),
        P("tp"),
        P(None, "tp"),
        P("tp"),
        P(None, "tp"),
        P("tp"),
    )
    out_specs = P(("run", "ctx"), "tp")
    return jax.shard_map(body, mesh=mesh, in_specs=in_specs, out_specs=out_specs, check_vma=False)
```

```python
import jax
import jax.numpy as jnp
from jax import lax
from jax.experimental import pallas as pl
from jax.experimental.pallas import tpu as pltpu
from jax.sharding import PartitionSpec as P

HD = 128
BLOCK = 64
MOST_DOC = 1024


THETA = 1000000.0


def rotate(head_rows, offset):
    half = head_rows.shape[-1] // 2
    frequency = jnp.power(
        jnp.float32(THETA), -2.0 * jnp.arange(half, dtype=jnp.float32) / head_rows.shape[-1]
    )
    angles = offset.astype(jnp.float32)[:, None] * frequency[None, :]
    cosines = jnp.cos(angles)[:, None, :]
    sines = jnp.sin(angles)[:, None, :]
    first_half = head_rows[..., :half]
    second_half = head_rows[..., half:]
    return jnp.concatenate(
        [first_half * cosines - second_half * sines, second_half * cosines + first_half * sines],
        axis=-1,
    )


def project(source, weight, bias, offset, rotated):
    result = (
        jnp.dot(source, weight, preferred_element_type=jnp.float32)
        + bias.astype(jnp.float32)[None, :]
    )
    if rotated:
        result = rotate(result.reshape(source.shape[0], -1, HD), offset).reshape(
            source.shape[0], -1
        )
    return result.astype(jnp.bfloat16)


def slot_places(order, first_row, row_count):
    slots = first_row + jnp.arange(row_count, dtype=jnp.int32)
    owners = slots // BLOCK
    selector = owners[:, None] == jnp.arange(order.shape[0], dtype=jnp.int32)[None, :]
    picked = jnp.sum(jnp.where(selector, order[None, :], 0), axis=1)
    return picked * BLOCK + slots % BLOCK


def document_of(places, bounds):
    return jnp.sum((places[..., None] >= bounds).astype(jnp.int32), axis=-1)


def document_info(places, lengths):
    bounds = jnp.cumsum(lengths)
    passed = places[:, None] >= bounds[None, :]
    documents = jnp.sum(passed.astype(jnp.int32), axis=1)
    starts = jnp.sum(jnp.where(passed, lengths[None, :], 0), axis=1)
    return (documents, places - starts)


def body(
    tokens,
    block_order,
    doc_lengths,
    patch_pos,
    clean_rows,
    w_query,
    q_bias,
    w_key,
    k_bias,
    w_value,
    v_bias,
):
    rows = tokens.shape[0]
    patches = patch_pos.shape[0]
    nblocks = block_order.shape[0]
    heads = w_query.shape[1] // HD
    me = lax.axis_index("ctx")
    places = slot_places(block_order, me * rows, rows)
    documents, offset = document_info(places, doc_lengths)
    patch_offset = document_info(patch_pos, doc_lengths)[1]

    width = 2 * HD
    pairs = (heads + 1) // 2
    coded = jnp.zeros((patches, HD), jnp.bfloat16)
    coded = coded.at[:, 0].set((patch_pos // BLOCK).astype(jnp.bfloat16))
    coded = coded.at[:, 1].set((patch_pos % BLOCK).astype(jnp.bfloat16))
    packed = pack(tokens, clean_rows, w_query, w_key, w_value,
                  q_bias.astype(jnp.float32)[None, :], k_bias.astype(jnp.float32)[None, :],
                  v_bias.astype(jnp.float32)[None, :], *rope_tables(offset),
                  *rope_tables(patch_offset), coded)
    lines = packed.shape[0]
    gathered = lax.all_gather(packed, "ctx", axis=0, tiled=False)
    peers = gathered.shape[0]
    per_peer = lines // BLOCK
    local_blocks = rows // BLOCK

    first_q = rows + patches
    last = first_q + (pairs - 1) * patches
    code = gathered[:, last:last + patches, heads * HD - (pairs - 1) * width:][..., :2]
    code = code.reshape(peers * patches, 2).astype(jnp.float32)
    positions = (code[:, 0] * BLOCK + code[:, 1]).astype(jnp.int32)
    bounds = jnp.cumsum(doc_lengths)
    clean_documents = document_of(positions, bounds)
    query = project(tokens, w_query, q_bias, offset, True)

    inverse = jnp.zeros((nblocks,), jnp.int32).at[block_order].set(
        jnp.arange(nblocks, dtype=jnp.int32)
    )
    block_hit = (positions[None, :] // BLOCK == jnp.arange(nblocks, dtype=jnp.int32)[:, None])
    row_hit = (positions[:, None] % BLOCK == jnp.arange(BLOCK, dtype=jnp.int32)[None, :])
    patched_place = jnp.dot(
        block_hit.astype(jnp.bfloat16), row_hit.astype(jnp.bfloat16),
        preferred_element_type=jnp.float32,
    ) > 0.5

    back = MOST_DOC // BLOCK + 1
    window = (back + 1) * BLOCK
    seq_blocks = lax.dynamic_slice_in_dim(block_order, me * local_blocks, local_blocks)
    wanted = seq_blocks[:, None] - back + jnp.arange(back + 1, dtype=jnp.int32)[None, :]
    window_slots = inverse[jnp.clip(wanted, 0, nblocks - 1)]
    window_blocks = (window_slots // local_blocks) * per_peer + window_slots % local_blocks
    key_places = seq_blocks[:, None] * BLOCK - back * BLOCK + jnp.arange(window, dtype=jnp.int32)[None, :]
    key_documents = document_of(key_places, bounds)
    window_patched = patched_place[jnp.clip(wanted, 0, nblocks - 1)].reshape(local_blocks, window)
    key_kept = ((key_places >= 0) & ~window_patched).astype(jnp.int32)

    return attend(
        window_blocks.reshape(-1),
        gathered.reshape(peers * lines, width),
        query,
        places[:, None],
        documents[:, None],
        key_places,
        key_documents,
        key_kept,
        positions[None, :],
        clean_documents[None, :],
        heads=heads,
        patches=patches,
        lines=lines,
        pairs=pairs,
        back=back,
    )


def rope_tables(offset):
    half = HD // 2
    frequency = jnp.power(jnp.float32(THETA), -2.0 * jnp.arange(half, dtype=jnp.float32) / HD)
    angles = offset.astype(jnp.float32)[:, None] * frequency[None, :]
    cosines, sines = jnp.cos(angles), jnp.sin(angles)
    return (jnp.concatenate([cosines, cosines], axis=1), jnp.concatenate([-sines, sines], axis=1))


def pack(tokens, clean_rows, w_query, w_key, w_value, q_bias, k_bias, v_bias, cos_rows,
         sin_rows, cos_clean, sin_clean, coded):
    rows = tokens.shape[0]
    patches = clean_rows.shape[0]
    heads = w_query.shape[1] // HD
    width = 2 * HD
    pairs = (heads + 1) // 2
    lines = rows + patches + pairs * patches

    depth = 512
    steps = tokens.shape[1] // depth

    def kernel(t_ref, c_ref, wq_ref, wk_ref, wv_ref, qb_ref, kb_ref, vb_ref, cr_ref, sr_ref,
               cc_ref, sc_ref, code_ref, out_ref, kv_acc, clean_acc):
        step = pl.program_id(0)

        @pl.when(step == 0)
        def _():
            kv_acc[...] = jnp.zeros_like(kv_acc)
            clean_acc[...] = jnp.zeros_like(clean_acc)

        t = t_ref[...]
        c = c_ref[...]
        kv_acc[:, 0:HD] += jnp.dot(t, wk_ref[...], preferred_element_type=jnp.float32)
        kv_acc[:, HD:width] += jnp.dot(t, wv_ref[...], preferred_element_type=jnp.float32)
        clean_acc[:, 0:heads * HD] += jnp.dot(c, wq_ref[...], preferred_element_type=jnp.float32)
        clean_acc[:, heads * HD:(heads + 1) * HD] += jnp.dot(
            c, wk_ref[...], preferred_element_type=jnp.float32)
        clean_acc[:, (heads + 1) * HD:(heads + 2) * HD] += jnp.dot(
            c, wv_ref[...], preferred_element_type=jnp.float32)

        @pl.when(step == steps - 1)
        def _():
            def rope(x, cos, sin):
                return x * cos + pltpu.roll(x, HD // 2, 1) * sin

            keys = kv_acc[:, 0:HD] + kb_ref[...]
            values = kv_acc[:, HD:width] + vb_ref[...]
            out_ref[0:rows, 0:HD] = rope(keys, cr_ref[...], sr_ref[...]).astype(out_ref.dtype)
            out_ref[0:rows, HD:width] = values.astype(out_ref.dtype)
            keys = clean_acc[:, heads * HD:(heads + 1) * HD] + kb_ref[...]
            values = clean_acc[:, (heads + 1) * HD:(heads + 2) * HD] + vb_ref[...]
            out_ref[rows:rows + patches, 0:HD] = rope(keys, cc_ref[...], sc_ref[...]).astype(out_ref.dtype)
            out_ref[rows:rows + patches, HD:width] = values.astype(out_ref.dtype)
            for h in range(heads):
                at = rows + patches + (h // 2) * patches
                col = (h % 2) * HD
                head = clean_acc[:, h * HD:(h + 1) * HD] + qb_ref[:, h * HD:(h + 1) * HD]
                head = rope(head, cc_ref[...], sc_ref[...])
                out_ref[at:at + patches, col:col + HD] = head.astype(out_ref.dtype)
            at = rows + patches + (pairs - 1) * patches
            col = (heads % 2) * HD
            out_ref[at:at + patches, col:col + HD] = code_ref[...]
            if col + HD < width:
                out_ref[at:at + patches, col + HD:width] = jnp.zeros(
                    (patches, width - col - HD), out_ref.dtype)

    operands = (tokens, clean_rows, w_query, w_key, w_value, q_bias, k_bias, v_bias, cos_rows,
                sin_rows, cos_clean, sin_clean, coded)
    full = lambda shape: pl.BlockSpec(shape, lambda i: (0,) * len(shape))
    in_specs = [
        pl.BlockSpec((rows, depth), lambda i: (0, i)),
        pl.BlockSpec((patches, depth), lambda i: (0, i)),
        pl.BlockSpec((depth, w_query.shape[1]), lambda i: (i, 0)),
        pl.BlockSpec((depth, HD), lambda i: (i, 0)),
        pl.BlockSpec((depth, HD), lambda i: (i, 0)),
    ] + [full(x.shape) for x in operands[5:]]
    return pl.pallas_call(
        kernel,
        out_shape=jax.ShapeDtypeStruct((lines, width), jnp.bfloat16),
        grid=(steps,),
        in_specs=in_specs,
        out_specs=full((lines, width)),
        scratch_shapes=[
            pltpu.VMEM((rows, width), jnp.float32),
            pltpu.VMEM((patches, (heads + 2) * HD), jnp.float32),
        ],
        compiler_params=pltpu.CompilerParams(vmem_limit_bytes=48 * 1024 * 1024),
    )(*operands)


def attend(window_blocks, gathered, query, query_places, query_documents, key_places,
           key_documents, key_kept, clean_places, clean_documents, *, heads, patches, lines,
           pairs, back):
    rows = query.shape[0]
    width = gathered.shape[1]
    peers = gathered.shape[0] // lines
    local_blocks = rows // BLOCK
    window = (back + 1) * BLOCK
    clean_count = peers * patches
    score_scale = HD ** (-0.5)

    def kernel(blocks_ref, g_ref, q_ref, qp_ref, qd_ref, kp_ref, kd_ref, kk_ref, cp_ref, cd_ref,
               out_ref, window_kv, clean_kv, clean_q):
        for p in range(peers):
            base = p * lines + rows
            clean_kv[p * patches:(p + 1) * patches, :] = g_ref[base:base + patches, :]
            for k in range(pairs):
                at = base + patches + k * patches
                clean_q[p * patches:(p + 1) * patches, k * width:(k + 1) * width] = g_ref[at:at + patches, :]
        match = qp_ref[...] == cp_ref[...]
        hit = match.astype(jnp.float32)
        present = jnp.sum(hit, axis=1, keepdims=True) > 0.5
        picked = jnp.dot(
            hit.astype(jnp.bfloat16), clean_q[...], preferred_element_type=jnp.float32
        ).astype(jnp.bfloat16)
        clean_visible_all = qd_ref[...] == cd_ref[...]
        for b in range(local_blocks):
            for j in range(back + 1):
                block = blocks_ref[b * (back + 1) + j]
                start = pl.multiple_of(block * BLOCK, BLOCK)
                window_kv[j * BLOCK:(j + 1) * BLOCK, :] = g_ref[pl.ds(start, BLOCK), :]
            rows_at = slice(b * BLOCK, (b + 1) * BLOCK)
            qp = qp_ref[rows_at, :]
            qd = qd_ref[rows_at, :]
            kp = kp_ref[b:b + 1, :]
            visible = (qd == kd_ref[b:b + 1, :]) & (kp <= qp) & (kk_ref[b:b + 1, :] != 0)
            clean_visible = clean_visible_all[rows_at, :] & (cp_ref[...] <= qp)
            block_present = present[rows_at, :]
            for h in range(heads):
                cols = slice(h * HD, (h + 1) * HD)
                q = jnp.where(block_present, picked[rows_at, cols], q_ref[rows_at, cols])
                scores = lax.dot_general(
                    q, window_kv[:, :HD], (((1,), (1,)), ((), ())),
                    preferred_element_type=jnp.float32,
                ) * score_scale
                clean_scores = lax.dot_general(
                    q, clean_kv[:, :HD], (((1,), (1,)), ((), ())),
                    preferred_element_type=jnp.float32,
                ) * score_scale
                masked = jnp.where(visible, scores, -1e30)
                clean_masked = jnp.where(clean_visible, clean_scores, -1e30)
                peak = jnp.maximum(
                    jnp.max(masked, axis=1, keepdims=True),
                    jnp.max(clean_masked, axis=1, keepdims=True),
                )
                weights = jnp.where(visible, jnp.exp(masked - peak), 0.0)
                clean_weights = jnp.where(clean_visible, jnp.exp(clean_masked - peak), 0.0)
                total = jnp.sum(weights, axis=1, keepdims=True) + jnp.sum(
                    clean_weights, axis=1, keepdims=True
                )
                mixed = jnp.dot(
                    weights.astype(jnp.bfloat16), window_kv[:, HD:],
                    preferred_element_type=jnp.float32,
                ) + jnp.dot(
                    clean_weights.astype(jnp.bfloat16), clean_kv[:, HD:],
                    preferred_element_type=jnp.float32,
                )
                out_ref[rows_at, cols] = (mixed / total).astype(out_ref.dtype)

    full = lambda shape: pl.BlockSpec(shape, lambda i, *_: (0,) * len(shape))
    operands = (gathered, query, query_places, query_documents, key_places, key_documents,
                key_kept, clean_places, clean_documents)
    return pl.pallas_call(
        kernel,
        out_shape=jax.ShapeDtypeStruct(query.shape, query.dtype),
        grid_spec=pltpu.PrefetchScalarGridSpec(
            num_scalar_prefetch=1,
            grid=(1,),
            in_specs=[full(x.shape) for x in operands],
            out_specs=full(query.shape),
            scratch_shapes=[
                pltpu.VMEM((window, width), jnp.bfloat16),
                pltpu.VMEM((clean_count, width), jnp.bfloat16),
                pltpu.VMEM((clean_count, pairs * width), jnp.bfloat16),
            ],
        ),
        compiler_params=pltpu.CompilerParams(vmem_limit_bytes=48 * 1024 * 1024),
    )(window_blocks, *operands)


def solution(mesh):
    in_specs = (
        P(("run", "ctx"), None),
        P(),
        P(),
        P(("run", "ctx")),
        P(("run", "ctx"), None),
        P(None, "tp"),
        P("tp"),
        P(None, "tp"),
        P("tp"),
        P(None, "tp"),
        P("tp"),
    )
    out_specs = P(("run", "ctx"), "tp")
    return jax.shard_map(body, mesh=mesh, in_specs=in_specs, out_specs=out_specs, check_vma=False)
```

```python
import jax
import jax.numpy as jnp
from jax import lax
from jax.experimental import pallas as pl
from jax.experimental.pallas import tpu as pltpu
from jax.sharding import PartitionSpec as P

HD = 128
BLOCK = 64
MOST_DOC = 1024


THETA = 1000000.0


def rotate(head_rows, offset):
    half = head_rows.shape[-1] // 2
    frequency = jnp.power(
        jnp.float32(THETA), -2.0 * jnp.arange(half, dtype=jnp.float32) / head_rows.shape[-1]
    )
    angles = offset.astype(jnp.float32)[:, None] * frequency[None, :]
    cosines = jnp.cos(angles)[:, None, :]
    sines = jnp.sin(angles)[:, None, :]
    first_half = head_rows[..., :half]
    second_half = head_rows[..., half:]
    return jnp.concatenate(
        [first_half * cosines - second_half * sines, second_half * cosines + first_half * sines],
        axis=-1,
    )


def project(source, weight, bias, offset, rotated):
    result = (
        jnp.dot(source, weight, preferred_element_type=jnp.float32)
        + bias.astype(jnp.float32)[None, :]
    )
    if rotated:
        result = rotate(result.reshape(source.shape[0], -1, HD), offset).reshape(
            source.shape[0], -1
        )
    return result.astype(jnp.bfloat16)


def slot_places(order, first_row, row_count):
    slots = first_row + jnp.arange(row_count, dtype=jnp.int32)
    owners = slots // BLOCK
    selector = owners[:, None] == jnp.arange(order.shape[0], dtype=jnp.int32)[None, :]
    picked = jnp.sum(jnp.where(selector, order[None, :], 0), axis=1)
    return picked * BLOCK + slots % BLOCK


def document_of(places, bounds):
    return jnp.sum((places[..., None] >= bounds).astype(jnp.int32), axis=-1)


def document_info(places, lengths):
    bounds = jnp.cumsum(lengths)
    passed = places[:, None] >= bounds[None, :]
    documents = jnp.sum(passed.astype(jnp.int32), axis=1)
    starts = jnp.sum(jnp.where(passed, lengths[None, :], 0), axis=1)
    return (documents, places - starts)


def body(
    tokens,
    block_order,
    doc_lengths,
    patch_pos,
    clean_rows,
    w_query,
    q_bias,
    w_key,
    k_bias,
    w_value,
    v_bias,
):
    rows = tokens.shape[0]
    patches = patch_pos.shape[0]
    nblocks = block_order.shape[0]
    heads = w_query.shape[1] // HD
    me = lax.axis_index("ctx")
    places = slot_places(block_order, me * rows, rows)
    documents, offset = document_info(places, doc_lengths)
    patch_offset = document_info(patch_pos, doc_lengths)[1]

    keys = project(tokens, w_key, k_bias, offset, True)
    values = project(tokens, w_value, v_bias, offset, False)
    clean_query = project(clean_rows, w_query, q_bias, patch_offset, True)
    clean_keys = project(clean_rows, w_key, k_bias, patch_offset, True)
    clean_values = project(clean_rows, w_value, v_bias, patch_offset, False)

    width = 2 * HD
    pairs = (heads + 1) // 2
    spare = pairs * width - heads * HD
    coded = jnp.stack(
        [(patch_pos // BLOCK).astype(jnp.bfloat16), (patch_pos % BLOCK).astype(jnp.bfloat16)], axis=1
    )
    padded_query = jnp.concatenate(
        [clean_query, coded, jnp.zeros((patches, spare - 2), jnp.bfloat16)], axis=1
    )
    parts = [
        jnp.concatenate([keys, values], axis=1),
        jnp.concatenate([clean_keys, clean_values], axis=1),
    ]
    parts += [padded_query[:, p * width:(p + 1) * width] for p in range(pairs)]
    packed = jnp.concatenate(parts, axis=0)
    lines = packed.shape[0]
    gathered = lax.all_gather(packed, "ctx", axis=0, tiled=False)
    peers = gathered.shape[0]
    per_peer = lines // BLOCK
    local_blocks = rows // BLOCK

    first_q = rows + patches
    last = first_q + (pairs - 1) * patches
    code = gathered[:, last:last + patches, heads * HD - (pairs - 1) * width:][..., :2]
    code = code.reshape(peers * patches, 2).astype(jnp.float32)
    positions = (code[:, 0] * BLOCK + code[:, 1]).astype(jnp.int32)
    bounds = jnp.cumsum(doc_lengths)
    clean_documents = document_of(positions, bounds)
    query = project(tokens, w_query, q_bias, offset, True)

    inverse = jnp.zeros((nblocks,), jnp.int32).at[block_order].set(
        jnp.arange(nblocks, dtype=jnp.int32)
    )
    block_hit = (positions[None, :] // BLOCK == jnp.arange(nblocks, dtype=jnp.int32)[:, None])
    row_hit = (positions[:, None] % BLOCK == jnp.arange(BLOCK, dtype=jnp.int32)[None, :])
    patched_place = jnp.dot(
        block_hit.astype(jnp.bfloat16), row_hit.astype(jnp.bfloat16),
        preferred_element_type=jnp.float32,
    ) > 0.5

    back = MOST_DOC // BLOCK + 1
    window = (back + 1) * BLOCK
    seq_blocks = lax.dynamic_slice_in_dim(block_order, me * local_blocks, local_blocks)
    wanted = seq_blocks[:, None] - back + jnp.arange(back + 1, dtype=jnp.int32)[None, :]
    window_slots = inverse[jnp.clip(wanted, 0, nblocks - 1)]
    window_blocks = (window_slots // local_blocks) * per_peer + window_slots % local_blocks
    key_places = seq_blocks[:, None] * BLOCK - back * BLOCK + jnp.arange(window, dtype=jnp.int32)[None, :]
    key_documents = document_of(key_places, bounds)
    window_patched = patched_place[jnp.clip(wanted, 0, nblocks - 1)].reshape(local_blocks, window)
    key_kept = ((key_places >= 0) & ~window_patched).astype(jnp.int32)

    return attend(
        window_blocks.reshape(-1),
        gathered.reshape(peers * lines, width),
        query,
        places[:, None],
        documents[:, None],
        key_places,
        key_documents,
        key_kept,
        positions[None, :],
        clean_documents[None, :],
        heads=heads,
        patches=patches,
        lines=lines,
        pairs=pairs,
        back=back,
    )


def attend(window_blocks, gathered, query, query_places, query_documents, key_places,
           key_documents, key_kept, clean_places, clean_documents, *, heads, patches, lines,
           pairs, back):
    rows = query.shape[0]
    width = gathered.shape[1]
    peers = gathered.shape[0] // lines
    local_blocks = rows // BLOCK
    window = (back + 1) * BLOCK
    clean_count = peers * patches
    score_scale = HD ** (-0.5)

    def kernel(blocks_ref, g_ref, q_ref, qp_ref, qd_ref, kp_ref, kd_ref, kk_ref, cp_ref, cd_ref,
               out_ref, window_kv, clean_kv, clean_q):
        for p in range(peers):
            base = p * lines + rows
            clean_kv[p * patches:(p + 1) * patches, :] = g_ref[base:base + patches, :]
            for k in range(pairs):
                at = base + patches + k * patches
                clean_q[p * patches:(p + 1) * patches, k * width:(k + 1) * width] = g_ref[at:at + patches, :]
        match = qp_ref[...] == cp_ref[...]
        hit = match.astype(jnp.float32)
        present = jnp.sum(hit, axis=1, keepdims=True) > 0.5
        picked = jnp.dot(
            hit.astype(jnp.bfloat16), clean_q[...], preferred_element_type=jnp.float32
        ).astype(jnp.bfloat16)
        for b in range(local_blocks):
            for j in range(back + 1):
                block = blocks_ref[b * (back + 1) + j]
                start = pl.multiple_of(block * BLOCK, BLOCK)
                window_kv[j * BLOCK:(j + 1) * BLOCK, :] = g_ref[pl.ds(start, BLOCK), :]
            rows_at = slice(b * BLOCK, (b + 1) * BLOCK)
            block_present = present[rows_at, :]
            block_query = jnp.where(block_present, picked[rows_at, :heads * HD], q_ref[rows_at, :])
            q = jnp.concatenate([block_query[:, h * HD:(h + 1) * HD] for h in range(heads)], axis=0)
            qp = jnp.concatenate([qp_ref[rows_at, :]] * heads, axis=0)
            qd = jnp.concatenate([qd_ref[rows_at, :]] * heads, axis=0)
            visible = (qd == kd_ref[b:b + 1, :]) & (kp_ref[b:b + 1, :] <= qp) & (kk_ref[b:b + 1, :] != 0)
            clean_visible = (qd == cd_ref[...]) & (cp_ref[...] <= qp)
            scores = lax.dot_general(
                q, window_kv[:, :HD], (((1,), (1,)), ((), ())),
                preferred_element_type=jnp.float32,
            ) * score_scale
            clean_scores = lax.dot_general(
                q, clean_kv[:, :HD], (((1,), (1,)), ((), ())),
                preferred_element_type=jnp.float32,
            ) * score_scale
            masked = jnp.where(visible, scores, -1e30)
            clean_masked = jnp.where(clean_visible, clean_scores, -1e30)
            peak = jnp.maximum(
                jnp.max(masked, axis=1, keepdims=True),
                jnp.max(clean_masked, axis=1, keepdims=True),
            )
            weights = jnp.where(visible, jnp.exp(masked - peak), 0.0)
            clean_weights = jnp.where(clean_visible, jnp.exp(clean_masked - peak), 0.0)
            total = jnp.sum(weights, axis=1, keepdims=True) + jnp.sum(
                clean_weights, axis=1, keepdims=True
            )
            mixed = jnp.dot(
                weights.astype(jnp.bfloat16), window_kv[:, HD:],
                preferred_element_type=jnp.float32,
            ) + jnp.dot(
                clean_weights.astype(jnp.bfloat16), clean_kv[:, HD:],
                preferred_element_type=jnp.float32,
            )
            result = (mixed / total).astype(out_ref.dtype)
            for h in range(heads):
                out_ref[rows_at, h * HD:(h + 1) * HD] = result[h * BLOCK:(h + 1) * BLOCK, :]

    full = lambda shape: pl.BlockSpec(shape, lambda i, *_: (0,) * len(shape))
    operands = (gathered, query, query_places, query_documents, key_places, key_documents,
                key_kept, clean_places, clean_documents)
    return pl.pallas_call(
        kernel,
        out_shape=jax.ShapeDtypeStruct(query.shape, query.dtype),
        grid_spec=pltpu.PrefetchScalarGridSpec(
            num_scalar_prefetch=1,
            grid=(1,),
            in_specs=[full(x.shape) for x in operands],
            out_specs=full(query.shape),
            scratch_shapes=[
                pltpu.VMEM((window, width), jnp.bfloat16),
                pltpu.VMEM((clean_count, width), jnp.bfloat16),
                pltpu.VMEM((clean_count, pairs * width), jnp.bfloat16),
            ],
        ),
        compiler_params=pltpu.CompilerParams(vmem_limit_bytes=48 * 1024 * 1024),
    )(window_blocks, *operands)


def solution(mesh):
    in_specs = (
        P(("run", "ctx"), None),
        P(),
        P(),
        P(("run", "ctx")),
        P(("run", "ctx"), None),
        P(None, "tp"),
        P("tp"),
        P(None, "tp"),
        P("tp"),
        P(None, "tp"),
        P("tp"),
    )
    out_specs = P(("run", "ctx"), "tp")
    return jax.shard_map(body, mesh=mesh, in_specs=in_specs, out_specs=out_specs, check_vma=False)
```

```python
import jax
import jax.numpy as jnp
from jax import lax
from jax.experimental import pallas as pl
from jax.experimental.pallas import tpu as pltpu
from jax.sharding import PartitionSpec as P

HD = 128
BLOCK = 64
MOST_DOC = 1024


THETA = 1000000.0


def rotate(head_rows, offset):
    half = head_rows.shape[-1] // 2
    frequency = jnp.power(
        jnp.float32(THETA), -2.0 * jnp.arange(half, dtype=jnp.float32) / head_rows.shape[-1]
    )
    angles = offset.astype(jnp.float32)[:, None] * frequency[None, :]
    cosines = jnp.cos(angles)[:, None, :]
    sines = jnp.sin(angles)[:, None, :]
    first_half = head_rows[..., :half]
    second_half = head_rows[..., half:]
    return jnp.concatenate(
        [first_half * cosines - second_half * sines, second_half * cosines + first_half * sines],
        axis=-1,
    )


def project(source, weight, bias, offset, rotated):
    result = (
        jnp.dot(source, weight, preferred_element_type=jnp.float32)
        + bias.astype(jnp.float32)[None, :]
    )
    if rotated:
        result = rotate(result.reshape(source.shape[0], -1, HD), offset).reshape(
            source.shape[0], -1
        )
    return result.astype(jnp.bfloat16)


def slot_places(order, first_row, row_count):
    slots = first_row + jnp.arange(row_count, dtype=jnp.int32)
    owners = slots // BLOCK
    selector = owners[:, None] == jnp.arange(order.shape[0], dtype=jnp.int32)[None, :]
    picked = jnp.sum(jnp.where(selector, order[None, :], 0), axis=1)
    return picked * BLOCK + slots % BLOCK


def document_of(places, bounds):
    return jnp.sum((places[..., None] >= bounds).astype(jnp.int32), axis=-1)


def document_info(places, lengths):
    bounds = jnp.cumsum(lengths)
    passed = places[:, None] >= bounds[None, :]
    documents = jnp.sum(passed.astype(jnp.int32), axis=1)
    starts = jnp.sum(jnp.where(passed, lengths[None, :], 0), axis=1)
    return (documents, places - starts)


def body(
    tokens,
    block_order,
    doc_lengths,
    patch_pos,
    clean_rows,
    w_query,
    q_bias,
    w_key,
    k_bias,
    w_value,
    v_bias,
):
    rows = tokens.shape[0]
    patches = patch_pos.shape[0]
    nblocks = block_order.shape[0]
    heads = w_query.shape[1] // HD
    me = lax.axis_index("ctx")
    places = slot_places(block_order, me * rows, rows)
    documents, offset = document_info(places, doc_lengths)
    patch_offset = document_info(patch_pos, doc_lengths)[1]

    keys = project(tokens, w_key, k_bias, offset, True)
    values = project(tokens, w_value, v_bias, offset, False)
    clean_query = project(clean_rows, w_query, q_bias, patch_offset, True)
    clean_keys = project(clean_rows, w_key, k_bias, patch_offset, True)
    clean_values = project(clean_rows, w_value, v_bias, patch_offset, False)

    width = 2 * HD
    pairs = (heads + 1) // 2
    spare = pairs * width - heads * HD
    coded = jnp.stack(
        [(patch_pos // BLOCK).astype(jnp.bfloat16), (patch_pos % BLOCK).astype(jnp.bfloat16)], axis=1
    )
    padded_query = jnp.concatenate(
        [clean_query, coded, jnp.zeros((patches, spare - 2), jnp.bfloat16)], axis=1
    )
    parts = [
        jnp.concatenate([keys, values], axis=1),
        jnp.concatenate([clean_keys, clean_values], axis=1),
    ]
    parts += [padded_query[:, p * width:(p + 1) * width] for p in range(pairs)]
    packed = jnp.concatenate(parts, axis=0)
    lines = packed.shape[0]
    gathered = lax.all_gather(packed, "ctx", axis=0, tiled=False)
    peers = gathered.shape[0]
    per_peer = lines // BLOCK
    local_blocks = rows // BLOCK

    first_q = rows + patches
    last = first_q + (pairs - 1) * patches
    code = gathered[:, last:last + patches, heads * HD - (pairs - 1) * width:][..., :2]
    code = code.reshape(peers * patches, 2).astype(jnp.float32)
    positions = (code[:, 0] * BLOCK + code[:, 1]).astype(jnp.int32)
    bounds = jnp.cumsum(doc_lengths)
    clean_documents = document_of(positions, bounds)
    query = project(tokens, w_query, q_bias, offset, True)

    inverse = jnp.zeros((nblocks,), jnp.int32).at[block_order].set(
        jnp.arange(nblocks, dtype=jnp.int32)
    )
    block_hit = (positions[None, :] // BLOCK == jnp.arange(nblocks, dtype=jnp.int32)[:, None])
    row_hit = (positions[:, None] % BLOCK == jnp.arange(BLOCK, dtype=jnp.int32)[None, :])
    patched_place = jnp.dot(
        block_hit.astype(jnp.bfloat16), row_hit.astype(jnp.bfloat16),
        preferred_element_type=jnp.float32,
    ) > 0.5

    back = MOST_DOC // BLOCK + 1
    window = (back + 1) * BLOCK
    seq_blocks = lax.dynamic_slice_in_dim(block_order, me * local_blocks, local_blocks)
    wanted = seq_blocks[:, None] - back + jnp.arange(back + 1, dtype=jnp.int32)[None, :]
    window_slots = inverse[jnp.clip(wanted, 0, nblocks - 1)]
    window_blocks = (window_slots // local_blocks) * per_peer + window_slots % local_blocks
    key_places = seq_blocks[:, None] * BLOCK - back * BLOCK + jnp.arange(window, dtype=jnp.int32)[None, :]
    key_documents = document_of(key_places, bounds)
    window_patched = patched_place[jnp.clip(wanted, 0, nblocks - 1)].reshape(local_blocks, window)
    key_kept = ((key_places >= 0) & ~window_patched).astype(jnp.int32)

    return attend(
        window_blocks.reshape(-1),
        gathered.reshape(peers * lines, width),
        query,
        places[:, None],
        documents[:, None],
        key_places,
        key_documents,
        key_kept,
        positions[None, :],
        clean_documents[None, :],
        heads=heads,
        patches=patches,
        lines=lines,
        pairs=pairs,
        back=back,
    )


def attend(window_blocks, gathered, query, query_places, query_documents, key_places,
           key_documents, key_kept, clean_places, clean_documents, *, heads, patches, lines,
           pairs, back):
    rows = query.shape[0]
    width = gathered.shape[1]
    peers = gathered.shape[0] // lines
    local_blocks = rows // BLOCK
    window = (back + 1) * BLOCK
    clean_count = peers * patches
    score_scale = HD ** (-0.5)

    def kernel(blocks_ref, g_ref, q_ref, qp_ref, qd_ref, kp_ref, kd_ref, kk_ref, cp_ref, cd_ref,
               out_ref, window_kv, clean_kv, clean_q, window_sems, clean_sems):
        clean_copies = []
        for p in range(peers):
            base = p * lines + rows
            parts = [(clean_kv.at[p * patches:(p + 1) * patches, :], base)]
            for k in range(pairs):
                parts.append((clean_q.at[p * patches:(p + 1) * patches, k * width:(k + 1) * width],
                              base + patches + k * patches))
            for k, (target, at) in enumerate(parts):
                copy = pltpu.make_async_copy(
                    g_ref.at[at:at + patches, :], target, clean_sems.at[p, k])
                copy.start()
                clean_copies.append(copy)
        window_copies = []
        for b in range(local_blocks):
            copies = []
            for j in range(back + 1):
                block = blocks_ref[b * (back + 1) + j]
                start = pl.multiple_of(block * BLOCK, BLOCK)
                copy = pltpu.make_async_copy(
                    g_ref.at[pl.ds(start, BLOCK), :],
                    window_kv.at[b, j * BLOCK:(j + 1) * BLOCK, :],
                    window_sems.at[b, j],
                )
                copy.start()
                copies.append(copy)
            window_copies.append(copies)
        for copy in clean_copies:
            copy.wait()
        match = qp_ref[...] == cp_ref[...]
        hit = match.astype(jnp.float32)
        present = jnp.sum(hit, axis=1, keepdims=True) > 0.5
        picked = jnp.dot(
            hit.astype(jnp.bfloat16), clean_q[...], preferred_element_type=jnp.float32
        ).astype(jnp.bfloat16)
        for b in range(local_blocks):
            for copy in window_copies[b]:
                copy.wait()
            block_kv = window_kv.at[b]
            rows_at = slice(b * BLOCK, (b + 1) * BLOCK)
            block_present = present[rows_at, :]
            block_query = jnp.where(block_present, picked[rows_at, :heads * HD], q_ref[rows_at, :])
            q = jnp.concatenate([block_query[:, h * HD:(h + 1) * HD] for h in range(heads)], axis=0)
            qp = jnp.concatenate([qp_ref[rows_at, :]] * heads, axis=0)
            qd = jnp.concatenate([qd_ref[rows_at, :]] * heads, axis=0)
            visible = (qd == kd_ref[b:b + 1, :]) & (kp_ref[b:b + 1, :] <= qp) & (kk_ref[b:b + 1, :] != 0)
            clean_visible = (qd == cd_ref[...]) & (cp_ref[...] <= qp)
            scores = lax.dot_general(
                q, block_kv[:, :HD], (((1,), (1,)), ((), ())),
                preferred_element_type=jnp.float32,
            ) * score_scale
            clean_scores = lax.dot_general(
                q, clean_kv[:, :HD], (((1,), (1,)), ((), ())),
                preferred_element_type=jnp.float32,
            ) * score_scale
            masked = jnp.where(visible, scores, -1e30)
            clean_masked = jnp.where(clean_visible, clean_scores, -1e30)
            peak = jnp.maximum(
                jnp.max(masked, axis=1, keepdims=True),
                jnp.max(clean_masked, axis=1, keepdims=True),
            )
            weights = jnp.where(visible, jnp.exp(masked - peak), 0.0)
            clean_weights = jnp.where(clean_visible, jnp.exp(clean_masked - peak), 0.0)
            total = jnp.sum(weights, axis=1, keepdims=True) + jnp.sum(
                clean_weights, axis=1, keepdims=True
            )
            mixed = jnp.dot(
                weights.astype(jnp.bfloat16), block_kv[:, HD:],
                preferred_element_type=jnp.float32,
            ) + jnp.dot(
                clean_weights.astype(jnp.bfloat16), clean_kv[:, HD:],
                preferred_element_type=jnp.float32,
            )
            result = (mixed / total).astype(out_ref.dtype)
            for h in range(heads):
                out_ref[rows_at, h * HD:(h + 1) * HD] = result[h * BLOCK:(h + 1) * BLOCK, :]

    full = lambda shape: pl.BlockSpec(shape, lambda i, *_: (0,) * len(shape))
    operands = (gathered, query, query_places, query_documents, key_places, key_documents,
                key_kept, clean_places, clean_documents)
    return pl.pallas_call(
        kernel,
        out_shape=jax.ShapeDtypeStruct(query.shape, query.dtype),
        grid_spec=pltpu.PrefetchScalarGridSpec(
            num_scalar_prefetch=1,
            grid=(1,),
            in_specs=[pl.BlockSpec(memory_space=pl.ANY)] + [full(x.shape) for x in operands[1:]],
            out_specs=full(query.shape),
            scratch_shapes=[
                pltpu.VMEM((local_blocks, window, width), jnp.bfloat16),
                pltpu.VMEM((clean_count, width), jnp.bfloat16),
                pltpu.VMEM((clean_count, pairs * width), jnp.bfloat16),
                pltpu.SemaphoreType.DMA((local_blocks, back + 1)),
                pltpu.SemaphoreType.DMA((peers, pairs + 1)),
            ],
        ),
        compiler_params=pltpu.CompilerParams(vmem_limit_bytes=48 * 1024 * 1024),
    )(window_blocks, *operands)


def solution(mesh):
    in_specs = (
        P(("run", "ctx"), None),
        P(),
        P(),
        P(("run", "ctx")),
        P(("run", "ctx"), None),
        P(None, "tp"),
        P("tp"),
        P(None, "tp"),
        P("tp"),
        P(None, "tp"),
        P("tp"),
    )
    out_specs = P(("run", "ctx"), "tp")
    return jax.shard_map(body, mesh=mesh, in_specs=in_specs, out_specs=out_specs, check_vma=False)
```

```python
import jax
import jax.numpy as jnp
from jax import lax
from jax.experimental import pallas as pl
from jax.experimental.pallas import tpu as pltpu
from jax.sharding import PartitionSpec as P

HD = 128
BLOCK = 64
MOST_DOC = 1024


THETA = 1000000.0


def rotate(head_rows, offset):
    half = head_rows.shape[-1] // 2
    frequency = jnp.power(
        jnp.float32(THETA), -2.0 * jnp.arange(half, dtype=jnp.float32) / head_rows.shape[-1]
    )
    angles = offset.astype(jnp.float32)[:, None] * frequency[None, :]
    cosines = jnp.cos(angles)[:, None, :]
    sines = jnp.sin(angles)[:, None, :]
    first_half = head_rows[..., :half]
    second_half = head_rows[..., half:]
    return jnp.concatenate(
        [first_half * cosines - second_half * sines, second_half * cosines + first_half * sines],
        axis=-1,
    )


def project(source, weight, bias, offset, rotated):
    result = (
        jnp.dot(source, weight, preferred_element_type=jnp.float32)
        + bias.astype(jnp.float32)[None, :]
    )
    if rotated:
        result = rotate(result.reshape(source.shape[0], -1, HD), offset).reshape(
            source.shape[0], -1
        )
    return result.astype(jnp.bfloat16)


def slot_places(order, first_row, row_count):
    slots = first_row + jnp.arange(row_count, dtype=jnp.int32)
    owners = slots // BLOCK
    selector = owners[:, None] == jnp.arange(order.shape[0], dtype=jnp.int32)[None, :]
    picked = jnp.sum(jnp.where(selector, order[None, :], 0), axis=1)
    return picked * BLOCK + slots % BLOCK


def document_of(places, bounds):
    return jnp.sum((places[..., None] >= bounds).astype(jnp.int32), axis=-1)


def document_info(places, lengths):
    bounds = jnp.cumsum(lengths)
    passed = places[:, None] >= bounds[None, :]
    documents = jnp.sum(passed.astype(jnp.int32), axis=1)
    starts = jnp.sum(jnp.where(passed, lengths[None, :], 0), axis=1)
    return (documents, places - starts)


def body(
    tokens,
    block_order,
    doc_lengths,
    patch_pos,
    clean_rows,
    w_query,
    q_bias,
    w_key,
    k_bias,
    w_value,
    v_bias,
):
    rows = tokens.shape[0]
    patches = patch_pos.shape[0]
    nblocks = block_order.shape[0]
    heads = w_query.shape[1] // HD
    me = lax.axis_index("ctx")
    places = slot_places(block_order, me * rows, rows)
    documents, offset = document_info(places, doc_lengths)
    patch_offset = document_info(patch_pos, doc_lengths)[1]

    keys = project(tokens, w_key, k_bias, offset, True)
    values = project(tokens, w_value, v_bias, offset, False)
    clean_query = project(clean_rows, w_query, q_bias, patch_offset, True)
    clean_keys = project(clean_rows, w_key, k_bias, patch_offset, True)
    clean_values = project(clean_rows, w_value, v_bias, patch_offset, False)

    width = 2 * HD
    pairs = (heads + 1) // 2
    spare = pairs * width - heads * HD
    coded = jnp.stack(
        [(patch_pos // BLOCK).astype(jnp.bfloat16), (patch_pos % BLOCK).astype(jnp.bfloat16)], axis=1
    )
    padded_query = jnp.concatenate(
        [clean_query, coded, jnp.zeros((patches, spare - 2), jnp.bfloat16)], axis=1
    )
    parts = [
        jnp.concatenate([keys, values], axis=1),
        jnp.concatenate([clean_keys, clean_values], axis=1),
    ]
    parts += [padded_query[:, p * width:(p + 1) * width] for p in range(pairs)]
    packed = jnp.concatenate(parts, axis=0)
    lines = packed.shape[0]
    gathered = lax.all_gather(packed, "ctx", axis=0, tiled=False)
    peers = gathered.shape[0]
    per_peer = lines // BLOCK
    local_blocks = rows // BLOCK

    first_q = rows + patches
    last = first_q + (pairs - 1) * patches
    code = gathered[:, last:last + patches, heads * HD - (pairs - 1) * width:][..., :2]
    code = code.reshape(peers * patches, 2).astype(jnp.float32)
    positions = (code[:, 0] * BLOCK + code[:, 1]).astype(jnp.int32)
    bounds = jnp.cumsum(doc_lengths)
    clean_documents = document_of(positions, bounds)
    query = project(tokens, w_query, q_bias, offset, True)

    inverse = jnp.zeros((nblocks,), jnp.int32).at[block_order].set(
        jnp.arange(nblocks, dtype=jnp.int32)
    )
    block_hit = (positions[None, :] // BLOCK == jnp.arange(nblocks, dtype=jnp.int32)[:, None])
    row_hit = (positions[:, None] % BLOCK == jnp.arange(BLOCK, dtype=jnp.int32)[None, :])
    patched_place = jnp.dot(
        block_hit.astype(jnp.bfloat16), row_hit.astype(jnp.bfloat16),
        preferred_element_type=jnp.float32,
    ) > 0.5

    back = MOST_DOC // BLOCK + 1
    window = (back + 1) * BLOCK
    seq_blocks = lax.dynamic_slice_in_dim(block_order, me * local_blocks, local_blocks)
    wanted = seq_blocks[:, None] - back + jnp.arange(back + 1, dtype=jnp.int32)[None, :]
    window_slots = inverse[jnp.clip(wanted, 0, nblocks - 1)]
    window_blocks = (window_slots // local_blocks) * per_peer + window_slots % local_blocks
    key_places = seq_blocks[:, None] * BLOCK - back * BLOCK + jnp.arange(window, dtype=jnp.int32)[None, :]
    key_documents = document_of(key_places, bounds)
    window_patched = patched_place[jnp.clip(wanted, 0, nblocks - 1)].reshape(local_blocks, window)
    key_kept = ((key_places >= 0) & ~window_patched).astype(jnp.int32)

    chunk = 2 * BLOCK
    chunks = window // chunk
    first_needed = (places - offset).reshape(local_blocks, BLOCK)[:, 0]
    chunk_ends = key_places[:, 0:1] + chunk * (1 + jnp.arange(chunks, dtype=jnp.int32))[None, :]
    needed = (chunk_ends > first_needed[:, None]).astype(jnp.int32)

    return attend(
        jnp.concatenate([window_blocks.reshape(-1), needed.reshape(-1)]),
        gathered.reshape(peers * lines, width),
        query,
        places[:, None],
        documents[:, None],
        key_places,
        key_documents,
        key_kept,
        positions[None, :],
        clean_documents[None, :],
        heads=heads,
        patches=patches,
        lines=lines,
        pairs=pairs,
        back=back,
    )


def attend(window_blocks, gathered, query, query_places, query_documents, key_places,
           key_documents, key_kept, clean_places, clean_documents, *, heads, patches, lines,
           pairs, back):
    rows = query.shape[0]
    width = gathered.shape[1]
    peers = gathered.shape[0] // lines
    local_blocks = rows // BLOCK
    window = (back + 1) * BLOCK
    clean_count = peers * patches
    score_scale = HD ** (-0.5)

    chunk = 2 * BLOCK
    chunks = window // chunk
    flags_at = local_blocks * (back + 1)

    def kernel(blocks_ref, g_ref, q_ref, qp_ref, qd_ref, kp_ref, kd_ref, kk_ref, cp_ref, cd_ref,
               out_ref, window_kv, clean_kv, clean_q, score_ref, peak_ref, total_ref, mixed_ref):
        for p in range(peers):
            base = p * lines + rows
            clean_kv[p * patches:(p + 1) * patches, :] = g_ref[base:base + patches, :]
            for k in range(pairs):
                at = base + patches + k * patches
                clean_q[p * patches:(p + 1) * patches, k * width:(k + 1) * width] = g_ref[at:at + patches, :]
        match = qp_ref[...] == cp_ref[...]
        hit = match.astype(jnp.float32)
        present = jnp.sum(hit, axis=1, keepdims=True) > 0.5
        picked = jnp.dot(
            hit.astype(jnp.bfloat16), clean_q[...], preferred_element_type=jnp.float32
        ).astype(jnp.bfloat16)
        for b in range(local_blocks):
            for j in range(back + 1):
                block = blocks_ref[b * (back + 1) + j]
                start = pl.multiple_of(block * BLOCK, BLOCK)
                window_kv[j * BLOCK:(j + 1) * BLOCK, :] = g_ref[pl.ds(start, BLOCK), :]
            rows_at = slice(b * BLOCK, (b + 1) * BLOCK)
            block_present = present[rows_at, :]
            block_query = jnp.where(block_present, picked[rows_at, :heads * HD], q_ref[rows_at, :])
            q = jnp.concatenate([block_query[:, h * HD:(h + 1) * HD] for h in range(heads)], axis=0)
            qp = jnp.concatenate([qp_ref[rows_at, :]] * heads, axis=0)
            qd = jnp.concatenate([qd_ref[rows_at, :]] * heads, axis=0)
            clean_visible = (qd == cd_ref[...]) & (cp_ref[...] <= qp)
            clean_scores = lax.dot_general(
                q, clean_kv[:, :HD], (((1,), (1,)), ((), ())),
                preferred_element_type=jnp.float32,
            ) * score_scale
            clean_masked = jnp.where(clean_visible, clean_scores, -1e30)
            peak_ref[...] = jnp.max(clean_masked, axis=1, keepdims=True)
            for c in range(chunks):
                keys_at = slice(c * chunk, (c + 1) * chunk)

                @pl.when(blocks_ref[flags_at + b * chunks + c] != 0)
                def _():
                    visible = (
                        (qd == kd_ref[b:b + 1, keys_at])
                        & (kp_ref[b:b + 1, keys_at] <= qp)
                        & (kk_ref[b:b + 1, keys_at] != 0)
                    )
                    scores = lax.dot_general(
                        q, window_kv[keys_at, :HD], (((1,), (1,)), ((), ())),
                        preferred_element_type=jnp.float32,
                    ) * score_scale
                    masked = jnp.where(visible, scores, -1e30)
                    score_ref[:, keys_at] = masked
                    peak_ref[...] = jnp.maximum(peak_ref[...], jnp.max(masked, axis=1, keepdims=True))

            peak = peak_ref[...]
            clean_weights = jnp.where(clean_visible, jnp.exp(clean_masked - peak), 0.0)
            total_ref[...] = jnp.sum(clean_weights, axis=1, keepdims=True)
            mixed_ref[...] = jnp.dot(
                clean_weights.astype(jnp.bfloat16), clean_kv[:, HD:],
                preferred_element_type=jnp.float32,
            )
            for c in range(chunks):
                keys_at = slice(c * chunk, (c + 1) * chunk)

                @pl.when(blocks_ref[flags_at + b * chunks + c] != 0)
                def _():
                    masked = score_ref[:, keys_at]
                    visible = masked > -1e29
                    weights = jnp.where(visible, jnp.exp(masked - peak), 0.0)
                    total_ref[...] += jnp.sum(weights, axis=1, keepdims=True)
                    mixed_ref[...] += jnp.dot(
                        weights.astype(jnp.bfloat16), window_kv[keys_at, HD:],
                        preferred_element_type=jnp.float32,
                    )

            mixed = mixed_ref[...]
            total = total_ref[...]
            result = (mixed / total).astype(out_ref.dtype)
            for h in range(heads):
                out_ref[rows_at, h * HD:(h + 1) * HD] = result[h * BLOCK:(h + 1) * BLOCK, :]

    full = lambda shape: pl.BlockSpec(shape, lambda i, *_: (0,) * len(shape))
    operands = (gathered, query, query_places, query_documents, key_places, key_documents,
                key_kept, clean_places, clean_documents)
    return pl.pallas_call(
        kernel,
        out_shape=jax.ShapeDtypeStruct(query.shape, query.dtype),
        grid_spec=pltpu.PrefetchScalarGridSpec(
            num_scalar_prefetch=1,
            grid=(1,),
            in_specs=[full(x.shape) for x in operands],
            out_specs=full(query.shape),
            scratch_shapes=[
                pltpu.VMEM((window, width), jnp.bfloat16),
                pltpu.VMEM((clean_count, width), jnp.bfloat16),
                pltpu.VMEM((clean_count, pairs * width), jnp.bfloat16),
                pltpu.VMEM((heads * BLOCK, window), jnp.float32),
                pltpu.VMEM((heads * BLOCK, 1), jnp.float32),
                pltpu.VMEM((heads * BLOCK, 1), jnp.float32),
                pltpu.VMEM((heads * BLOCK, HD), jnp.float32),
            ],
        ),
        compiler_params=pltpu.CompilerParams(vmem_limit_bytes=48 * 1024 * 1024),
    )(window_blocks, *operands)


def solution(mesh):
    in_specs = (
        P(("run", "ctx"), None),
        P(),
        P(),
        P(("run", "ctx")),
        P(("run", "ctx"), None),
        P(None, "tp"),
        P("tp"),
        P(None, "tp"),
        P("tp"),
        P(None, "tp"),
        P("tp"),
    )
    out_specs = P(("run", "ctx"), "tp")
    return jax.shard_map(body, mesh=mesh, in_specs=in_specs, out_specs=out_specs, check_vma=False)
```

```python
import jax
import jax.numpy as jnp
from jax import lax
from jax.experimental import pallas as pl
from jax.experimental.pallas import tpu as pltpu
from jax.sharding import PartitionSpec as P

HD = 128
BLOCK = 64
MOST_DOC = 1024


THETA = 1000000.0


def rotate(head_rows, offset):
    half = head_rows.shape[-1] // 2
    frequency = jnp.power(
        jnp.float32(THETA), -2.0 * jnp.arange(half, dtype=jnp.float32) / head_rows.shape[-1]
    )
    angles = offset.astype(jnp.float32)[:, None] * frequency[None, :]
    cosines = jnp.cos(angles)[:, None, :]
    sines = jnp.sin(angles)[:, None, :]
    first_half = head_rows[..., :half]
    second_half = head_rows[..., half:]
    return jnp.concatenate(
        [first_half * cosines - second_half * sines, second_half * cosines + first_half * sines],
        axis=-1,
    )


def project(source, weight, bias, offset, rotated):
    result = (
        jnp.dot(source, weight, preferred_element_type=jnp.float32)
        + bias.astype(jnp.float32)[None, :]
    )
    if rotated:
        result = rotate(result.reshape(source.shape[0], -1, HD), offset).reshape(
            source.shape[0], -1
        )
    return result.astype(jnp.bfloat16)


def slot_places(order, first_row, row_count):
    slots = first_row + jnp.arange(row_count, dtype=jnp.int32)
    owners = slots // BLOCK
    selector = owners[:, None] == jnp.arange(order.shape[0], dtype=jnp.int32)[None, :]
    picked = jnp.sum(jnp.where(selector, order[None, :], 0), axis=1)
    return picked * BLOCK + slots % BLOCK


def document_of(places, bounds):
    return jnp.sum((places[..., None] >= bounds).astype(jnp.int32), axis=-1)


def document_info(places, lengths):
    bounds = jnp.cumsum(lengths)
    passed = places[:, None] >= bounds[None, :]
    documents = jnp.sum(passed.astype(jnp.int32), axis=1)
    starts = jnp.sum(jnp.where(passed, lengths[None, :], 0), axis=1)
    return (documents, places - starts)


def body(
    tokens,
    block_order,
    doc_lengths,
    patch_pos,
    clean_rows,
    w_query,
    q_bias,
    w_key,
    k_bias,
    w_value,
    v_bias,
):
    rows = tokens.shape[0]
    patches = patch_pos.shape[0]
    nblocks = block_order.shape[0]
    heads = w_query.shape[1] // HD
    me = lax.axis_index("ctx")
    places = slot_places(block_order, me * rows, rows)
    documents, offset = document_info(places, doc_lengths)
    patch_offset = document_info(patch_pos, doc_lengths)[1]

    keys = project(tokens, w_key, k_bias, offset, True)
    values = project(tokens, w_value, v_bias, offset, False)
    clean_query = project(clean_rows, w_query, q_bias, patch_offset, True)
    clean_keys = project(clean_rows, w_key, k_bias, patch_offset, True)
    clean_values = project(clean_rows, w_value, v_bias, patch_offset, False)

    width = 2 * HD
    pairs = (heads + 1) // 2
    spare = pairs * width - heads * HD
    coded = jnp.stack(
        [(patch_pos // BLOCK).astype(jnp.bfloat16), (patch_pos % BLOCK).astype(jnp.bfloat16)], axis=1
    )
    padded_query = jnp.concatenate(
        [clean_query, coded, jnp.zeros((patches, spare - 2), jnp.bfloat16)], axis=1
    )
    parts = [
        jnp.concatenate([keys, values], axis=1),
        jnp.concatenate([clean_keys, clean_values], axis=1),
    ]
    parts += [padded_query[:, p * width:(p + 1) * width] for p in range(pairs)]
    packed = jnp.concatenate(parts, axis=0)
    lines = packed.shape[0]
    gathered = lax.all_gather(packed, "ctx", axis=0, tiled=False)
    peers = gathered.shape[0]
    per_peer = lines // BLOCK
    local_blocks = rows // BLOCK

    first_q = rows + patches
    last = first_q + (pairs - 1) * patches
    code = gathered[:, last:last + patches, heads * HD - (pairs - 1) * width:][..., :2]
    code = code.reshape(peers * patches, 2).astype(jnp.float32)
    positions = (code[:, 0] * BLOCK + code[:, 1]).astype(jnp.int32)
    bounds = jnp.cumsum(doc_lengths)
    clean_documents = document_of(positions, bounds)
    query = project(tokens, w_query, q_bias, offset, True)

    inverse = jnp.zeros((nblocks,), jnp.int32).at[block_order].set(
        jnp.arange(nblocks, dtype=jnp.int32)
    )
    block_hit = (positions[None, :] // BLOCK == jnp.arange(nblocks, dtype=jnp.int32)[:, None])
    row_hit = (positions[:, None] % BLOCK == jnp.arange(BLOCK, dtype=jnp.int32)[None, :])
    patched_place = jnp.dot(
        block_hit.astype(jnp.bfloat16), row_hit.astype(jnp.bfloat16),
        preferred_element_type=jnp.float32,
    ) > 0.5

    back = MOST_DOC // BLOCK + 1
    window = (back + 1) * BLOCK
    seq_blocks = lax.dynamic_slice_in_dim(block_order, me * local_blocks, local_blocks)
    wanted = seq_blocks[:, None] - back + jnp.arange(back + 1, dtype=jnp.int32)[None, :]
    window_slots = inverse[jnp.clip(wanted, 0, nblocks - 1)]
    window_blocks = (window_slots // local_blocks) * per_peer + window_slots % local_blocks
    key_places = seq_blocks[:, None] * BLOCK - back * BLOCK + jnp.arange(window, dtype=jnp.int32)[None, :]
    key_documents = document_of(key_places, bounds)
    window_patched = patched_place[jnp.clip(wanted, 0, nblocks - 1)].reshape(local_blocks, window)
    key_kept = ((key_places >= 0) & ~window_patched).astype(jnp.int32)

    return attend(
        window_blocks.reshape(-1),
        gathered.reshape(peers * lines, width),
        query,
        places[:, None],
        documents[:, None],
        key_places,
        key_documents,
        key_kept,
        positions[None, :],
        clean_documents[None, :],
        heads=heads,
        patches=patches,
        lines=lines,
        pairs=pairs,
        back=back,
    )


def attend(window_blocks, gathered, query, query_places, query_documents, key_places,
           key_documents, key_kept, clean_places, clean_documents, *, heads, patches, lines,
           pairs, back):
    rows = query.shape[0]
    width = gathered.shape[1]
    peers = gathered.shape[0] // lines
    local_blocks = rows // BLOCK
    window = (back + 1) * BLOCK
    clean_count = peers * patches
    score_scale = HD ** (-0.5)

    def kernel(blocks_ref, g_hbm, q_ref, qp_ref, qd_ref, kp_ref, kd_ref, kk_ref, cp_ref, cd_ref,
               out_ref, window_kv, clean_kv, clean_q, g_ref, g_sem):
        arrival = pltpu.make_async_copy(g_hbm, g_ref, g_sem)
        arrival.start()
        arrival.wait()
        for p in range(peers):
            base = p * lines + rows
            clean_kv[p * patches:(p + 1) * patches, :] = g_ref[base:base + patches, :]
            for k in range(pairs):
                at = base + patches + k * patches
                clean_q[p * patches:(p + 1) * patches, k * width:(k + 1) * width] = g_ref[at:at + patches, :]
        match = qp_ref[...] == cp_ref[...]
        hit = match.astype(jnp.float32)
        present = jnp.sum(hit, axis=1, keepdims=True) > 0.5
        picked = jnp.dot(
            hit.astype(jnp.bfloat16), clean_q[...], preferred_element_type=jnp.float32
        ).astype(jnp.bfloat16)
        for b in range(local_blocks):
            for j in range(back + 1):
                block = blocks_ref[b * (back + 1) + j]
                start = pl.multiple_of(block * BLOCK, BLOCK)
                window_kv[j * BLOCK:(j + 1) * BLOCK, :] = g_ref[pl.ds(start, BLOCK), :]
            rows_at = slice(b * BLOCK, (b + 1) * BLOCK)
            block_present = present[rows_at, :]
            block_query = jnp.where(block_present, picked[rows_at, :heads * HD], q_ref[rows_at, :])
            q = jnp.concatenate([block_query[:, h * HD:(h + 1) * HD] for h in range(heads)], axis=0)
            qp = jnp.concatenate([qp_ref[rows_at, :]] * heads, axis=0)
            qd = jnp.concatenate([qd_ref[rows_at, :]] * heads, axis=0)
            visible = (qd == kd_ref[b:b + 1, :]) & (kp_ref[b:b + 1, :] <= qp) & (kk_ref[b:b + 1, :] != 0)
            clean_visible = (qd == cd_ref[...]) & (cp_ref[...] <= qp)
            scores = lax.dot_general(
                q, window_kv[:, :HD], (((1,), (1,)), ((), ())),
                preferred_element_type=jnp.float32,
            ) * score_scale
            clean_scores = lax.dot_general(
                q, clean_kv[:, :HD], (((1,), (1,)), ((), ())),
                preferred_element_type=jnp.float32,
            ) * score_scale
            masked = jnp.where(visible, scores, -1e30)
            clean_masked = jnp.where(clean_visible, clean_scores, -1e30)
            peak = jnp.maximum(
                jnp.max(masked, axis=1, keepdims=True),
                jnp.max(clean_masked, axis=1, keepdims=True),
            )
            weights = jnp.where(visible, jnp.exp(masked - peak), 0.0)
            clean_weights = jnp.where(clean_visible, jnp.exp(clean_masked - peak), 0.0)
            total = jnp.sum(weights, axis=1, keepdims=True) + jnp.sum(
                clean_weights, axis=1, keepdims=True
            )
            mixed = jnp.dot(
                weights.astype(jnp.bfloat16), window_kv[:, HD:],
                preferred_element_type=jnp.float32,
            ) + jnp.dot(
                clean_weights.astype(jnp.bfloat16), clean_kv[:, HD:],
                preferred_element_type=jnp.float32,
            )
            result = (mixed / total).astype(out_ref.dtype)
            for h in range(heads):
                out_ref[rows_at, h * HD:(h + 1) * HD] = result[h * BLOCK:(h + 1) * BLOCK, :]

    full = lambda shape: pl.BlockSpec(shape, lambda i, *_: (0,) * len(shape))
    operands = (gathered, query, query_places, query_documents, key_places, key_documents,
                key_kept, clean_places, clean_documents)
    return pl.pallas_call(
        kernel,
        out_shape=jax.ShapeDtypeStruct(query.shape, query.dtype),
        grid_spec=pltpu.PrefetchScalarGridSpec(
            num_scalar_prefetch=1,
            grid=(1,),
            in_specs=[pl.BlockSpec(memory_space=pl.ANY)] + [full(x.shape) for x in operands[1:]],
            out_specs=full(query.shape),
            scratch_shapes=[
                pltpu.VMEM((window, width), jnp.bfloat16),
                pltpu.VMEM((clean_count, width), jnp.bfloat16),
                pltpu.VMEM((clean_count, pairs * width), jnp.bfloat16),
                pltpu.VMEM(gathered.shape, gathered.dtype),
                pltpu.SemaphoreType.DMA(()),
            ],
        ),
        compiler_params=pltpu.CompilerParams(vmem_limit_bytes=67043328),
    )(window_blocks, *operands)


def solution(mesh):
    in_specs = (
        P(("run", "ctx"), None),
        P(),
        P(),
        P(("run", "ctx")),
        P(("run", "ctx"), None),
        P(None, "tp"),
        P("tp"),
        P(None, "tp"),
        P("tp"),
        P(None, "tp"),
        P("tp"),
    )
    out_specs = P(("run", "ctx"), "tp")
    return jax.shard_map(body, mesh=mesh, in_specs=in_specs, out_specs=out_specs, check_vma=False)
```

```python
import jax
import jax.numpy as jnp
from jax import lax
from jax.experimental import pallas as pl
from jax.experimental.pallas import tpu as pltpu
from jax.sharding import PartitionSpec as P

HD = 128
BLOCK = 64
MOST_DOC = 1024


THETA = 1000000.0


def rotate(head_rows, offset):
    half = head_rows.shape[-1] // 2
    frequency = jnp.power(
        jnp.float32(THETA), -2.0 * jnp.arange(half, dtype=jnp.float32) / head_rows.shape[-1]
    )
    angles = offset.astype(jnp.float32)[:, None] * frequency[None, :]
    cosines = jnp.cos(angles)[:, None, :]
    sines = jnp.sin(angles)[:, None, :]
    first_half = head_rows[..., :half]
    second_half = head_rows[..., half:]
    return jnp.concatenate(
        [first_half * cosines - second_half * sines, second_half * cosines + first_half * sines],
        axis=-1,
    )


def project(source, weight, bias, offset, rotated):
    result = (
        jnp.dot(source, weight, preferred_element_type=jnp.float32)
        + bias.astype(jnp.float32)[None, :]
    )
    if rotated:
        result = rotate(result.reshape(source.shape[0], -1, HD), offset).reshape(
            source.shape[0], -1
        )
    return result.astype(jnp.bfloat16)


def slot_places(order, first_row, row_count):
    slots = first_row + jnp.arange(row_count, dtype=jnp.int32)
    owners = slots // BLOCK
    selector = owners[:, None] == jnp.arange(order.shape[0], dtype=jnp.int32)[None, :]
    picked = jnp.sum(jnp.where(selector, order[None, :], 0), axis=1)
    return picked * BLOCK + slots % BLOCK


def document_of(places, bounds):
    return jnp.sum((places[..., None] >= bounds).astype(jnp.int32), axis=-1)


def document_info(places, lengths):
    bounds = jnp.cumsum(lengths)
    passed = places[:, None] >= bounds[None, :]
    documents = jnp.sum(passed.astype(jnp.int32), axis=1)
    starts = jnp.sum(jnp.where(passed, lengths[None, :], 0), axis=1)
    return (documents, places - starts)


def body(
    tokens,
    block_order,
    doc_lengths,
    patch_pos,
    clean_rows,
    w_query,
    q_bias,
    w_key,
    k_bias,
    w_value,
    v_bias,
):
    rows = tokens.shape[0]
    patches = patch_pos.shape[0]
    nblocks = block_order.shape[0]
    heads = w_query.shape[1] // HD
    me = lax.axis_index("ctx")
    places = slot_places(block_order, me * rows, rows)
    documents, offset = document_info(places, doc_lengths)
    patch_offset = document_info(patch_pos, doc_lengths)[1]

    keys = project(tokens, w_key, k_bias, offset, True)
    values = project(tokens, w_value, v_bias, offset, False)
    clean_query = project(clean_rows, w_query, q_bias, patch_offset, True)
    clean_keys = project(clean_rows, w_key, k_bias, patch_offset, True)
    clean_values = project(clean_rows, w_value, v_bias, patch_offset, False)

    width = 2 * HD
    pairs = (heads + 1) // 2
    spare = pairs * width - heads * HD
    coded = jnp.stack(
        [(patch_pos // BLOCK).astype(jnp.bfloat16), (patch_pos % BLOCK).astype(jnp.bfloat16)], axis=1
    )
    padded_query = jnp.concatenate(
        [clean_query, coded, jnp.zeros((patches, spare - 2), jnp.bfloat16)], axis=1
    )
    parts = [
        jnp.concatenate([keys, values], axis=1),
        jnp.concatenate([clean_keys, clean_values], axis=1),
    ]
    parts += [padded_query[:, p * width:(p + 1) * width] for p in range(pairs)]
    packed = jnp.concatenate(parts, axis=0)
    lines = packed.shape[0]
    gathered = lax.all_gather(packed, "ctx", axis=0, tiled=False)
    peers = gathered.shape[0]
    per_peer = lines // BLOCK
    local_blocks = rows // BLOCK

    first_q = rows + patches
    last = first_q + (pairs - 1) * patches
    code = gathered[:, last:last + patches, heads * HD - (pairs - 1) * width:][..., :2]
    code = code.reshape(peers * patches, 2).astype(jnp.float32)
    positions = (code[:, 0] * BLOCK + code[:, 1]).astype(jnp.int32)
    bounds = jnp.cumsum(doc_lengths)
    clean_documents = document_of(positions, bounds)
    query = project(tokens, w_query, q_bias, offset, True)

    inverse = jnp.zeros((nblocks,), jnp.int32).at[block_order].set(
        jnp.arange(nblocks, dtype=jnp.int32)
    )
    block_hit = (positions[None, :] // BLOCK == jnp.arange(nblocks, dtype=jnp.int32)[:, None])
    row_hit = (positions[:, None] % BLOCK == jnp.arange(BLOCK, dtype=jnp.int32)[None, :])
    patched_place = jnp.dot(
        block_hit.astype(jnp.bfloat16), row_hit.astype(jnp.bfloat16),
        preferred_element_type=jnp.float32,
    ) > 0.5

    back = MOST_DOC // BLOCK + 1
    window = (back + 1) * BLOCK
    seq_blocks = lax.dynamic_slice_in_dim(block_order, me * local_blocks, local_blocks)
    wanted = seq_blocks[:, None] - back + jnp.arange(back + 1, dtype=jnp.int32)[None, :]
    window_slots = inverse[jnp.clip(wanted, 0, nblocks - 1)]
    window_blocks = (window_slots // local_blocks) * per_peer + window_slots % local_blocks
    key_places = seq_blocks[:, None] * BLOCK - back * BLOCK + jnp.arange(window, dtype=jnp.int32)[None, :]
    key_documents = document_of(key_places, bounds)
    window_patched = patched_place[jnp.clip(wanted, 0, nblocks - 1)].reshape(local_blocks, window)
    key_kept = ((key_places >= 0) & ~window_patched).astype(jnp.int32)

    return attend(
        window_blocks.reshape(-1),
        gathered.reshape(peers * lines, width),
        query,
        places[:, None],
        documents[:, None],
        key_places,
        key_documents,
        key_kept,
        positions[None, :],
        clean_documents[None, :],
        heads=heads,
        patches=patches,
        lines=lines,
        pairs=pairs,
        back=back,
    )


def attend(window_blocks, gathered, query, query_places, query_documents, key_places,
           key_documents, key_kept, clean_places, clean_documents, *, heads, patches, lines,
           pairs, back):
    rows = query.shape[0]
    width = gathered.shape[1]
    peers = gathered.shape[0] // lines
    local_blocks = rows // BLOCK
    window = (back + 1) * BLOCK
    clean_count = peers * patches
    score_scale = HD ** (-0.5)

    def kernel(blocks_ref, g_ref, q_ref, qp_ref, qd_ref, kp_ref, kd_ref, kk_ref, cp_ref, cd_ref,
               out_ref, window_kv, clean_kv, clean_q):
        for p in range(peers):
            base = p * lines + rows
            clean_kv[p * patches:(p + 1) * patches, :] = g_ref[base:base + patches, :]
            for k in range(pairs):
                at = base + patches + k * patches
                clean_q[p * patches:(p + 1) * patches, k * width:(k + 1) * width] = g_ref[at:at + patches, :]
        match = qp_ref[...] == cp_ref[...]
        hit = match.astype(jnp.float32)
        present = jnp.sum(hit, axis=1, keepdims=True) > 0.5
        picked = jnp.dot(
            hit.astype(jnp.bfloat16), clean_q[...], preferred_element_type=jnp.float32
        ).astype(jnp.bfloat16)
        for b in range(local_blocks):
            for j in range(back + 1):
                block = blocks_ref[b * (back + 1) + j]
                start = pl.multiple_of(block * BLOCK, BLOCK)
                window_kv[j * BLOCK:(j + 1) * BLOCK, :] = g_ref[pl.ds(start, BLOCK), :]
            rows_at = slice(b * BLOCK, (b + 1) * BLOCK)
            block_present = present[rows_at, :]
            block_query = jnp.where(block_present, picked[rows_at, :heads * HD], q_ref[rows_at, :])
            q = jnp.concatenate([block_query[:, h * HD:(h + 1) * HD] for h in range(heads)], axis=0)
            qp = qp_ref[rows_at, :]
            qd = qd_ref[rows_at, :]
            visible = (qd == kd_ref[b:b + 1, :]) & (kp_ref[b:b + 1, :] <= qp) & (kk_ref[b:b + 1, :] != 0)
            clean_visible = (qd == cd_ref[...]) & (cp_ref[...] <= qp)
            hidden = jnp.concatenate([jnp.where(visible, 0.0, -1e30)] * heads, axis=0)
            clean_hidden = jnp.concatenate([jnp.where(clean_visible, 0.0, -1e30)] * heads, axis=0)
            scores = lax.dot_general(
                q, window_kv[:, :HD], (((1,), (1,)), ((), ())),
                preferred_element_type=jnp.float32,
            ) * score_scale
            clean_scores = lax.dot_general(
                q, clean_kv[:, :HD], (((1,), (1,)), ((), ())),
                preferred_element_type=jnp.float32,
            ) * score_scale
            masked = scores + hidden
            clean_masked = clean_scores + clean_hidden
            peak = jnp.maximum(
                jnp.max(masked, axis=1, keepdims=True),
                jnp.max(clean_masked, axis=1, keepdims=True),
            )
            weights = jnp.exp(masked - peak)
            clean_weights = jnp.exp(clean_masked - peak)
            total = jnp.sum(weights, axis=1, keepdims=True) + jnp.sum(
                clean_weights, axis=1, keepdims=True
            )
            mixed = jnp.dot(
                weights.astype(jnp.bfloat16), window_kv[:, HD:],
                preferred_element_type=jnp.float32,
            ) + jnp.dot(
                clean_weights.astype(jnp.bfloat16), clean_kv[:, HD:],
                preferred_element_type=jnp.float32,
            )
            result = (mixed / total).astype(out_ref.dtype)
            for h in range(heads):
                out_ref[rows_at, h * HD:(h + 1) * HD] = result[h * BLOCK:(h + 1) * BLOCK, :]

    full = lambda shape: pl.BlockSpec(shape, lambda i, *_: (0,) * len(shape))
    operands = (gathered, query, query_places, query_documents, key_places, key_documents,
                key_kept, clean_places, clean_documents)
    return pl.pallas_call(
        kernel,
        out_shape=jax.ShapeDtypeStruct(query.shape, query.dtype),
        grid_spec=pltpu.PrefetchScalarGridSpec(
            num_scalar_prefetch=1,
            grid=(1,),
            in_specs=[full(x.shape) for x in operands],
            out_specs=full(query.shape),
            scratch_shapes=[
                pltpu.VMEM((window, width), jnp.bfloat16),
                pltpu.VMEM((clean_count, width), jnp.bfloat16),
                pltpu.VMEM((clean_count, pairs * width), jnp.bfloat16),
            ],
        ),
        compiler_params=pltpu.CompilerParams(vmem_limit_bytes=48 * 1024 * 1024),
    )(window_blocks, *operands)


def solution(mesh):
    in_specs = (
        P(("run", "ctx"), None),
        P(),
        P(),
        P(("run", "ctx")),
        P(("run", "ctx"), None),
        P(None, "tp"),
        P("tp"),
        P(None, "tp"),
        P("tp"),
        P(None, "tp"),
        P("tp"),
    )
    out_specs = P(("run", "ctx"), "tp")
    return jax.shard_map(body, mesh=mesh, in_specs=in_specs, out_specs=out_specs, check_vma=False)
```

```python
import jax
import jax.numpy as jnp
from jax import lax
from jax.experimental import pallas as pl
from jax.experimental.pallas import tpu as pltpu
from jax.sharding import PartitionSpec as P

HD = 128
BLOCK = 64
MOST_DOC = 1024


THETA = 1000000.0


def rotate(head_rows, offset):
    half = head_rows.shape[-1] // 2
    frequency = jnp.power(
        jnp.float32(THETA), -2.0 * jnp.arange(half, dtype=jnp.float32) / head_rows.shape[-1]
    )
    angles = offset.astype(jnp.float32)[:, None] * frequency[None, :]
    cosines = jnp.cos(angles)[:, None, :]
    sines = jnp.sin(angles)[:, None, :]
    first_half = head_rows[..., :half]
    second_half = head_rows[..., half:]
    return jnp.concatenate(
        [first_half * cosines - second_half * sines, second_half * cosines + first_half * sines],
        axis=-1,
    )


def project(source, weight, bias, offset, rotated):
    result = (
        jnp.dot(source, weight, preferred_element_type=jnp.float32)
        + bias.astype(jnp.float32)[None, :]
    )
    if rotated:
        result = rotate(result.reshape(source.shape[0], -1, HD), offset).reshape(
            source.shape[0], -1
        )
    return result.astype(jnp.bfloat16)


def slot_places(order, first_row, row_count):
    slots = first_row + jnp.arange(row_count, dtype=jnp.int32)
    owners = slots // BLOCK
    selector = owners[:, None] == jnp.arange(order.shape[0], dtype=jnp.int32)[None, :]
    picked = jnp.sum(jnp.where(selector, order[None, :], 0), axis=1)
    return picked * BLOCK + slots % BLOCK


def document_of(places, bounds):
    return jnp.sum((places[..., None] >= bounds).astype(jnp.int32), axis=-1)


def document_info(places, lengths):
    bounds = jnp.cumsum(lengths)
    passed = places[:, None] >= bounds[None, :]
    documents = jnp.sum(passed.astype(jnp.int32), axis=1)
    starts = jnp.sum(jnp.where(passed, lengths[None, :], 0), axis=1)
    return (documents, places - starts)


def body(
    tokens,
    block_order,
    doc_lengths,
    patch_pos,
    clean_rows,
    w_query,
    q_bias,
    w_key,
    k_bias,
    w_value,
    v_bias,
):
    rows = tokens.shape[0]
    patches = patch_pos.shape[0]
    nblocks = block_order.shape[0]
    heads = w_query.shape[1] // HD
    me = lax.axis_index("ctx")
    places = slot_places(block_order, me * rows, rows)
    documents, offset = document_info(places, doc_lengths)
    patch_offset = document_info(patch_pos, doc_lengths)[1]

    clean_query = project(clean_rows, w_query, q_bias, patch_offset, True)
    clean_keys = project(clean_rows, w_key, k_bias, patch_offset, True)
    clean_values = project(clean_rows, w_value, v_bias, patch_offset, False)
    tokens, clean_query = lax.optimization_barrier((tokens, clean_query))
    keys = project(tokens, w_key, k_bias, offset, True)
    values = project(tokens, w_value, v_bias, offset, False)

    width = 2 * HD
    pairs = (heads + 1) // 2
    spare = pairs * width - heads * HD
    coded = jnp.stack(
        [(patch_pos // BLOCK).astype(jnp.bfloat16), (patch_pos % BLOCK).astype(jnp.bfloat16)], axis=1
    )
    padded_query = jnp.concatenate(
        [clean_query, coded, jnp.zeros((patches, spare - 2), jnp.bfloat16)], axis=1
    )
    parts = [
        jnp.concatenate([keys, values], axis=1),
        jnp.concatenate([clean_keys, clean_values], axis=1),
    ]
    parts += [padded_query[:, p * width:(p + 1) * width] for p in range(pairs)]
    packed = jnp.concatenate(parts, axis=0)
    lines = packed.shape[0]
    gathered = lax.all_gather(packed, "ctx", axis=0, tiled=False)
    peers = gathered.shape[0]
    per_peer = lines // BLOCK
    local_blocks = rows // BLOCK

    first_q = rows + patches
    last = first_q + (pairs - 1) * patches
    code = gathered[:, last:last + patches, heads * HD - (pairs - 1) * width:][..., :2]
    code = code.reshape(peers * patches, 2).astype(jnp.float32)
    positions = (code[:, 0] * BLOCK + code[:, 1]).astype(jnp.int32)
    bounds = jnp.cumsum(doc_lengths)
    clean_documents = document_of(positions, bounds)
    query = project(tokens, w_query, q_bias, offset, True)

    inverse = jnp.zeros((nblocks,), jnp.int32).at[block_order].set(
        jnp.arange(nblocks, dtype=jnp.int32)
    )
    block_hit = (positions[None, :] // BLOCK == jnp.arange(nblocks, dtype=jnp.int32)[:, None])
    row_hit = (positions[:, None] % BLOCK == jnp.arange(BLOCK, dtype=jnp.int32)[None, :])
    patched_place = jnp.dot(
        block_hit.astype(jnp.bfloat16), row_hit.astype(jnp.bfloat16),
        preferred_element_type=jnp.float32,
    ) > 0.5

    back = MOST_DOC // BLOCK + 1
    window = (back + 1) * BLOCK
    seq_blocks = lax.dynamic_slice_in_dim(block_order, me * local_blocks, local_blocks)
    wanted = seq_blocks[:, None] - back + jnp.arange(back + 1, dtype=jnp.int32)[None, :]
    window_slots = inverse[jnp.clip(wanted, 0, nblocks - 1)]
    window_blocks = (window_slots // local_blocks) * per_peer + window_slots % local_blocks
    key_places = seq_blocks[:, None] * BLOCK - back * BLOCK + jnp.arange(window, dtype=jnp.int32)[None, :]
    key_documents = document_of(key_places, bounds)
    window_patched = patched_place[jnp.clip(wanted, 0, nblocks - 1)].reshape(local_blocks, window)
    key_kept = ((key_places >= 0) & ~window_patched).astype(jnp.int32)

    return attend(
        window_blocks.reshape(-1),
        gathered.reshape(peers * lines, width),
        query,
        places[:, None],
        documents[:, None],
        key_places,
        key_documents,
        key_kept,
        positions[None, :],
        clean_documents[None, :],
        heads=heads,
        patches=patches,
        lines=lines,
        pairs=pairs,
        back=back,
    )


def attend(window_blocks, gathered, query, query_places, query_documents, key_places,
           key_documents, key_kept, clean_places, clean_documents, *, heads, patches, lines,
           pairs, back):
    rows = query.shape[0]
    width = gathered.shape[1]
    peers = gathered.shape[0] // lines
    local_blocks = rows // BLOCK
    window = (back + 1) * BLOCK
    clean_count = peers * patches
    score_scale = HD ** (-0.5)

    def kernel(blocks_ref, g_ref, q_ref, qp_ref, qd_ref, kp_ref, kd_ref, kk_ref, cp_ref, cd_ref,
               out_ref, window_kv, clean_kv, clean_q):
        for p in range(peers):
            base = p * lines + rows
            clean_kv[p * patches:(p + 1) * patches, :] = g_ref[base:base + patches, :]
            for k in range(pairs):
                at = base + patches + k * patches
                clean_q[p * patches:(p + 1) * patches, k * width:(k + 1) * width] = g_ref[at:at + patches, :]
        match = qp_ref[...] == cp_ref[...]
        hit = match.astype(jnp.float32)
        present = jnp.sum(hit, axis=1, keepdims=True) > 0.5
        picked = jnp.dot(
            hit.astype(jnp.bfloat16), clean_q[...], preferred_element_type=jnp.float32
        ).astype(jnp.bfloat16)
        for b in range(local_blocks):
            for j in range(back + 1):
                block = blocks_ref[b * (back + 1) + j]
                start = pl.multiple_of(block * BLOCK, BLOCK)
                window_kv[j * BLOCK:(j + 1) * BLOCK, :] = g_ref[pl.ds(start, BLOCK), :]
            rows_at = slice(b * BLOCK, (b + 1) * BLOCK)
            block_present = present[rows_at, :]
            block_query = jnp.where(block_present, picked[rows_at, :heads * HD], q_ref[rows_at, :])
            q = jnp.concatenate([block_query[:, h * HD:(h + 1) * HD] for h in range(heads)], axis=0)
            qp = qp_ref[rows_at, :]
            qd = qd_ref[rows_at, :]
            visible = (qd == kd_ref[b:b + 1, :]) & (kp_ref[b:b + 1, :] <= qp) & (kk_ref[b:b + 1, :] != 0)
            clean_visible = (qd == cd_ref[...]) & (cp_ref[...] <= qp)
            hidden = jnp.concatenate([jnp.where(visible, 0.0, -1e30)] * heads, axis=0)
            clean_hidden = jnp.concatenate([jnp.where(clean_visible, 0.0, -1e30)] * heads, axis=0)
            scores = lax.dot_general(
                q, window_kv[:, :HD], (((1,), (1,)), ((), ())),
                preferred_element_type=jnp.float32,
            ) * score_scale
            clean_scores = lax.dot_general(
                q, clean_kv[:, :HD], (((1,), (1,)), ((), ())),
                preferred_element_type=jnp.float32,
            ) * score_scale
            masked = scores + hidden
            clean_masked = clean_scores + clean_hidden
            peak = jnp.maximum(
                jnp.max(masked, axis=1, keepdims=True),
                jnp.max(clean_masked, axis=1, keepdims=True),
            )
            weights = jnp.exp(masked - peak)
            clean_weights = jnp.exp(clean_masked - peak)
            total = jnp.sum(weights, axis=1, keepdims=True) + jnp.sum(
                clean_weights, axis=1, keepdims=True
            )
            mixed = jnp.dot(
                weights.astype(jnp.bfloat16), window_kv[:, HD:],
                preferred_element_type=jnp.float32,
            ) + jnp.dot(
                clean_weights.astype(jnp.bfloat16), clean_kv[:, HD:],
                preferred_element_type=jnp.float32,
            )
            result = (mixed / total).astype(out_ref.dtype)
            for h in range(heads):
                out_ref[rows_at, h * HD:(h + 1) * HD] = result[h * BLOCK:(h + 1) * BLOCK, :]

    full = lambda shape: pl.BlockSpec(shape, lambda i, *_: (0,) * len(shape))
    operands = (gathered, query, query_places, query_documents, key_places, key_documents,
                key_kept, clean_places, clean_documents)
    return pl.pallas_call(
        kernel,
        out_shape=jax.ShapeDtypeStruct(query.shape, query.dtype),
        grid_spec=pltpu.PrefetchScalarGridSpec(
            num_scalar_prefetch=1,
            grid=(1,),
            in_specs=[full(x.shape) for x in operands],
            out_specs=full(query.shape),
            scratch_shapes=[
                pltpu.VMEM((window, width), jnp.bfloat16),
                pltpu.VMEM((clean_count, width), jnp.bfloat16),
                pltpu.VMEM((clean_count, pairs * width), jnp.bfloat16),
            ],
        ),
        compiler_params=pltpu.CompilerParams(vmem_limit_bytes=48 * 1024 * 1024),
    )(window_blocks, *operands)


def solution(mesh):
    in_specs = (
        P(("run", "ctx"), None),
        P(),
        P(),
        P(("run", "ctx")),
        P(("run", "ctx"), None),
        P(None, "tp"),
        P("tp"),
        P(None, "tp"),
        P("tp"),
        P(None, "tp"),
        P("tp"),
    )
    out_specs = P(("run", "ctx"), "tp")
    return jax.shard_map(body, mesh=mesh, in_specs=in_specs, out_specs=out_specs, check_vma=False)
```

```python
import jax
import jax.numpy as jnp
from jax import lax
from jax.experimental import pallas as pl
from jax.experimental.pallas import tpu as pltpu
from jax.sharding import PartitionSpec as P

HD = 128
BLOCK = 64
MOST_DOC = 1024


THETA = 1000000.0


def rotate(head_rows, offset):
    half = head_rows.shape[-1] // 2
    frequency = jnp.power(
        jnp.float32(THETA), -2.0 * jnp.arange(half, dtype=jnp.float32) / head_rows.shape[-1]
    )
    angles = offset.astype(jnp.float32)[:, None] * frequency[None, :]
    cosines = jnp.cos(angles)[:, None, :]
    sines = jnp.sin(angles)[:, None, :]
    first_half = head_rows[..., :half]
    second_half = head_rows[..., half:]
    return jnp.concatenate(
        [first_half * cosines - second_half * sines, second_half * cosines + first_half * sines],
        axis=-1,
    )


def project(source, weight, bias, offset, rotated):
    result = (
        jnp.dot(source, weight, preferred_element_type=jnp.float32)
        + bias.astype(jnp.float32)[None, :]
    )
    if rotated:
        result = rotate(result.reshape(source.shape[0], -1, HD), offset).reshape(
            source.shape[0], -1
        )
    return result.astype(jnp.bfloat16)


def slot_places(order, first_row, row_count):
    slots = first_row + jnp.arange(row_count, dtype=jnp.int32)
    owners = slots // BLOCK
    selector = owners[:, None] == jnp.arange(order.shape[0], dtype=jnp.int32)[None, :]
    picked = jnp.sum(jnp.where(selector, order[None, :], 0), axis=1)
    return picked * BLOCK + slots % BLOCK


def document_of(places, bounds):
    return jnp.sum((places[..., None] >= bounds).astype(jnp.int32), axis=-1)


def document_info(places, lengths):
    bounds = jnp.cumsum(lengths)
    passed = places[:, None] >= bounds[None, :]
    documents = jnp.sum(passed.astype(jnp.int32), axis=1)
    starts = jnp.sum(jnp.where(passed, lengths[None, :], 0), axis=1)
    return (documents, places - starts)


def body(
    tokens,
    block_order,
    doc_lengths,
    patch_pos,
    clean_rows,
    w_query,
    q_bias,
    w_key,
    k_bias,
    w_value,
    v_bias,
):
    rows = tokens.shape[0]
    patches = patch_pos.shape[0]
    nblocks = block_order.shape[0]
    heads = w_query.shape[1] // HD
    me = lax.axis_index("ctx")
    places = slot_places(block_order, me * rows, rows)
    documents, offset = document_info(places, doc_lengths)
    patch_offset = document_info(patch_pos, doc_lengths)[1]

    keys = project(tokens, w_key, k_bias, offset, True)
    values = project(tokens, w_value, v_bias, offset, False)
    clean_query = project(clean_rows, w_query, q_bias, patch_offset, True)
    clean_keys = project(clean_rows, w_key, k_bias, patch_offset, True)
    clean_values = project(clean_rows, w_value, v_bias, patch_offset, False)

    width = 2 * HD
    pairs = (heads + 1) // 2
    spare = pairs * width - heads * HD
    coded = jnp.stack(
        [(patch_pos // BLOCK).astype(jnp.bfloat16), (patch_pos % BLOCK).astype(jnp.bfloat16)], axis=1
    )
    padded_query = jnp.concatenate(
        [clean_query, coded, jnp.zeros((patches, spare - 2), jnp.bfloat16)], axis=1
    )
    parts = [
        jnp.concatenate([keys, values], axis=1),
        jnp.concatenate([clean_keys, clean_values], axis=1),
    ]
    parts += [padded_query[:, p * width:(p + 1) * width] for p in range(pairs)]
    packed = jnp.concatenate(parts, axis=0)
    lines = packed.shape[0]
    gathered = lax.all_gather(packed, "ctx", axis=0, tiled=False)
    peers = gathered.shape[0]
    per_peer = lines // BLOCK
    local_blocks = rows // BLOCK

    bounds = jnp.cumsum(doc_lengths)
    query = project(tokens, w_query, q_bias, offset, True)

    inverse = jnp.zeros((nblocks,), jnp.int32).at[block_order].set(
        jnp.arange(nblocks, dtype=jnp.int32)
    )
    back = MOST_DOC // BLOCK + 1
    window = (back + 1) * BLOCK
    seq_blocks = lax.dynamic_slice_in_dim(block_order, me * local_blocks, local_blocks)
    wanted = seq_blocks[:, None] - back + jnp.arange(back + 1, dtype=jnp.int32)[None, :]
    window_slots = inverse[jnp.clip(wanted, 0, nblocks - 1)]
    window_blocks = (window_slots // local_blocks) * per_peer + window_slots % local_blocks
    key_places = seq_blocks[:, None] * BLOCK - back * BLOCK + jnp.arange(window, dtype=jnp.int32)[None, :]
    key_documents = document_of(key_places, bounds)
    return attend(
        window_blocks.reshape(-1),
        gathered.reshape(peers * lines, width),
        query,
        places[:, None],
        documents[:, None],
        key_places,
        key_documents,
        bounds[:, None],
        heads=heads,
        patches=patches,
        lines=lines,
        pairs=pairs,
        back=back,
    )


def attend(window_blocks, gathered, query, query_places, query_documents, key_places,
           key_documents, bounds, *, heads, patches, lines,
           pairs, back):
    rows = query.shape[0]
    width = gathered.shape[1]
    peers = gathered.shape[0] // lines
    local_blocks = rows // BLOCK
    window = (back + 1) * BLOCK
    clean_count = peers * patches
    score_scale = HD ** (-0.5)

    def kernel(blocks_ref, g_ref, q_ref, qp_ref, qd_ref, kp_ref, kd_ref, bounds_ref,
               out_ref, window_kv, clean_kv, clean_q):
        for p in range(peers):
            base = p * lines + rows
            clean_kv[p * patches:(p + 1) * patches, :] = g_ref[base:base + patches, :]
            for k in range(pairs):
                at = base + patches + k * patches
                clean_q[p * patches:(p + 1) * patches, k * width:(k + 1) * width] = g_ref[at:at + patches, :]
        codes = clean_q[:, heads * HD:heads * HD + HD].astype(jnp.float32)
        clean_column = (codes[:, 0:1] * BLOCK + codes[:, 1:2]).astype(jnp.int32)
        codes = jnp.transpose(codes)
        clean_row = (codes[0:1, :] * BLOCK + codes[1:2, :]).astype(jnp.int32)
        clean_documents = jnp.sum(
            (clean_row >= bounds_ref[...]).astype(jnp.int32), axis=0, keepdims=True)
        match = qp_ref[...] == clean_row
        hit = match.astype(jnp.float32)
        present = jnp.sum(hit, axis=1, keepdims=True) > 0.5
        picked = jnp.dot(
            hit.astype(jnp.bfloat16), clean_q[...], preferred_element_type=jnp.float32
        ).astype(jnp.bfloat16)
        for b in range(local_blocks):
            for j in range(back + 1):
                block = blocks_ref[b * (back + 1) + j]
                start = pl.multiple_of(block * BLOCK, BLOCK)
                window_kv[j * BLOCK:(j + 1) * BLOCK, :] = g_ref[pl.ds(start, BLOCK), :]
            rows_at = slice(b * BLOCK, (b + 1) * BLOCK)
            block_present = present[rows_at, :]
            block_query = jnp.where(block_present, picked[rows_at, :heads * HD], q_ref[rows_at, :])
            q = jnp.concatenate([block_query[:, h * HD:(h + 1) * HD] for h in range(heads)], axis=0)
            qp = qp_ref[rows_at, :]
            qd = qd_ref[rows_at, :]
            kp = kp_ref[b:b + 1, :]
            patched = jnp.max((clean_column == kp).astype(jnp.int32), axis=0, keepdims=True)
            kept = (kp >= 0) & (patched == 0)
            visible = (qd == kd_ref[b:b + 1, :]) & (kp <= qp) & kept
            clean_visible = (qd == clean_documents) & (clean_row <= qp)
            hidden = jnp.concatenate([jnp.where(visible, 0.0, -1e30)] * heads, axis=0)
            clean_hidden = jnp.concatenate([jnp.where(clean_visible, 0.0, -1e30)] * heads, axis=0)
            scores = lax.dot_general(
                q, window_kv[:, :HD], (((1,), (1,)), ((), ())),
                preferred_element_type=jnp.float32,
            ) * score_scale
            clean_scores = lax.dot_general(
                q, clean_kv[:, :HD], (((1,), (1,)), ((), ())),
                preferred_element_type=jnp.float32,
            ) * score_scale
            masked = scores + hidden
            clean_masked = clean_scores + clean_hidden
            peak = jnp.maximum(
                jnp.max(masked, axis=1, keepdims=True),
                jnp.max(clean_masked, axis=1, keepdims=True),
            )
            weights = jnp.exp(masked - peak)
            clean_weights = jnp.exp(clean_masked - peak)
            total = jnp.sum(weights, axis=1, keepdims=True) + jnp.sum(
                clean_weights, axis=1, keepdims=True
            )
            mixed = jnp.dot(
                weights.astype(jnp.bfloat16), window_kv[:, HD:],
                preferred_element_type=jnp.float32,
            ) + jnp.dot(
                clean_weights.astype(jnp.bfloat16), clean_kv[:, HD:],
                preferred_element_type=jnp.float32,
            )
            result = (mixed / total).astype(out_ref.dtype)
            for h in range(heads):
                out_ref[rows_at, h * HD:(h + 1) * HD] = result[h * BLOCK:(h + 1) * BLOCK, :]

    full = lambda shape: pl.BlockSpec(shape, lambda i, *_: (0,) * len(shape))
    operands = (gathered, query, query_places, query_documents, key_places, key_documents,
                bounds)
    return pl.pallas_call(
        kernel,
        out_shape=jax.ShapeDtypeStruct(query.shape, query.dtype),
        grid_spec=pltpu.PrefetchScalarGridSpec(
            num_scalar_prefetch=1,
            grid=(1,),
            in_specs=[full(x.shape) for x in operands],
            out_specs=full(query.shape),
            scratch_shapes=[
                pltpu.VMEM((window, width), jnp.bfloat16),
                pltpu.VMEM((clean_count, width), jnp.bfloat16),
                pltpu.VMEM((clean_count, pairs * width), jnp.bfloat16),
            ],
        ),
        compiler_params=pltpu.CompilerParams(vmem_limit_bytes=48 * 1024 * 1024),
    )(window_blocks, *operands)


def solution(mesh):
    in_specs = (
        P(("run", "ctx"), None),
        P(),
        P(),
        P(("run", "ctx")),
        P(("run", "ctx"), None),
        P(None, "tp"),
        P("tp"),
        P(None, "tp"),
        P("tp"),
        P(None, "tp"),
        P("tp"),
    )
    out_specs = P(("run", "ctx"), "tp")
    return jax.shard_map(body, mesh=mesh, in_specs=in_specs, out_specs=out_specs, check_vma=False)
```

```python
import jax
import jax.numpy as jnp
from jax import lax
from jax.experimental import pallas as pl
from jax.experimental.pallas import tpu as pltpu
from jax.sharding import PartitionSpec as P

HD = 128
BLOCK = 64
MOST_DOC = 1024


THETA = 1000000.0


def rotate(head_rows, offset):
    half = head_rows.shape[-1] // 2
    frequency = jnp.power(
        jnp.float32(THETA), -2.0 * jnp.arange(half, dtype=jnp.float32) / head_rows.shape[-1]
    )
    angles = offset.astype(jnp.float32)[:, None] * frequency[None, :]
    cosines = jnp.cos(angles)[:, None, :]
    sines = jnp.sin(angles)[:, None, :]
    first_half = head_rows[..., :half]
    second_half = head_rows[..., half:]
    return jnp.concatenate(
        [first_half * cosines - second_half * sines, second_half * cosines + first_half * sines],
        axis=-1,
    )


def project(source, weight, bias, offset, rotated):
    result = (
        jnp.dot(source, weight, preferred_element_type=jnp.float32)
        + bias.astype(jnp.float32)[None, :]
    )
    if rotated:
        result = rotate(result.reshape(source.shape[0], -1, HD), offset).reshape(
            source.shape[0], -1
        )
    return result.astype(jnp.bfloat16)


def slot_places(order, first_row, row_count):
    slots = first_row + jnp.arange(row_count, dtype=jnp.int32)
    owners = slots // BLOCK
    selector = owners[:, None] == jnp.arange(order.shape[0], dtype=jnp.int32)[None, :]
    picked = jnp.sum(jnp.where(selector, order[None, :], 0), axis=1)
    return picked * BLOCK + slots % BLOCK


def document_of(places, bounds):
    return jnp.sum((places[..., None] >= bounds).astype(jnp.int32), axis=-1)


def document_info(places, lengths):
    bounds = jnp.cumsum(lengths)
    passed = places[:, None] >= bounds[None, :]
    documents = jnp.sum(passed.astype(jnp.int32), axis=1)
    starts = jnp.sum(jnp.where(passed, lengths[None, :], 0), axis=1)
    return (documents, places - starts)


def body(
    tokens,
    block_order,
    doc_lengths,
    patch_pos,
    clean_rows,
    w_query,
    q_bias,
    w_key,
    k_bias,
    w_value,
    v_bias,
):
    rows = tokens.shape[0]
    patches = patch_pos.shape[0]
    nblocks = block_order.shape[0]
    heads = w_query.shape[1] // HD
    me = lax.axis_index("ctx")
    places = slot_places(block_order, me * rows, rows)
    documents, offset = document_info(places, doc_lengths)
    patch_offset = document_info(patch_pos, doc_lengths)[1]

    keys = project(tokens, w_key, k_bias, offset, True)
    values = project(tokens, w_value, v_bias, offset, False)
    clean_query = project(clean_rows, w_query, q_bias, patch_offset, True)
    clean_keys = project(clean_rows, w_key, k_bias, patch_offset, True)
    clean_values = project(clean_rows, w_value, v_bias, patch_offset, False)

    width = 2 * HD
    pairs = (heads + 1) // 2
    spare = pairs * width - heads * HD
    coded = jnp.stack(
        [(patch_pos // BLOCK).astype(jnp.bfloat16), (patch_pos % BLOCK).astype(jnp.bfloat16)], axis=1
    )
    padded_query = jnp.concatenate(
        [clean_query, coded, jnp.zeros((patches, spare - 2), jnp.bfloat16)], axis=1
    )
    parts = [
        jnp.concatenate([keys, values], axis=1),
        jnp.concatenate([clean_keys, clean_values], axis=1),
    ]
    parts += [padded_query[:, p * width:(p + 1) * width] for p in range(pairs)]
    packed = jnp.concatenate(parts, axis=0)
    lines = packed.shape[0]
    gathered = lax.all_gather(packed, "ctx", axis=0, tiled=False)
    peers = gathered.shape[0]
    per_peer = lines // BLOCK
    local_blocks = rows // BLOCK

    bounds = jnp.cumsum(doc_lengths)
    query = project(tokens, w_query, q_bias, offset, True)

    inverse = jnp.zeros((nblocks,), jnp.int32).at[block_order].set(
        jnp.arange(nblocks, dtype=jnp.int32)
    )
    back = MOST_DOC // BLOCK + 1
    window = (back + 1) * BLOCK
    seq_blocks = lax.dynamic_slice_in_dim(block_order, me * local_blocks, local_blocks)
    wanted = seq_blocks[:, None] - back + jnp.arange(back + 1, dtype=jnp.int32)[None, :]
    window_slots = inverse[jnp.clip(wanted, 0, nblocks - 1)]
    window_blocks = (window_slots // local_blocks) * per_peer + window_slots % local_blocks
    key_places = seq_blocks[:, None] * BLOCK - back * BLOCK + jnp.arange(window, dtype=jnp.int32)[None, :]
    key_documents = document_of(key_places, bounds)
    return attend(
        window_blocks.reshape(-1),
        gathered.reshape(peers * lines, width),
        query,
        places[:, None],
        documents[:, None],
        key_places,
        key_documents,
        bounds[:, None],
        jnp.floor_divide(key_places, BLOCK),
        jnp.remainder(key_places, BLOCK),
        heads=heads,
        patches=patches,
        lines=lines,
        pairs=pairs,
        back=back,
    )


def attend(window_blocks, gathered, query, query_places, query_documents, key_places,
           key_documents, bounds, key_blocks, key_rows, *, heads, patches, lines,
           pairs, back):
    rows = query.shape[0]
    width = gathered.shape[1]
    peers = gathered.shape[0] // lines
    local_blocks = rows // BLOCK
    window = (back + 1) * BLOCK
    clean_count = peers * patches
    score_scale = HD ** (-0.5)

    def kernel(blocks_ref, g_ref, q_ref, qp_ref, qd_ref, kp_ref, kd_ref, bounds_ref, kb_ref, kr_ref,
               out_ref, window_kv, clean_kv, clean_q):
        for p in range(peers):
            base = p * lines + rows
            clean_kv[p * patches:(p + 1) * patches, :] = g_ref[base:base + patches, :]
            for k in range(pairs):
                at = base + patches + k * patches
                clean_q[p * patches:(p + 1) * patches, k * width:(k + 1) * width] = g_ref[at:at + patches, :]
        codes = clean_q[:, heads * HD:heads * HD + HD].astype(jnp.float32)
        clean_column = (codes[:, 0:1] * BLOCK + codes[:, 1:2]).astype(jnp.int32)
        codes = jnp.transpose(codes)
        clean_row = (codes[0:1, :] * BLOCK + codes[1:2, :]).astype(jnp.int32)
        clean_documents = jnp.sum(
            (clean_row >= bounds_ref[...]).astype(jnp.int32), axis=0, keepdims=True)
        lanes = lax.broadcasted_iota(jnp.int32, (1, BLOCK), 1)
        sublanes = lax.broadcasted_iota(jnp.int32, (BLOCK, 1), 0)
        row_hit = (codes[1:2, :].astype(jnp.int32) == sublanes).astype(jnp.bfloat16)
        block_hit = (clean_q[:, heads * HD:heads * HD + 1].astype(jnp.int32) == lanes).astype(jnp.bfloat16)
        grid = jnp.dot(row_hit, block_hit, preferred_element_type=jnp.float32)
        match = qp_ref[...] == clean_row
        hit = match.astype(jnp.float32)
        present = jnp.sum(hit, axis=1, keepdims=True) > 0.5
        picked = jnp.dot(
            hit.astype(jnp.bfloat16), clean_q[...], preferred_element_type=jnp.float32
        ).astype(jnp.bfloat16)
        for b in range(local_blocks):
            for j in range(back + 1):
                block = blocks_ref[b * (back + 1) + j]
                start = pl.multiple_of(block * BLOCK, BLOCK)
                window_kv[j * BLOCK:(j + 1) * BLOCK, :] = g_ref[pl.ds(start, BLOCK), :]
            rows_at = slice(b * BLOCK, (b + 1) * BLOCK)
            block_present = present[rows_at, :]
            block_query = jnp.where(block_present, picked[rows_at, :heads * HD], q_ref[rows_at, :])
            q = jnp.concatenate([block_query[:, h * HD:(h + 1) * HD] for h in range(heads)], axis=0)
            qp = qp_ref[rows_at, :]
            qd = qd_ref[rows_at, :]
            kp = kp_ref[b:b + 1, :]
            block_of = (kb_ref[b:b + 1, :] == sublanes).astype(jnp.float32)
            by_row = jnp.dot(grid, block_of, preferred_element_type=jnp.float32)
            row_of = (kr_ref[b:b + 1, :] == sublanes).astype(jnp.float32)
            patched = jnp.sum(by_row * row_of, axis=0, keepdims=True)
            kept = (kp >= 0) & (patched < 0.5)
            visible = (qd == kd_ref[b:b + 1, :]) & (kp <= qp) & kept
            clean_visible = (qd == clean_documents) & (clean_row <= qp)
            hidden = jnp.concatenate([jnp.where(visible, 0.0, -1e30)] * heads, axis=0)
            clean_hidden = jnp.concatenate([jnp.where(clean_visible, 0.0, -1e30)] * heads, axis=0)
            scores = lax.dot_general(
                q, window_kv[:, :HD], (((1,), (1,)), ((), ())),
                preferred_element_type=jnp.float32,
            ) * score_scale
            clean_scores = lax.dot_general(
                q, clean_kv[:, :HD], (((1,), (1,)), ((), ())),
                preferred_element_type=jnp.float32,
            ) * score_scale
            masked = scores + hidden
            clean_masked = clean_scores + clean_hidden
            peak = jnp.maximum(
                jnp.max(masked, axis=1, keepdims=True),
                jnp.max(clean_masked, axis=1, keepdims=True),
            )
            weights = jnp.exp(masked - peak)
            clean_weights = jnp.exp(clean_masked - peak)
            total = jnp.sum(weights, axis=1, keepdims=True) + jnp.sum(
                clean_weights, axis=1, keepdims=True
            )
            mixed = jnp.dot(
                weights.astype(jnp.bfloat16), window_kv[:, HD:],
                preferred_element_type=jnp.float32,
            ) + jnp.dot(
                clean_weights.astype(jnp.bfloat16), clean_kv[:, HD:],
                preferred_element_type=jnp.float32,
            )
            result = (mixed / total).astype(out_ref.dtype)
            for h in range(heads):
                out_ref[rows_at, h * HD:(h + 1) * HD] = result[h * BLOCK:(h + 1) * BLOCK, :]

    full = lambda shape: pl.BlockSpec(shape, lambda i, *_: (0,) * len(shape))
    operands = (gathered, query, query_places, query_documents, key_places, key_documents,
                bounds, key_blocks, key_rows)
    return pl.pallas_call(
        kernel,
        out_shape=jax.ShapeDtypeStruct(query.shape, query.dtype),
        grid_spec=pltpu.PrefetchScalarGridSpec(
            num_scalar_prefetch=1,
            grid=(1,),
            in_specs=[full(x.shape) for x in operands],
            out_specs=full(query.shape),
            scratch_shapes=[
                pltpu.VMEM((window, width), jnp.bfloat16),
                pltpu.VMEM((clean_count, width), jnp.bfloat16),
                pltpu.VMEM((clean_count, pairs * width), jnp.bfloat16),
            ],
        ),
        compiler_params=pltpu.CompilerParams(vmem_limit_bytes=48 * 1024 * 1024),
    )(window_blocks, *operands)


def solution(mesh):
    in_specs = (
        P(("run", "ctx"), None),
        P(),
        P(),
        P(("run", "ctx")),
        P(("run", "ctx"), None),
        P(None, "tp"),
        P("tp"),
        P(None, "tp"),
        P("tp"),
        P(None, "tp"),
        P("tp"),
    )
    out_specs = P(("run", "ctx"), "tp")
    return jax.shard_map(body, mesh=mesh, in_specs=in_specs, out_specs=out_specs, check_vma=False)
```

```python
import jax
import jax.numpy as jnp
from jax import lax
from jax.experimental import pallas as pl
from jax.experimental.pallas import tpu as pltpu
from jax.sharding import PartitionSpec as P

HD = 128
BLOCK = 64
MOST_DOC = 1024


THETA = 1000000.0


def rotate(head_rows, offset):
    half = head_rows.shape[-1] // 2
    frequency = jnp.power(
        jnp.float32(THETA), -2.0 * jnp.arange(half, dtype=jnp.float32) / head_rows.shape[-1]
    )
    angles = offset.astype(jnp.float32)[:, None] * frequency[None, :]
    cosines = jnp.cos(angles)[:, None, :]
    sines = jnp.sin(angles)[:, None, :]
    first_half = head_rows[..., :half]
    second_half = head_rows[..., half:]
    return jnp.concatenate(
        [first_half * cosines - second_half * sines, second_half * cosines + first_half * sines],
        axis=-1,
    )


def project(source, weight, bias, offset, rotated):
    result = (
        jnp.dot(source, weight, preferred_element_type=jnp.float32)
        + bias.astype(jnp.float32)[None, :]
    )
    if rotated:
        result = rotate(result.reshape(source.shape[0], -1, HD), offset).reshape(
            source.shape[0], -1
        )
    return result.astype(jnp.bfloat16)


def slot_places(order, first_row, row_count):
    slots = first_row + jnp.arange(row_count, dtype=jnp.int32)
    owners = slots // BLOCK
    selector = owners[:, None] == jnp.arange(order.shape[0], dtype=jnp.int32)[None, :]
    picked = jnp.sum(jnp.where(selector, order[None, :], 0), axis=1)
    return picked * BLOCK + slots % BLOCK


def document_of(places, bounds):
    return jnp.sum((places[..., None] >= bounds).astype(jnp.int32), axis=-1)


def document_info(places, lengths):
    bounds = jnp.cumsum(lengths)
    passed = places[:, None] >= bounds[None, :]
    documents = jnp.sum(passed.astype(jnp.int32), axis=1)
    starts = jnp.sum(jnp.where(passed, lengths[None, :], 0), axis=1)
    return (documents, places - starts)


def body(
    tokens,
    block_order,
    doc_lengths,
    patch_pos,
    clean_rows,
    w_query,
    q_bias,
    w_key,
    k_bias,
    w_value,
    v_bias,
):
    rows = tokens.shape[0]
    patches = patch_pos.shape[0]
    nblocks = block_order.shape[0]
    heads = w_query.shape[1] // HD
    me = lax.axis_index("ctx")
    places = slot_places(block_order, me * rows, rows)
    documents, offset = document_info(places, doc_lengths)
    patch_offset = document_info(patch_pos, doc_lengths)[1]

    keys = project(tokens, w_key, k_bias, offset, True)
    values = project(tokens, w_value, v_bias, offset, False)
    clean_query = project(clean_rows, w_query, q_bias, patch_offset, True)
    clean_keys = project(clean_rows, w_key, k_bias, patch_offset, True)
    clean_values = project(clean_rows, w_value, v_bias, patch_offset, False)

    width = 2 * HD
    pairs = (heads + 1) // 2
    spare = pairs * width - heads * HD
    coded = jnp.stack(
        [(patch_pos // BLOCK).astype(jnp.bfloat16), (patch_pos % BLOCK).astype(jnp.bfloat16)], axis=1
    )
    padded_query = jnp.concatenate(
        [clean_query, coded, jnp.zeros((patches, spare - 2), jnp.bfloat16)], axis=1
    )
    parts = [
        jnp.concatenate([keys, values], axis=1),
        jnp.concatenate([clean_keys, clean_values], axis=1),
    ]
    parts += [padded_query[:, p * width:(p + 1) * width] for p in range(pairs)]
    packed = jnp.concatenate(parts, axis=0)
    lines = packed.shape[0]
    gathered = lax.all_gather(packed, "ctx", axis=0, tiled=False)
    peers = gathered.shape[0]
    per_peer = lines // BLOCK
    local_blocks = rows // BLOCK

    bounds = jnp.cumsum(doc_lengths)
    query = project(tokens, w_query, q_bias, offset, True)

    inverse = jnp.zeros((nblocks,), jnp.int32).at[block_order].set(
        jnp.arange(nblocks, dtype=jnp.int32)
    )
    back = MOST_DOC // BLOCK + 1
    window = (back + 1) * BLOCK
    seq_blocks = lax.dynamic_slice_in_dim(block_order, me * local_blocks, local_blocks)
    wanted = seq_blocks[:, None] - back + jnp.arange(back + 1, dtype=jnp.int32)[None, :]
    window_slots = inverse[jnp.clip(wanted, 0, nblocks - 1)]
    window_blocks = (window_slots // local_blocks) * per_peer + window_slots % local_blocks
    key_places = seq_blocks[:, None] * BLOCK - back * BLOCK + jnp.arange(window, dtype=jnp.int32)[None, :]
    key_documents = document_of(key_places, bounds)
    return attend(
        window_blocks.reshape(-1),
        gathered.reshape(peers * lines, width),
        query,
        places[:, None],
        documents[:, None],
        key_places,
        key_documents,
        bounds[:, None],
        heads=heads,
        patches=patches,
        lines=lines,
        pairs=pairs,
        back=back,
    )


def attend(window_blocks, gathered, query, query_places, query_documents, key_places,
           key_documents, bounds, *, heads, patches, lines,
           pairs, back):
    rows = query.shape[0]
    width = gathered.shape[1]
    peers = gathered.shape[0] // lines
    local_blocks = rows // BLOCK
    window = (back + 1) * BLOCK
    clean_count = peers * patches
    score_scale = HD ** (-0.5)

    def kernel(blocks_ref, g_ref, q_ref, qp_ref, qd_ref, kp_ref, kd_ref, bounds_ref,
               out_ref, window_kv, clean_kv, clean_q):
        for p in range(peers):
            base = p * lines + rows
            clean_kv[p * patches:(p + 1) * patches, :] = g_ref[base:base + patches, :]
            for k in range(pairs):
                at = base + patches + k * patches
                clean_q[p * patches:(p + 1) * patches, k * width:(k + 1) * width] = g_ref[at:at + patches, :]
        codes = clean_q[:, heads * HD:heads * HD + HD].astype(jnp.float32)
        clean_column = (codes[:, 0:1] * BLOCK + codes[:, 1:2]).astype(jnp.int32)
        codes = jnp.transpose(codes)
        clean_row = (codes[0:1, :] * BLOCK + codes[1:2, :]).astype(jnp.int32)
        clean_documents = jnp.sum(
            (clean_row >= bounds_ref[...]).astype(jnp.int32), axis=0, keepdims=True)
        match = qp_ref[...] == clean_row
        hit = match.astype(jnp.float32)
        present = jnp.sum(hit, axis=1, keepdims=True) > 0.5
        picked = jnp.dot(
            hit.astype(jnp.bfloat16), clean_q[:, :heads * HD], preferred_element_type=jnp.float32
        ).astype(jnp.bfloat16)
        for b in range(local_blocks):
            for j in range(back + 1):
                block = blocks_ref[b * (back + 1) + j]
                start = pl.multiple_of(block * BLOCK, BLOCK)
                window_kv[j * BLOCK:(j + 1) * BLOCK, :] = g_ref[pl.ds(start, BLOCK), :]
            rows_at = slice(b * BLOCK, (b + 1) * BLOCK)
            block_present = present[rows_at, :]
            block_query = jnp.where(block_present, picked[rows_at, :], q_ref[rows_at, :])
            q = jnp.concatenate([block_query[:, h * HD:(h + 1) * HD] for h in range(heads)], axis=0)
            qp = qp_ref[rows_at, :]
            qd = qd_ref[rows_at, :]
            kp = kp_ref[b:b + 1, :]
            patched = jnp.max((clean_column == kp).astype(jnp.int32), axis=0, keepdims=True)
            kept = (kp >= 0) & (patched == 0)
            visible = (qd == kd_ref[b:b + 1, :]) & (kp <= qp) & kept
            clean_visible = (qd == clean_documents) & (clean_row <= qp)
            hidden = jnp.concatenate([jnp.where(visible, 0.0, -1e30)] * heads, axis=0)
            clean_hidden = jnp.concatenate([jnp.where(clean_visible, 0.0, -1e30)] * heads, axis=0)
            scores = lax.dot_general(
                q, window_kv[:, :HD], (((1,), (1,)), ((), ())),
                preferred_element_type=jnp.float32,
            ) * score_scale
            clean_scores = lax.dot_general(
                q, clean_kv[:, :HD], (((1,), (1,)), ((), ())),
                preferred_element_type=jnp.float32,
            ) * score_scale
            masked = scores + hidden
            clean_masked = clean_scores + clean_hidden
            peak = jnp.maximum(
                jnp.max(masked, axis=1, keepdims=True),
                jnp.max(clean_masked, axis=1, keepdims=True),
            )
            weights = jnp.exp(masked - peak)
            clean_weights = jnp.exp(clean_masked - peak)
            total = jnp.sum(weights, axis=1, keepdims=True) + jnp.sum(
                clean_weights, axis=1, keepdims=True
            )
            mixed = jnp.dot(
                weights.astype(jnp.bfloat16), window_kv[:, HD:],
                preferred_element_type=jnp.float32,
            ) + jnp.dot(
                clean_weights.astype(jnp.bfloat16), clean_kv[:, HD:],
                preferred_element_type=jnp.float32,
            )
            result = (mixed / total).astype(out_ref.dtype)
            for h in range(heads):
                out_ref[rows_at, h * HD:(h + 1) * HD] = result[h * BLOCK:(h + 1) * BLOCK, :]

    full = lambda shape: pl.BlockSpec(shape, lambda i, *_: (0,) * len(shape))
    operands = (gathered, query, query_places, query_documents, key_places, key_documents,
                bounds)
    return pl.pallas_call(
        kernel,
        out_shape=jax.ShapeDtypeStruct(query.shape, query.dtype),
        grid_spec=pltpu.PrefetchScalarGridSpec(
            num_scalar_prefetch=1,
            grid=(1,),
            in_specs=[full(x.shape) for x in operands],
            out_specs=full(query.shape),
            scratch_shapes=[
                pltpu.VMEM((window, width), jnp.bfloat16),
                pltpu.VMEM((clean_count, width), jnp.bfloat16),
                pltpu.VMEM((clean_count, pairs * width), jnp.bfloat16),
            ],
        ),
        compiler_params=pltpu.CompilerParams(vmem_limit_bytes=48 * 1024 * 1024),
    )(window_blocks, *operands)


def solution(mesh):
    in_specs = (
        P(("run", "ctx"), None),
        P(),
        P(),
        P(("run", "ctx")),
        P(("run", "ctx"), None),
        P(None, "tp"),
        P("tp"),
        P(None, "tp"),
        P("tp"),
        P(None, "tp"),
        P("tp"),
    )
    out_specs = P(("run", "ctx"), "tp")
    return jax.shard_map(body, mesh=mesh, in_specs=in_specs, out_specs=out_specs, check_vma=False)
```

```python
import jax
import jax.numpy as jnp
from jax import lax
from jax.experimental import pallas as pl
from jax.experimental.pallas import tpu as pltpu
from jax.sharding import PartitionSpec as P

HD = 128
BLOCK = 64
MOST_DOC = 1024


THETA = 1000000.0


def rotate(head_rows, offset):
    half = head_rows.shape[-1] // 2
    frequency = jnp.power(
        jnp.float32(THETA), -2.0 * jnp.arange(half, dtype=jnp.float32) / head_rows.shape[-1]
    )
    angles = offset.astype(jnp.float32)[:, None] * frequency[None, :]
    cosines = jnp.cos(angles)[:, None, :]
    sines = jnp.sin(angles)[:, None, :]
    first_half = head_rows[..., :half]
    second_half = head_rows[..., half:]
    return jnp.concatenate(
        [first_half * cosines - second_half * sines, second_half * cosines + first_half * sines],
        axis=-1,
    )


def project(source, weight, bias, offset, rotated):
    result = (
        jnp.dot(source, weight, preferred_element_type=jnp.float32)
        + bias.astype(jnp.float32)[None, :]
    )
    if rotated:
        result = rotate(result.reshape(source.shape[0], -1, HD), offset).reshape(
            source.shape[0], -1
        )
    return result.astype(jnp.bfloat16)


def slot_places(order, first_row, row_count):
    slots = first_row + jnp.arange(row_count, dtype=jnp.int32)
    owners = slots // BLOCK
    selector = owners[:, None] == jnp.arange(order.shape[0], dtype=jnp.int32)[None, :]
    picked = jnp.sum(jnp.where(selector, order[None, :], 0), axis=1)
    return picked * BLOCK + slots % BLOCK


def document_of(places, bounds):
    return jnp.sum((places[..., None] >= bounds).astype(jnp.int32), axis=-1)


def document_info(places, lengths):
    bounds = jnp.cumsum(lengths)
    passed = places[:, None] >= bounds[None, :]
    documents = jnp.sum(passed.astype(jnp.int32), axis=1)
    starts = jnp.sum(jnp.where(passed, lengths[None, :], 0), axis=1)
    return (documents, places - starts)


def body(
    tokens,
    block_order,
    doc_lengths,
    patch_pos,
    clean_rows,
    w_query,
    q_bias,
    w_key,
    k_bias,
    w_value,
    v_bias,
):
    rows = tokens.shape[0]
    patches = patch_pos.shape[0]
    nblocks = block_order.shape[0]
    heads = w_query.shape[1] // HD
    me = lax.axis_index("ctx")
    places = slot_places(block_order, me * rows, rows)
    documents, offset = document_info(places, doc_lengths)
    patch_offset = document_info(patch_pos, doc_lengths)[1]

    keys = project(tokens, w_key, k_bias, offset, True)
    values = project(tokens, w_value, v_bias, offset, False)
    clean_query = project(clean_rows, w_query, q_bias, patch_offset, True)
    clean_keys = project(clean_rows, w_key, k_bias, patch_offset, True)
    clean_values = project(clean_rows, w_value, v_bias, patch_offset, False)

    width = 2 * HD
    pairs = (heads + 1) // 2
    spare = pairs * width - heads * HD
    coded = jnp.stack(
        [(patch_pos // BLOCK).astype(jnp.bfloat16), (patch_pos % BLOCK).astype(jnp.bfloat16)], axis=1
    )
    padded_query = jnp.concatenate(
        [clean_query, coded, jnp.zeros((patches, spare - 2), jnp.bfloat16)], axis=1
    )
    parts = [
        jnp.concatenate([keys, values], axis=1),
        jnp.concatenate([clean_keys, clean_values], axis=1),
    ]
    parts += [padded_query[:, p * width:(p + 1) * width] for p in range(pairs)]
    packed = jnp.concatenate(parts, axis=0)
    lines = packed.shape[0]
    gathered = lax.all_gather(packed, "ctx", axis=0, tiled=False)
    peers = gathered.shape[0]
    per_peer = lines // BLOCK
    local_blocks = rows // BLOCK

    bounds = jnp.cumsum(doc_lengths)
    query = project(tokens, w_query, q_bias, offset, True)

    inverse = jnp.zeros((nblocks,), jnp.int32).at[block_order].set(
        jnp.arange(nblocks, dtype=jnp.int32)
    )
    back = MOST_DOC // BLOCK + 1
    window = (back + 1) * BLOCK
    seq_blocks = lax.dynamic_slice_in_dim(block_order, me * local_blocks, local_blocks)
    wanted = seq_blocks[:, None] - back + jnp.arange(back + 1, dtype=jnp.int32)[None, :]
    window_slots = inverse[jnp.clip(wanted, 0, nblocks - 1)]
    window_blocks = (window_slots // local_blocks) * per_peer + window_slots % local_blocks
    key_places = seq_blocks[:, None] * BLOCK - back * BLOCK + jnp.arange(window, dtype=jnp.int32)[None, :]
    key_documents = document_of(key_places, bounds)
    return attend(
        window_blocks.reshape(-1),
        gathered.reshape(peers * lines, width),
        query,
        places[:, None],
        documents[:, None],
        key_places,
        key_documents,
        bounds[:, None],
        jnp.floor_divide(key_places, BLOCK),
        jnp.remainder(key_places, BLOCK),
        heads=heads,
        patches=patches,
        lines=lines,
        pairs=pairs,
        back=back,
    )


def attend(window_blocks, gathered, query, query_places, query_documents, key_places,
           key_documents, bounds, key_blocks, key_rows, *, heads, patches, lines,
           pairs, back):
    rows = query.shape[0]
    width = gathered.shape[1]
    peers = gathered.shape[0] // lines
    local_blocks = rows // BLOCK
    window = (back + 1) * BLOCK
    clean_count = peers * patches
    score_scale = HD ** (-0.5)

    def kernel(blocks_ref, g_ref, q_ref, qp_ref, qd_ref, kp_ref, kd_ref, bounds_ref, kb_ref, kr_ref,
               out_ref, window_kv, clean_kv, clean_q):
        for p in range(peers):
            base = p * lines + rows
            clean_kv[p * patches:(p + 1) * patches, :] = g_ref[base:base + patches, :]
            for k in range(pairs):
                at = base + patches + k * patches
                clean_q[p * patches:(p + 1) * patches, k * width:(k + 1) * width] = g_ref[at:at + patches, :]
        codes = clean_q[:, heads * HD:heads * HD + HD].astype(jnp.float32)
        clean_column = (codes[:, 0:1] * BLOCK + codes[:, 1:2]).astype(jnp.int32)
        codes = jnp.transpose(codes)
        clean_row = (codes[0:1, :] * BLOCK + codes[1:2, :]).astype(jnp.int32)
        clean_documents = jnp.sum(
            (clean_row >= bounds_ref[...]).astype(jnp.int32), axis=0, keepdims=True)
        lanes = lax.broadcasted_iota(jnp.int32, (1, BLOCK), 1)
        sublanes = lax.broadcasted_iota(jnp.int32, (BLOCK, 1), 0)
        row_hit = (codes[1:2, :].astype(jnp.int32) == sublanes).astype(jnp.bfloat16)
        block_hit = (clean_q[:, heads * HD:heads * HD + 1].astype(jnp.int32) == lanes).astype(jnp.bfloat16)
        grid = jnp.dot(row_hit, block_hit, preferred_element_type=jnp.float32)
        match = qp_ref[...] == clean_row
        hit = match.astype(jnp.float32)
        present = jnp.sum(hit, axis=1, keepdims=True) > 0.5
        picked = jnp.dot(
            hit.astype(jnp.bfloat16), clean_q[:, :heads * HD], preferred_element_type=jnp.float32
        ).astype(jnp.bfloat16)
        for b in range(local_blocks):
            for j in range(back + 1):
                block = blocks_ref[b * (back + 1) + j]
                start = pl.multiple_of(block * BLOCK, BLOCK)
                window_kv[j * BLOCK:(j + 1) * BLOCK, :] = g_ref[pl.ds(start, BLOCK), :]
            rows_at = slice(b * BLOCK, (b + 1) * BLOCK)
            block_present = present[rows_at, :]
            block_query = jnp.where(block_present, picked[rows_at, :], q_ref[rows_at, :])
            q = jnp.concatenate([block_query[:, h * HD:(h + 1) * HD] for h in range(heads)], axis=0)
            qp = qp_ref[rows_at, :]
            qd = qd_ref[rows_at, :]
            kp = kp_ref[b:b + 1, :]
            block_of = (kb_ref[b:b + 1, :] == sublanes).astype(jnp.float32)
            by_row = jnp.dot(grid, block_of, preferred_element_type=jnp.float32)
            row_of = (kr_ref[b:b + 1, :] == sublanes).astype(jnp.float32)
            patched = jnp.sum(by_row * row_of, axis=0, keepdims=True)
            kept = (kp >= 0) & (patched < 0.5)
            visible = (qd == kd_ref[b:b + 1, :]) & (kp <= qp) & kept
            clean_visible = (qd == clean_documents) & (clean_row <= qp)
            hidden = jnp.concatenate([jnp.where(visible, 0.0, -1e30)] * heads, axis=0)
            clean_hidden = jnp.concatenate([jnp.where(clean_visible, 0.0, -1e30)] * heads, axis=0)
            scores = lax.dot_general(
                q, window_kv[:, :HD], (((1,), (1,)), ((), ())),
                preferred_element_type=jnp.float32,
            ) * score_scale
            clean_scores = lax.dot_general(
                q, clean_kv[:, :HD], (((1,), (1,)), ((), ())),
                preferred_element_type=jnp.float32,
            ) * score_scale
            masked = scores + hidden
            clean_masked = clean_scores + clean_hidden
            peak = jnp.maximum(
                jnp.max(masked, axis=1, keepdims=True),
                jnp.max(clean_masked, axis=1, keepdims=True),
            )
            weights = jnp.exp(masked - peak)
            clean_weights = jnp.exp(clean_masked - peak)
            total = jnp.sum(weights, axis=1, keepdims=True) + jnp.sum(
                clean_weights, axis=1, keepdims=True
            )
            mixed = jnp.dot(
                weights.astype(jnp.bfloat16), window_kv[:, HD:],
                preferred_element_type=jnp.float32,
            ) + jnp.dot(
                clean_weights.astype(jnp.bfloat16), clean_kv[:, HD:],
                preferred_element_type=jnp.float32,
            )
            result = (mixed / total).astype(out_ref.dtype)
            for h in range(heads):
                out_ref[rows_at, h * HD:(h + 1) * HD] = result[h * BLOCK:(h + 1) * BLOCK, :]

    full = lambda shape: pl.BlockSpec(shape, lambda i, *_: (0,) * len(shape))
    operands = (gathered, query, query_places, query_documents, key_places, key_documents,
                bounds, key_blocks, key_rows)
    return pl.pallas_call(
        kernel,
        out_shape=jax.ShapeDtypeStruct(query.shape, query.dtype),
        grid_spec=pltpu.PrefetchScalarGridSpec(
            num_scalar_prefetch=1,
            grid=(1,),
            in_specs=[full(x.shape) for x in operands],
            out_specs=full(query.shape),
            scratch_shapes=[
                pltpu.VMEM((window, width), jnp.bfloat16),
                pltpu.VMEM((clean_count, width), jnp.bfloat16),
                pltpu.VMEM((clean_count, pairs * width), jnp.bfloat16),
            ],
        ),
        compiler_params=pltpu.CompilerParams(vmem_limit_bytes=48 * 1024 * 1024),
    )(window_blocks, *operands)


def solution(mesh):
    in_specs = (
        P(("run", "ctx"), None),
        P(),
        P(),
        P(("run", "ctx")),
        P(("run", "ctx"), None),
        P(None, "tp"),
        P("tp"),
        P(None, "tp"),
        P("tp"),
        P(None, "tp"),
        P("tp"),
    )
    out_specs = P(("run", "ctx"), "tp")
    return jax.shard_map(body, mesh=mesh, in_specs=in_specs, out_specs=out_specs, check_vma=False)
```
